32 devices in a mesh: wide: 8 (over y, x, core), lon: 4 (over z).
Axes of the slice: x: 2, y: 2, z: 4, core: 2. Of those that a mesh axis runs over, the one named last changes fastest.
Arguments:
- background_ensemble: bfloat16 [256, 64, 1024], P('wide', None, 'lon'), may hold values from -6 to 6
- innov: bfloat16 [256, 64, 1024], P(None, 'wide', 'lon'), may hold values from -6 to 6
- obs_index: int32 [4, 64, 1024], P(None, None, 'lon'), may hold values from 0 to 16383, as said below
- obs_weight: float32 [4, 64, 1024], P(None, None, 'lon'), may hold values from 0.05 to 0.5
- obs_list: int32 [4, 128, 16], P('lon', 'wide'), may hold values from 0 to 23, as said below
- tile_count: int32 [4, 128], P('lon', 'wide'), may hold values from 1 to 16
- taper_class: int32 [4, 128, 16], P('lon', 'wide'), may hold values from 0 to 3
Outputs:
- analysis: bfloat16 [256, 64, 1024], P('wide', None, 'lon')
The draws below stay inside these ranges and needn't reach their ends.
Inputs may be any that keep to these rules, and one draw needn't show every extreme that they name: obs_index[k, i, c] = r * 256 + q names the cell in row r and column q of the observation's own longitude tile, and row r lies among the 8 rows of the region that holds row i. Each row of obs_list names 16 different candidates of its region.
All inputs are finite; a program needn't handle non-finite values.
Results may differ from the reference program's by a relative error of at most 0.0056.
Values may be sent and summed in bfloat16 or wider, within the bound.
No kernel may reach another device: no remote copies, remote signals or barrier semaphores. Data moves between devices by JAX's collectives and lax.ppermute only.
A program may use at most 64 MiB of HBM per device.

```python
import jax
import jax.numpy as jnp
from jax import lax

ENSEMBLE_SIZE = 256
LAT_DEV = 8
PATCH_MERIDIANS = 256
BLK = 128
LIST = 16
HALO_BLK = 4
BLOCKS = 16
PARALLEL_LINES = 64
LON = 1024
SB_ALL = 128
TILES = 4
N_WIDE = 8
N_LON = 4


def draw_obs_index(key, part):
    row_ids = lax.broadcasted_iota(jnp.int32, (PARALLEL_LINES, LON), 0)
    col_ids = lax.broadcasted_iota(jnp.int32, (PARALLEL_LINES, LON), 1)
    region = row_ids // LAT_DEV
    extent = (LAT_DEV - 1) * PATCH_MERIDIANS - 1
    anchor = region * (LAT_DEV * PATCH_MERIDIANS) + jax.random.randint(key, (PARALLEL_LINES, LON), 0, extent)
    anchor = jnp.where((row_ids == 0) & (col_ids == 0), 0, anchor)
    anchor = jnp.where((row_ids == PARALLEL_LINES - 1) & (col_ids == 0), PARALLEL_LINES * PATCH_MERIDIANS - PATCH_MERIDIANS - 2, anchor)
    offsets = jnp.array([0, 1, PATCH_MERIDIANS, PATCH_MERIDIANS + 1], jnp.int32)
    return (anchor[None, :, :] + offsets[:, None, None]).astype(jnp.int32)


def draw_obs_list(key, part):
    candidates = BLOCKS + 2 * HALO_BLK
    array_shape = (TILES, SB_ALL, candidates)
    scores = jax.random.randint(key, array_shape, 0, 65536) * candidates + lax.broadcasted_iota(jnp.int32, array_shape, 2)
    ranking = jnp.argsort(scores, axis=-1)
    return ranking[..., :LIST].astype(jnp.int32)


def draw_tile_count(key, part):
    level_key, jitter_key, top_key = jax.random.split(key, 3)
    quarter = LIST // 4
    regions = SB_ALL // BLOCKS
    density = jax.random.randint(level_key, (TILES, regions, 1), 0, 4)
    jitter = jax.random.randint(jitter_key, (TILES, regions, BLOCKS), 0, quarter)
    counts = (1 + quarter * density + jitter).reshape(TILES, SB_ALL)
    top_place = jax.random.randint(top_key, (TILES, 1), 0, SB_ALL)
    low_place = (top_place + BLOCKS) % SB_ALL
    block_ids = lax.broadcasted_iota(jnp.int32, (TILES, SB_ALL), 1)
    counts = jnp.where(block_ids == top_place, LIST, counts)
    counts = jnp.where(block_ids == low_place, 1, counts)
    return counts.astype(jnp.int32)


def with_ends(values, key, smallest, high):
    index_at = [jax.random.randint(jax.random.fold_in(key, axis), (), 0, length) for axis, length in enumerate(values.shape)]
    widest = values.shape.index(max(values.shape))
    beside = index_at[:widest] + [(index_at[widest] + 1) % values.shape[widest]] + index_at[widest + 1:]
    return values.at[tuple(index_at)].set(smallest).at[tuple(beside)].set(high)


def shard_levels(key, dims, shards, least, high):
    def one(dim, blocks):
        heights = jax.random.uniform(jax.random.fold_in(jax.random.fold_in(key, 6), dim), (blocks,), jnp.float32, least / len(shards), high / len(shards))
        return jnp.repeat(jnp.exp(heights), dims[dim] // blocks).reshape((-1,) + (1,) * (len(dims) - dim - 1))

    factor_of = one(*shards[0])
    for cut in shards[1:]:
        factor_of = factor_of * one(*cut)
    return factor_of


def scatter_about(rng, shape, scale, limit, cuts=(), held_as=jnp.bfloat16):
    entries = jax.random.normal(rng, shape, jnp.float32) * scale
    if len(cuts) > 0:
        entries = shard_levels(rng, shape, cuts, -0.22, 0.18) * entries
    return jnp.clip(entries, min=-limit, max=limit).astype(held_as)


def setup_inputs(seed: int = 0) -> dict:
    streams_of = jax.random.split(jax.random.key(seed), 8)
    background_ensemble = scatter_about(streams_of[0], (ENSEMBLE_SIZE, PARALLEL_LINES, LON), 1.0, 6.0, ((0, 8), (2, 4)))
    innov = scatter_about(streams_of[1], (ENSEMBLE_SIZE, PARALLEL_LINES, LON), 1.0, 6.0, ((1, 8), (2, 4)))
    obs_index = draw_obs_index(jax.random.fold_in(streams_of[7], 71), 0)
    obs_weight = jnp.clip(0.05 + 0.45 * jax.random.uniform(streams_of[3], (4, PARALLEL_LINES, LON), jnp.float32) ** shard_levels(streams_of[3], (4, PARALLEL_LINES, LON), ((2, 4),), -0.2, 0.2), 0.05, 0.5)
    obs_list = draw_obs_list(jax.random.fold_in(streams_of[7], 71), 0)
    tile_count = draw_tile_count(jax.random.fold_in(streams_of[7], 71), 0)
    taper_class = with_ends(jax.random.randint(streams_of[6], (TILES, SB_ALL, LIST), 0, 4), jax.random.fold_in(streams_of[6], 1), 0, 3).astype(jnp.int32)
    return dict(background_ensemble=background_ensemble, innov=innov, obs_index=obs_index, obs_weight=obs_weight, obs_list=obs_list, tile_count=tile_count, taper_class=taper_class)


def propagate_model(background_ensemble):
    state_values = background_ensemble.astype(jnp.float32)
    east_neighbour = jnp.roll(state_values, -1, axis=2)
    west_neighbour = jnp.roll(state_values, 1, axis=2)
    northern = jnp.pad(state_values[:, 1:, :], ((0, 0), (0, 1), (0, 0)))
    southern = jnp.pad(state_values[:, :-1, :], ((0, 0), (1, 0), (0, 0)))
    member_spread = east_neighbour + west_neighbour + northern + southern - 4.0 * state_values
    return (state_values + 0.2 * member_spread - 0.3 * (east_neighbour - west_neighbour)).astype(jnp.bfloat16)


def observe(flat, index, weight):
    summed = jnp.zeros((flat.shape[0], index.shape[1]), jnp.float32)
    for k in range(4):
        summed = summed + weight[k][None, :] * jnp.take(flat, index[k], axis=1).astype(jnp.float32)
    return summed.astype(jnp.bfloat16)


def anomaly_from_mean(state_values):
    centred = state_values.astype(jnp.float32)
    return (centred - jnp.mean(centred, axis=-2, keepdims=True)).astype(jnp.bfloat16)


def taper_tiles(classes, in_use, tile_width):
    row_ids = lax.broadcasted_iota(jnp.float32, (tile_width, tile_width), 0)
    col_ids = lax.broadcasted_iota(jnp.float32, (tile_width, tile_width), 1)
    offset = row_ids - col_ids
    length = 8.0 * jnp.exp2(classes.astype(jnp.float32))
    scaled = offset / length[..., None, None]
    return in_use[..., None, None] / (1.0 + scaled * scaled)


def partition_patches(grid):
    shaped = grid.reshape(ENSEMBLE_SIZE, N_WIDE, LAT_DEV, N_LON, PATCH_MERIDIANS).transpose(3, 1, 0, 2, 4)
    return shaped.reshape(N_LON, N_WIDE, ENSEMBLE_SIZE, LAT_DEV * PATCH_MERIDIANS)


def widen_regions(regions):
    blocks = regions.reshape(N_LON, N_WIDE, ENSEMBLE_SIZE, BLOCKS, BLK)
    west_neighbour = jnp.roll(blocks, 1, axis=0)[:, :, :, BLOCKS - HALO_BLK:]
    east_neighbour = jnp.roll(blocks, -1, axis=0)[:, :, :, :HALO_BLK]
    return jnp.concatenate([west_neighbour, blocks, east_neighbour], axis=3)


def update_region(inputs):
    model_anomaly, anchor, cand_obs, cand_innov, lists, counts, classes = inputs
    state_tile = model_anomaly.reshape(ENSEMBLE_SIZE, BLOCKS, BLK).astype(jnp.float32)
    picked_obs = jnp.take(cand_obs, lists, axis=1).astype(jnp.float32)
    picked_innov = jnp.take(cand_innov, lists, axis=1).astype(jnp.float32)
    in_use = (jnp.arange(LIST, dtype=jnp.int32)[None, :] < counts[:, None]).astype(jnp.float32)
    covariance = jnp.einsum('mbc,mbjo->bjco', state_tile, picked_obs) / (ENSEMBLE_SIZE - 1.0)
    tapered = (covariance * taper_tiles(classes, in_use, BLK)).astype(jnp.bfloat16)
    tapered = lax.optimization_barrier(tapered).astype(jnp.float32)
    change = jnp.einsum('mbjo,bjco->mbc', picked_innov, tapered)
    return (anchor.astype(jnp.float32) + change.reshape(ENSEMBLE_SIZE, BLOCKS * BLK)).astype(jnp.bfloat16)


def reference(background_ensemble, innov, obs_index, obs_weight, obs_list, tile_count, taper_class):
    prediction_increment = propagate_model(background_ensemble)
    zonal_bands = prediction_increment.reshape(ENSEMBLE_SIZE, PARALLEL_LINES, N_LON, PATCH_MERIDIANS).transpose(2, 0, 1, 3).reshape(N_LON, ENSEMBLE_SIZE, PARALLEL_LINES * PATCH_MERIDIANS)
    strip_index = obs_index.reshape(4, PARALLEL_LINES, N_LON, PATCH_MERIDIANS).transpose(2, 0, 1, 3).reshape(N_LON, 4, PARALLEL_LINES * PATCH_MERIDIANS)
    strip_weight = obs_weight.reshape(4, PARALLEL_LINES, N_LON, PATCH_MERIDIANS).transpose(2, 0, 1, 3).reshape(N_LON, 4, PARALLEL_LINES * PATCH_MERIDIANS)
    observed = lax.map(lambda a: observe(a[0], a[1], a[2]), (zonal_bands, strip_index, strip_weight))
    obs_regions = observed.reshape(N_LON, ENSEMBLE_SIZE, N_WIDE, LAT_DEV * PATCH_MERIDIANS).transpose(0, 2, 1, 3)
    predicted_patches = partition_patches(prediction_increment)
    model_anomaly = anomaly_from_mean(predicted_patches)
    obs_dev = anomaly_from_mean(obs_regions)
    cand_obs = widen_regions(obs_dev)
    cand_innov = widen_regions(partition_patches(innov))
    total_tally = N_LON * N_WIDE
    patch_gridpoints = LAT_DEV * PATCH_MERIDIANS
    candidates = BLOCKS + 2 * HALO_BLK
    updated = lax.map(update_region, (
        model_anomaly.reshape(total_tally, ENSEMBLE_SIZE, patch_gridpoints),
        predicted_patches.reshape(total_tally, ENSEMBLE_SIZE, patch_gridpoints),
        cand_obs.reshape(total_tally, ENSEMBLE_SIZE, candidates, BLK),
        cand_innov.reshape(total_tally, ENSEMBLE_SIZE, candidates, BLK),
        obs_list.reshape(total_tally, BLOCKS, LIST),
        tile_count.reshape(total_tally, BLOCKS),
        taper_class.reshape(total_tally, BLOCKS, LIST)))
    shaped = updated.reshape(N_LON, N_WIDE, ENSEMBLE_SIZE, LAT_DEV, PATCH_MERIDIANS).transpose(2, 1, 3, 0, 4)
    return shaped.reshape(ENSEMBLE_SIZE, PARALLEL_LINES, LON)
```

```python
import math

import jax
import jax.numpy as jnp
from jax import lax
from jax.sharding import PartitionSpec as P
from jax.experimental import pallas as pl
from jax.experimental.pallas import tpu as pltpu

BLK = 128
HALO_BLK = 4


def padded_2(value, sides, width):
    for axis, dim in sides:
        size, length = (lax.axis_size(axis), value.shape[dim])
        up = [(i, (i + 1) % size) for i in range(size)]
        down = [(j, i) for i, j in up]
        last = lax.slice_in_dim(value, length - width, length, axis=dim)
        first = lax.slice_in_dim(value, 0, width, axis=dim)
        before = lax.ppermute(last, axis, up)
        after = lax.ppermute(first, axis, down)
        value = jnp.concatenate([before, value, after], axis=dim)
    return value


def observe_region(state, index, weight):
    members, cells = state.shape
    width = math.gcd(512, cells)
    nblocks = cells // width
    index_blocks = index.reshape(4, nblocks, width).transpose(1, 0, 2)
    weight_blocks = weight.reshape(4, nblocks, width).transpose(1, 0, 2)
    cell_ids = lax.broadcasted_iota(jnp.int32, (cells, width), 0)

    def observe_one_block(pieces):
        index_here, weight_here = pieces
        summed = jnp.zeros((members, width), jnp.float32)
        for k in range(4):
            selector = (cell_ids == index_here[k][None, :]).astype(jnp.bfloat16)
            picked = jnp.dot(state, selector, preferred_element_type=jnp.float32)
            summed = summed + weight_here[k][None, :] * picked
        return summed.astype(jnp.bfloat16)

    result = lax.map(observe_one_block, (index_blocks, weight_blocks))
    return result.transpose(1, 0, 2).reshape(members, cells)


def anomaly_from_mean(state_values):
    centred = state_values.astype(jnp.float32)
    return (centred - jnp.mean(centred, axis=-2, keepdims=True)).astype(jnp.bfloat16)


def taper_tiles(classes, in_use, tile_width):
    row_ids = lax.broadcasted_iota(jnp.float32, (tile_width, tile_width), 0)
    col_ids = lax.broadcasted_iota(jnp.float32, (tile_width, tile_width), 1)
    offset = row_ids - col_ids
    length = 8.0 * jnp.exp2(classes.astype(jnp.float32))
    scaled = offset / length[..., None, None]
    return in_use[..., None, None] / (1.0 + scaled * scaled)


def body(background_ensemble, innov, obs_index, obs_weight, obs_list, tile_count, taper_class):
    padded = padded_2(background_ensemble, (("lon", 2),), 1)
    state_values = background_ensemble.astype(jnp.float32)
    east_neighbour = padded[:, :, 2:].astype(jnp.float32)
    west_neighbour = padded[:, :, :-2].astype(jnp.float32)
    northern = jnp.pad(state_values[:, 1:, :], ((0, 0), (0, 1), (0, 0)))
    southern = jnp.pad(state_values[:, :-1, :], ((0, 0), (1, 0), (0, 0)))
    member_spread = east_neighbour + west_neighbour + northern + southern - 4.0 * state_values
    prediction_increment = (
        state_values + 0.2 * member_spread - 0.3 * (east_neighbour - west_neighbour)
    ).astype(jnp.bfloat16)
    ensemble_lines_here, whole_parallel_set, patch_meridian_lines = prediction_increment.shape
    members = innov.shape[0]
    band_rows = innov.shape[1]
    patch_gridpoints = band_rows * patch_meridian_lines
    region = lax.all_to_all(prediction_increment, "wide", split_axis=1, concat_axis=0, tiled=True)
    region_state = region.reshape(members, patch_gridpoints)
    first_row = lax.axis_index("wide") * band_rows
    local_index = lax.dynamic_slice_in_dim(obs_index, first_row, band_rows, 1).reshape(
        4, patch_gridpoints
    )
    local_index = local_index - first_row * patch_meridian_lines
    local_weight = lax.dynamic_slice_in_dim(obs_weight, first_row, band_rows, 1).reshape(
        4, patch_gridpoints
    )
    region_obs = observe_region(region_state, local_index, local_weight)
    model_anomaly = anomaly_from_mean(region_state)
    obs_dev = anomaly_from_mean(region_obs)
    stacked = jnp.stack([obs_dev, innov.reshape(members, patch_gridpoints)])
    widened = padded_2(stacked, (("lon", 2),), HALO_BLK * BLK)
    candidate_count = widened.shape[2] // BLK
    block_count = patch_gridpoints // BLK
    code = block_codes(obs_list[0], tile_count[0], taper_class[0], candidate_count)
    tiles = taper_table(BLK, members)
    cand_obs = widened[0]
    cand_innov_t = widened[1].T
    result_t = update_call(
        code.reshape(-1),
        model_anomaly.T,
        region_state.T,
        cand_obs,
        cand_innov_t,
        tiles,
        block_count,
        candidate_count,
    )
    result = result_t.T
    return lax.all_to_all(
        result.reshape(members, band_rows, patch_meridian_lines),
        "wide",
        split_axis=0,
        concat_axis=1,
        tiled=True,
    )


def block_codes(lists, counts, classes, candidate_count):
    zero_code = 4
    entries = jnp.arange(lists.shape[1], dtype=jnp.int32)
    value = jnp.where(entries[None, :] < counts[:, None], classes, zero_code)
    hit = lists[:, :, None] == jnp.arange(candidate_count, dtype=jnp.int32)[None, None, :]
    code = zero_code + jnp.sum(jnp.where(hit, value[:, :, None] - zero_code, 0), axis=1)
    return jnp.clip(code, 0, zero_code).astype(jnp.int32)


def taper_table(tile_width, members):
    row_ids = lax.broadcasted_iota(jnp.float32, (tile_width, tile_width), 0)
    col_ids = lax.broadcasted_iota(jnp.float32, (tile_width, tile_width), 1)
    offset = row_ids - col_ids
    length = 8.0 * jnp.exp2(jnp.arange(4, dtype=jnp.float32))
    scaled = offset[None] / length[:, None, None]
    tiles = (1.0 / (1.0 + scaled * scaled)) / (members - 1.0)
    return jnp.concatenate([tiles, jnp.zeros((1, tile_width, tile_width), jnp.float32)], axis=0)


GROUP = 4


def update_call(code, state_t, anchor_t, cand_obs, cand_innov_t, tiles, block_count, candidate_count):
    cells, members = state_t.shape
    rows = GROUP * BLK
    width = candidate_count * BLK

    def kernel(code_ref, st_ref, ft_ref, o_ref, it_ref, taper_ref, out_ref, cov_scr, tap_scr):
        g = pl.program_id(0)
        cov_scr[...] = jnp.dot(st_ref[...], o_ref[...], preferred_element_type=jnp.float32)
        for sl in range(GROUP):
            s = g * GROUP + sl
            for b in range(candidate_count):
                c = code_ref[s * candidate_count + b]
                tile = cov_scr[sl * BLK:(sl + 1) * BLK, b * BLK:(b + 1) * BLK] * taper_ref[c]
                tap_scr[sl * BLK:(sl + 1) * BLK, b * BLK:(b + 1) * BLK] = tile.astype(jnp.bfloat16)
        change = jnp.dot(tap_scr[...], it_ref[...], preferred_element_type=jnp.float32)
        out_ref[...] = (ft_ref[...].astype(jnp.float32) + change).astype(jnp.bfloat16)

    grid_spec = pltpu.PrefetchScalarGridSpec(
        num_scalar_prefetch=1,
        grid=(block_count // GROUP,),
        in_specs=[
            pl.BlockSpec((rows, members), lambda g, code: (g, 0)),
            pl.BlockSpec((rows, members), lambda g, code: (g, 0)),
            pl.BlockSpec((members, width), lambda g, code: (0, 0)),
            pl.BlockSpec((width, members), lambda g, code: (0, 0)),
            pl.BlockSpec(tiles.shape, lambda g, code: (0, 0, 0)),
        ],
        out_specs=pl.BlockSpec((rows, members), lambda g, code: (g, 0)),
        scratch_shapes=[
            pltpu.VMEM((rows, width), jnp.float32),
            pltpu.VMEM((rows, width), jnp.bfloat16),
        ],
    )
    return pl.pallas_call(
        kernel,
        grid_spec=grid_spec,
        out_shape=jax.ShapeDtypeStruct((cells, members), jnp.bfloat16),
    )(code, state_t, anchor_t, cand_obs, cand_innov_t, tiles)


def solution(mesh):
    in_specs = (
        P("wide", None, "lon"),
        P(None, "wide", "lon"),
        P(None, None, "lon"),
        P(None, None, "lon"),
        P("lon", "wide", None),
        P("lon", "wide"),
        P("lon", "wide", None),
    )
    out_specs = P("wide", None, "lon")
    return jax.shard_map(body, mesh=mesh, in_specs=in_specs, out_specs=out_specs, check_vma=False)
```

```python
import math

import jax
import jax.numpy as jnp
from jax import lax
from jax.sharding import PartitionSpec as P
from jax.experimental import pallas as pl
from jax.experimental.pallas import tpu as pltpu

BLK = 128
HALO_BLK = 4


def padded_2(value, sides, width):
    for axis, dim in sides:
        size, length = (lax.axis_size(axis), value.shape[dim])
        up = [(i, (i + 1) % size) for i in range(size)]
        down = [(j, i) for i, j in up]
        last = lax.slice_in_dim(value, length - width, length, axis=dim)
        first = lax.slice_in_dim(value, 0, width, axis=dim)
        before = lax.ppermute(last, axis, up)
        after = lax.ppermute(first, axis, down)
        value = jnp.concatenate([before, value, after], axis=dim)
    return value


def column_halo(value, axis):
    size = lax.axis_size(axis)
    here = lax.axis_index(axis)
    edges = jnp.concatenate([value[..., :1], value[..., -1:]], axis=-1)
    spread = jnp.broadcast_to(edges[None], (size,) + edges.shape)
    got = lax.all_to_all(spread, axis, 0, 0, tiled=False)
    west = lax.dynamic_index_in_dim(got, (here - 1) % size, 0, keepdims=False)[..., 1:2]
    east = lax.dynamic_index_in_dim(got, (here + 1) % size, 0, keepdims=False)[..., 0:1]
    return jnp.concatenate([west, value, east], axis=-1)


def observe_region(state, index, weight):
    members, cells = state.shape
    width = math.gcd(512, cells)
    nblocks = cells // width
    index_blocks = index.reshape(4, nblocks, width).transpose(1, 0, 2)
    weight_blocks = weight.reshape(4, nblocks, width).transpose(1, 0, 2)
    cell_ids = lax.broadcasted_iota(jnp.int32, (cells, width), 0)

    def observe_one_block(pieces):
        index_here, weight_here = pieces
        summed = jnp.zeros((members, width), jnp.float32)
        for k in range(4):
            selector = (cell_ids == index_here[k][None, :]).astype(jnp.bfloat16)
            picked = jnp.dot(state, selector, preferred_element_type=jnp.float32)
            summed = summed + weight_here[k][None, :] * picked
        return summed.astype(jnp.bfloat16)

    result = lax.map(observe_one_block, (index_blocks, weight_blocks))
    return result.transpose(1, 0, 2).reshape(members, cells)


def anomaly_from_mean(state_values):
    centred = state_values.astype(jnp.float32)
    return (centred - jnp.mean(centred, axis=-2, keepdims=True)).astype(jnp.bfloat16)


def taper_tiles(classes, in_use, tile_width):
    row_ids = lax.broadcasted_iota(jnp.float32, (tile_width, tile_width), 0)
    col_ids = lax.broadcasted_iota(jnp.float32, (tile_width, tile_width), 1)
    offset = row_ids - col_ids
    length = 8.0 * jnp.exp2(classes.astype(jnp.float32))
    scaled = offset / length[..., None, None]
    return in_use[..., None, None] / (1.0 + scaled * scaled)


def body(background_ensemble, innov, obs_index, obs_weight, obs_list, tile_count, taper_class):
    padded = column_halo(background_ensemble, "lon")
    state_values = background_ensemble.astype(jnp.float32)
    east_neighbour = padded[:, :, 2:].astype(jnp.float32)
    west_neighbour = padded[:, :, :-2].astype(jnp.float32)
    northern = jnp.pad(state_values[:, 1:, :], ((0, 0), (0, 1), (0, 0)))
    southern = jnp.pad(state_values[:, :-1, :], ((0, 0), (1, 0), (0, 0)))
    member_spread = east_neighbour + west_neighbour + northern + southern - 4.0 * state_values
    prediction_increment = (
        state_values + 0.2 * member_spread - 0.3 * (east_neighbour - west_neighbour)
    ).astype(jnp.bfloat16)
    ensemble_lines_here, whole_parallel_set, patch_meridian_lines = prediction_increment.shape
    members = innov.shape[0]
    band_rows = innov.shape[1]
    patch_gridpoints = band_rows * patch_meridian_lines
    region = lax.all_to_all(prediction_increment, "wide", split_axis=1, concat_axis=0, tiled=True)
    region_state = region.reshape(members, patch_gridpoints)
    first_row = lax.axis_index("wide") * band_rows
    local_index = lax.dynamic_slice_in_dim(obs_index, first_row, band_rows, 1).reshape(
        4, patch_gridpoints
    )
    local_index = local_index - first_row * patch_meridian_lines
    local_weight = lax.dynamic_slice_in_dim(obs_weight, first_row, band_rows, 1).reshape(
        4, patch_gridpoints
    )
    region_obs = observe_region(region_state, local_index, local_weight)
    model_anomaly = anomaly_from_mean(region_state)
    obs_dev = anomaly_from_mean(region_obs)
    stacked = jnp.stack([obs_dev, innov.reshape(members, patch_gridpoints)])
    widened = padded_2(stacked, (("lon", 2),), HALO_BLK * BLK)
    candidate_count = widened.shape[2] // BLK
    block_count = patch_gridpoints // BLK
    code = block_codes(obs_list[0], tile_count[0], taper_class[0], candidate_count)
    tiles = taper_table(BLK, members)
    cand_obs = widened[0]
    cand_innov_t = widened[1].T
    result_t = update_call(
        code.reshape(-1),
        model_anomaly.T,
        region_state.T,
        cand_obs,
        cand_innov_t,
        tiles,
        block_count,
        candidate_count,
    )
    result = result_t.T
    return lax.all_to_all(
        result.reshape(members, band_rows, patch_meridian_lines),
        "wide",
        split_axis=0,
        concat_axis=1,
        tiled=True,
    )


def block_codes(lists, counts, classes, candidate_count):
    zero_code = 4
    entries = jnp.arange(lists.shape[1], dtype=jnp.int32)
    value = jnp.where(entries[None, :] < counts[:, None], classes, zero_code)
    hit = lists[:, :, None] == jnp.arange(candidate_count, dtype=jnp.int32)[None, None, :]
    code = zero_code + jnp.sum(jnp.where(hit, value[:, :, None] - zero_code, 0), axis=1)
    return jnp.clip(code, 0, zero_code).astype(jnp.int32)


def taper_table(tile_width, members):
    row_ids = lax.broadcasted_iota(jnp.float32, (tile_width, tile_width), 0)
    col_ids = lax.broadcasted_iota(jnp.float32, (tile_width, tile_width), 1)
    offset = row_ids - col_ids
    length = 8.0 * jnp.exp2(jnp.arange(4, dtype=jnp.float32))
    scaled = offset[None] / length[:, None, None]
    tiles = (1.0 / (1.0 + scaled * scaled)) / (members - 1.0)
    return jnp.concatenate([tiles, jnp.zeros((1, tile_width, tile_width), jnp.float32)], axis=0)


GROUP = 4


def update_call(code, state_t, anchor_t, cand_obs, cand_innov_t, tiles, block_count, candidate_count):
    cells, members = state_t.shape
    rows = GROUP * BLK
    width = candidate_count * BLK

    def kernel(code_ref, st_ref, ft_ref, o_ref, it_ref, taper_ref, out_ref, cov_scr, tap_scr):
        g = pl.program_id(0)
        cov_scr[...] = jnp.dot(st_ref[...], o_ref[...], preferred_element_type=jnp.float32)
        for sl in range(GROUP):
            s = g * GROUP + sl
            for b in range(candidate_count):
                c = code_ref[s * candidate_count + b]
                tile = cov_scr[sl * BLK:(sl + 1) * BLK, b * BLK:(b + 1) * BLK] * taper_ref[c]
                tap_scr[sl * BLK:(sl + 1) * BLK, b * BLK:(b + 1) * BLK] = tile.astype(jnp.bfloat16)
        change = jnp.dot(tap_scr[...], it_ref[...], preferred_element_type=jnp.float32)
        out_ref[...] = (ft_ref[...].astype(jnp.float32) + change).astype(jnp.bfloat16)

    grid_spec = pltpu.PrefetchScalarGridSpec(
        num_scalar_prefetch=1,
        grid=(block_count // GROUP,),
        in_specs=[
            pl.BlockSpec((rows, members), lambda g, code: (g, 0)),
            pl.BlockSpec((rows, members), lambda g, code: (g, 0)),
            pl.BlockSpec((members, width), lambda g, code: (0, 0)),
            pl.BlockSpec((width, members), lambda g, code: (0, 0)),
            pl.BlockSpec(tiles.shape, lambda g, code: (0, 0, 0)),
        ],
        out_specs=pl.BlockSpec((rows, members), lambda g, code: (g, 0)),
        scratch_shapes=[
            pltpu.VMEM((rows, width), jnp.float32),
            pltpu.VMEM((rows, width), jnp.bfloat16),
        ],
    )
    return pl.pallas_call(
        kernel,
        grid_spec=grid_spec,
        out_shape=jax.ShapeDtypeStruct((cells, members), jnp.bfloat16),
    )(code, state_t, anchor_t, cand_obs, cand_innov_t, tiles)


def solution(mesh):
    in_specs = (
        P("wide", None, "lon"),
        P(None, "wide", "lon"),
        P(None, None, "lon"),
        P(None, None, "lon"),
        P("lon", "wide", None),
        P("lon", "wide"),
        P("lon", "wide", None),
    )
    out_specs = P("wide", None, "lon")
    return jax.shard_map(body, mesh=mesh, in_specs=in_specs, out_specs=out_specs, check_vma=False)
```

```python
import math

import jax
import jax.numpy as jnp
from jax import lax
from jax.sharding import PartitionSpec as P
from jax.experimental import pallas as pl
from jax.experimental.pallas import tpu as pltpu

BLK = 128
HALO_BLK = 4


def padded_2(value, sides, width):
    for axis, dim in sides:
        size, length = (lax.axis_size(axis), value.shape[dim])
        up = [(i, (i + 1) % size) for i in range(size)]
        down = [(j, i) for i, j in up]
        last = lax.slice_in_dim(value, length - width, length, axis=dim)
        first = lax.slice_in_dim(value, 0, width, axis=dim)
        before = lax.ppermute(last, axis, up)
        after = lax.ppermute(first, axis, down)
        value = jnp.concatenate([before, value, after], axis=dim)
    return value


def column_halo(value, axis):
    size = lax.axis_size(axis)
    here = lax.axis_index(axis)
    edges = jnp.concatenate([value[..., :1], value[..., -1:]], axis=-1)
    spread = jnp.broadcast_to(edges[None], (size,) + edges.shape)
    got = lax.all_to_all(spread, axis, 0, 0, tiled=False)
    west = lax.dynamic_index_in_dim(got, (here - 1) % size, 0, keepdims=False)[..., 1:2]
    east = lax.dynamic_index_in_dim(got, (here + 1) % size, 0, keepdims=False)[..., 0:1]
    return jnp.concatenate([west, value, east], axis=-1)


def observe_region(state, index, weight):
    members, cells = state.shape
    count = index.shape[1]
    width = math.gcd(512, count)
    nblocks = count // width
    index_blocks = index.reshape(4, nblocks, width).transpose(1, 0, 2)
    weight_blocks = weight.reshape(4, nblocks, width).transpose(1, 0, 2)
    cell_ids = lax.broadcasted_iota(jnp.int32, (cells, width), 0)

    def observe_one_block(pieces):
        index_here, weight_here = pieces
        summed = jnp.zeros((members, width), jnp.float32)
        for k in range(4):
            selector = (cell_ids == index_here[k][None, :]).astype(jnp.bfloat16)
            picked = jnp.dot(state, selector, preferred_element_type=jnp.float32)
            summed = summed + weight_here[k][None, :] * picked
        return summed.astype(jnp.bfloat16)

    result = lax.map(observe_one_block, (index_blocks, weight_blocks))
    return result.transpose(1, 0, 2).reshape(members, count)


def anomaly_from_mean(state_values):
    centred = state_values.astype(jnp.float32)
    return (centred - jnp.mean(centred, axis=-2, keepdims=True)).astype(jnp.bfloat16)


def taper_tiles(classes, in_use, tile_width):
    row_ids = lax.broadcasted_iota(jnp.float32, (tile_width, tile_width), 0)
    col_ids = lax.broadcasted_iota(jnp.float32, (tile_width, tile_width), 1)
    offset = row_ids - col_ids
    length = 8.0 * jnp.exp2(classes.astype(jnp.float32))
    scaled = offset / length[..., None, None]
    return in_use[..., None, None] / (1.0 + scaled * scaled)


def body(background_ensemble, innov, obs_index, obs_weight, obs_list, tile_count, taper_class):
    padded = column_halo(background_ensemble, "lon")
    state_values = background_ensemble.astype(jnp.float32)
    east_neighbour = padded[:, :, 2:].astype(jnp.float32)
    west_neighbour = padded[:, :, :-2].astype(jnp.float32)
    northern = jnp.pad(state_values[:, 1:, :], ((0, 0), (0, 1), (0, 0)))
    southern = jnp.pad(state_values[:, :-1, :], ((0, 0), (1, 0), (0, 0)))
    member_spread = east_neighbour + west_neighbour + northern + southern - 4.0 * state_values
    prediction_increment = (
        state_values + 0.2 * member_spread - 0.3 * (east_neighbour - west_neighbour)
    ).astype(jnp.bfloat16)
    ensemble_lines_here, whole_parallel_set, patch_meridian_lines = prediction_increment.shape
    members = innov.shape[0]
    band_rows = innov.shape[1]
    patch_gridpoints = band_rows * patch_meridian_lines
    region = lax.all_to_all(prediction_increment, "wide", split_axis=1, concat_axis=0, tiled=True)
    region_state = region.reshape(members, patch_gridpoints)
    first_row = lax.axis_index("wide") * band_rows
    local_index = lax.dynamic_slice_in_dim(obs_index, first_row, band_rows, 1).reshape(
        4, patch_gridpoints
    )
    local_index = local_index - first_row * patch_meridian_lines
    local_weight = lax.dynamic_slice_in_dim(obs_weight, first_row, band_rows, 1).reshape(
        4, patch_gridpoints
    )
    halo = HALO_BLK * BLK
    innov_flat = innov.reshape(members, patch_gridpoints)
    edge_index = jnp.concatenate([local_index[:, :halo], local_index[:, -halo:]], axis=1)
    edge_weight = jnp.concatenate([local_weight[:, :halo], local_weight[:, -halo:]], axis=1)
    edge_dev = anomaly_from_mean(observe_region(region_state, edge_index, edge_weight))
    edge_innov = jnp.concatenate([innov_flat[:, :halo], innov_flat[:, -halo:]], axis=1)
    edges = jnp.stack([edge_dev, edge_innov])
    lon_size = lax.axis_size("lon")
    up = [(i, (i + 1) % lon_size) for i in range(lon_size)]
    down = [(j, i) for i, j in up]
    west = lax.ppermute(edges[:, :, halo:], "lon", up)
    east = lax.ppermute(edges[:, :, :halo], "lon", down)
    middle_dev = anomaly_from_mean(
        observe_region(region_state, local_index[:, halo:-halo], local_weight[:, halo:-halo])
    )
    obs_dev = jnp.concatenate([edge_dev[:, :halo], middle_dev, edge_dev[:, halo:]], axis=1)
    model_anomaly = anomaly_from_mean(region_state)
    halo_blocks = halo // BLK
    block_count = patch_gridpoints // BLK
    candidate_count = block_count + 2 * halo_blocks
    code = block_codes(obs_list[0], tile_count[0], taper_class[0], candidate_count)
    own_code = code[:, halo_blocks:halo_blocks + block_count]
    halo_code = jnp.concatenate([code[:, :halo_blocks], code[:, halo_blocks + block_count:]], axis=1)
    tiles = taper_table(BLK, members)
    state_t = model_anomaly.T
    partial = update_call(
        own_code.reshape(-1), state_t, None, None, obs_dev, innov_flat.T, tiles, block_count, block_count
    )
    halo_obs = jnp.concatenate([west[0], east[0]], axis=1)
    halo_innov = jnp.concatenate([west[1], east[1]], axis=1)
    result_t = update_call(
        halo_code.reshape(-1),
        state_t,
        partial,
        region_state.T,
        halo_obs,
        halo_innov.T,
        tiles,
        block_count,
        2 * halo_blocks,
    )
    result = result_t.T
    return lax.all_to_all(
        result.reshape(members, band_rows, patch_meridian_lines),
        "wide",
        split_axis=0,
        concat_axis=1,
        tiled=True,
    )


def block_codes(lists, counts, classes, candidate_count):
    zero_code = 4
    entries = jnp.arange(lists.shape[1], dtype=jnp.int32)
    value = jnp.where(entries[None, :] < counts[:, None], classes, zero_code)
    hit = lists[:, :, None] == jnp.arange(candidate_count, dtype=jnp.int32)[None, None, :]
    code = zero_code + jnp.sum(jnp.where(hit, value[:, :, None] - zero_code, 0), axis=1)
    return jnp.clip(code, 0, zero_code).astype(jnp.int32)


def taper_table(tile_width, members):
    row_ids = lax.broadcasted_iota(jnp.float32, (tile_width, tile_width), 0)
    col_ids = lax.broadcasted_iota(jnp.float32, (tile_width, tile_width), 1)
    offset = row_ids - col_ids
    length = 8.0 * jnp.exp2(jnp.arange(4, dtype=jnp.float32))
    scaled = offset[None] / length[:, None, None]
    tiles = (1.0 / (1.0 + scaled * scaled)) / (members - 1.0)
    return jnp.concatenate([tiles, jnp.zeros((1, tile_width, tile_width), jnp.float32)], axis=0)


GROUP = 4


def update_call(code, state_t, partial, anchor_t, cand_obs, cand_innov_t, tiles, block_count, candidate_count):
    cells, members = state_t.shape
    rows = GROUP * BLK
    width = candidate_count * BLK
    final = anchor_t is not None

    def kernel(code_ref, st_ref, o_ref, it_ref, taper_ref, *rest):
        if final:
            part_ref, ft_ref, out_ref, cov_scr, tap_scr = rest
        else:
            out_ref, cov_scr, tap_scr = rest
        g = pl.program_id(0)
        cov_scr[...] = jnp.dot(st_ref[...], o_ref[...], preferred_element_type=jnp.float32)
        for sl in range(GROUP):
            s = g * GROUP + sl
            for b in range(candidate_count):
                c = code_ref[s * candidate_count + b]
                tile = cov_scr[sl * BLK:(sl + 1) * BLK, b * BLK:(b + 1) * BLK] * taper_ref[c]
                tap_scr[sl * BLK:(sl + 1) * BLK, b * BLK:(b + 1) * BLK] = tile.astype(jnp.bfloat16)
        change = jnp.dot(tap_scr[...], it_ref[...], preferred_element_type=jnp.float32)
        if final:
            total = part_ref[...] + change
            out_ref[...] = (ft_ref[...].astype(jnp.float32) + total).astype(jnp.bfloat16)
        else:
            out_ref[...] = change

    row_spec = pl.BlockSpec((rows, members), lambda g, code: (g, 0))
    in_specs = [
        row_spec,
        pl.BlockSpec((members, width), lambda g, code: (0, 0)),
        pl.BlockSpec((width, members), lambda g, code: (0, 0)),
        pl.BlockSpec(tiles.shape, lambda g, code: (0, 0, 0)),
    ]
    operands = [state_t, cand_obs, cand_innov_t, tiles]
    if final:
        in_specs += [row_spec, row_spec]
        operands += [partial, anchor_t]
    grid_spec = pltpu.PrefetchScalarGridSpec(
        num_scalar_prefetch=1,
        grid=(block_count // GROUP,),
        in_specs=in_specs,
        out_specs=row_spec,
        scratch_shapes=[
            pltpu.VMEM((rows, width), jnp.float32),
            pltpu.VMEM((rows, width), jnp.bfloat16),
        ],
    )
    out_type = jnp.bfloat16 if final else jnp.float32
    return pl.pallas_call(
        kernel,
        grid_spec=grid_spec,
        out_shape=jax.ShapeDtypeStruct((cells, members), out_type),
        cost_estimate=pl.CostEstimate(flops=4 * cells * members * width, transcendentals=0, bytes_accessed=8 * cells * members),
    )(code, *operands)


def solution(mesh):
    in_specs = (
        P("wide", None, "lon"),
        P(None, "wide", "lon"),
        P(None, None, "lon"),
        P(None, None, "lon"),
        P("lon", "wide", None),
        P("lon", "wide"),
        P("lon", "wide", None),
    )
    out_specs = P("wide", None, "lon")
    return jax.shard_map(body, mesh=mesh, in_specs=in_specs, out_specs=out_specs, check_vma=False)
```

```python
import math

import jax
import jax.numpy as jnp
from jax import lax
from jax.sharding import PartitionSpec as P
from jax.experimental import pallas as pl
from jax.experimental.pallas import tpu as pltpu

BLK = 128
HALO_BLK = 4


def padded_2(value, sides, width):
    for axis, dim in sides:
        size, length = (lax.axis_size(axis), value.shape[dim])
        up = [(i, (i + 1) % size) for i in range(size)]
        down = [(j, i) for i, j in up]
        last = lax.slice_in_dim(value, length - width, length, axis=dim)
        first = lax.slice_in_dim(value, 0, width, axis=dim)
        before = lax.ppermute(last, axis, up)
        after = lax.ppermute(first, axis, down)
        value = jnp.concatenate([before, value, after], axis=dim)
    return value


def column_halo(value, axis):
    size = lax.axis_size(axis)
    here = lax.axis_index(axis)
    edges = jnp.concatenate([value[..., :1], value[..., -1:]], axis=-1)
    spread = jnp.broadcast_to(edges[None], (size,) + edges.shape)
    got = lax.all_to_all(spread, axis, 0, 0, tiled=False)
    west = lax.dynamic_index_in_dim(got, (here - 1) % size, 0, keepdims=False)[..., 1:2]
    east = lax.dynamic_index_in_dim(got, (here + 1) % size, 0, keepdims=False)[..., 0:1]
    return jnp.concatenate([west, value, east], axis=-1)


def observe_region(state, index, weight):
    members, cells = state.shape
    count = index.shape[1]
    cell_ids = lax.broadcasted_iota(jnp.int32, (cells, count), 0)
    combined = jnp.zeros((cells, count), jnp.float32)
    for k in range(4):
        combined = combined + jnp.where(cell_ids == index[k][None, :], weight[k][None, :], 0.0)
    high = combined.astype(jnp.bfloat16)
    low = (combined - high.astype(jnp.float32)).astype(jnp.bfloat16)
    summed = jnp.dot(state, high, preferred_element_type=jnp.float32)
    summed = summed + jnp.dot(state, low, preferred_element_type=jnp.float32)
    return summed.astype(jnp.bfloat16)


def anomaly_from_mean(state_values):
    centred = state_values.astype(jnp.float32)
    return (centred - jnp.mean(centred, axis=-2, keepdims=True)).astype(jnp.bfloat16)


def taper_tiles(classes, in_use, tile_width):
    row_ids = lax.broadcasted_iota(jnp.float32, (tile_width, tile_width), 0)
    col_ids = lax.broadcasted_iota(jnp.float32, (tile_width, tile_width), 1)
    offset = row_ids - col_ids
    length = 8.0 * jnp.exp2(classes.astype(jnp.float32))
    scaled = offset / length[..., None, None]
    return in_use[..., None, None] / (1.0 + scaled * scaled)


def body(background_ensemble, innov, obs_index, obs_weight, obs_list, tile_count, taper_class):
    padded = column_halo(background_ensemble, "lon")
    state_values = background_ensemble.astype(jnp.float32)
    east_neighbour = padded[:, :, 2:].astype(jnp.float32)
    west_neighbour = padded[:, :, :-2].astype(jnp.float32)
    northern = jnp.pad(state_values[:, 1:, :], ((0, 0), (0, 1), (0, 0)))
    southern = jnp.pad(state_values[:, :-1, :], ((0, 0), (1, 0), (0, 0)))
    member_spread = east_neighbour + west_neighbour + northern + southern - 4.0 * state_values
    prediction_increment = (
        state_values + 0.2 * member_spread - 0.3 * (east_neighbour - west_neighbour)
    ).astype(jnp.bfloat16)
    ensemble_lines_here, whole_parallel_set, patch_meridian_lines = prediction_increment.shape
    members = innov.shape[0]
    band_rows = innov.shape[1]
    patch_gridpoints = band_rows * patch_meridian_lines
    region = lax.all_to_all(prediction_increment, "wide", split_axis=1, concat_axis=0, tiled=True)
    region_state = region.reshape(members, patch_gridpoints)
    first_row = lax.axis_index("wide") * band_rows
    local_index = lax.dynamic_slice_in_dim(obs_index, first_row, band_rows, 1).reshape(
        4, patch_gridpoints
    )
    local_index = local_index - first_row * patch_meridian_lines
    local_weight = lax.dynamic_slice_in_dim(obs_weight, first_row, band_rows, 1).reshape(
        4, patch_gridpoints
    )
    halo = HALO_BLK * BLK
    innov_flat = innov.reshape(members, patch_gridpoints)
    edge_index = jnp.concatenate([local_index[:, :halo], local_index[:, -halo:]], axis=1)
    edge_weight = jnp.concatenate([local_weight[:, :halo], local_weight[:, -halo:]], axis=1)
    edge_dev = anomaly_from_mean(observe_region(region_state, edge_index, edge_weight))
    edge_innov = jnp.concatenate([innov_flat[:, :halo], innov_flat[:, -halo:]], axis=1)
    edges = jnp.stack([edge_dev, edge_innov])
    lon_size = lax.axis_size("lon")
    up = [(i, (i + 1) % lon_size) for i in range(lon_size)]
    down = [(j, i) for i, j in up]
    west = lax.ppermute(edges[:, :, halo:], "lon", up)
    east = lax.ppermute(edges[:, :, :halo], "lon", down)
    middle_dev = anomaly_from_mean(
        observe_region(region_state, local_index[:, halo:-halo], local_weight[:, halo:-halo])
    )
    obs_dev = jnp.concatenate([edge_dev[:, :halo], middle_dev, edge_dev[:, halo:]], axis=1)
    model_anomaly = anomaly_from_mean(region_state)
    halo_blocks = halo // BLK
    block_count = patch_gridpoints // BLK
    candidate_count = block_count + 2 * halo_blocks
    code = block_codes(obs_list[0], tile_count[0], taper_class[0], candidate_count)
    own_code = code[:, halo_blocks:halo_blocks + block_count]
    halo_code = jnp.concatenate([code[:, :halo_blocks], code[:, halo_blocks + block_count:]], axis=1)
    tiles = taper_table(BLK, members)
    state_t = model_anomaly.T
    partial = update_call(
        own_code.reshape(-1), state_t, None, None, obs_dev, innov_flat.T, tiles, block_count, block_count
    )
    halo_obs = jnp.concatenate([west[0], east[0]], axis=1)
    halo_innov = jnp.concatenate([west[1], east[1]], axis=1)
    result_t = update_call(
        halo_code.reshape(-1),
        state_t,
        partial,
        region_state.T,
        halo_obs,
        halo_innov.T,
        tiles,
        block_count,
        2 * halo_blocks,
    )
    result = result_t.T
    return lax.all_to_all(
        result.reshape(members, band_rows, patch_meridian_lines),
        "wide",
        split_axis=0,
        concat_axis=1,
        tiled=True,
    )


def block_codes(lists, counts, classes, candidate_count):
    zero_code = 4
    entries = jnp.arange(lists.shape[1], dtype=jnp.int32)
    value = jnp.where(entries[None, :] < counts[:, None], classes, zero_code)
    hit = lists[:, :, None] == jnp.arange(candidate_count, dtype=jnp.int32)[None, None, :]
    code = zero_code + jnp.sum(jnp.where(hit, value[:, :, None] - zero_code, 0), axis=1)
    return jnp.clip(code, 0, zero_code).astype(jnp.int32)


def taper_table(tile_width, members):
    row_ids = lax.broadcasted_iota(jnp.float32, (tile_width, tile_width), 0)
    col_ids = lax.broadcasted_iota(jnp.float32, (tile_width, tile_width), 1)
    offset = row_ids - col_ids
    length = 8.0 * jnp.exp2(jnp.arange(4, dtype=jnp.float32))
    scaled = offset[None] / length[:, None, None]
    tiles = (1.0 / (1.0 + scaled * scaled)) / (members - 1.0)
    return jnp.concatenate([tiles, jnp.zeros((1, tile_width, tile_width), jnp.float32)], axis=0)


GROUP = 4


def update_call(code, state_t, partial, anchor_t, cand_obs, cand_innov_t, tiles, block_count, candidate_count):
    cells, members = state_t.shape
    rows = GROUP * BLK
    width = candidate_count * BLK
    final = anchor_t is not None

    def kernel(code_ref, st_ref, o_ref, it_ref, taper_ref, *rest):
        if final:
            part_ref, ft_ref, out_ref, cov_scr, tap_scr = rest
        else:
            out_ref, cov_scr, tap_scr = rest
        g = pl.program_id(0)
        cov_scr[...] = jnp.dot(st_ref[...], o_ref[...], preferred_element_type=jnp.float32)
        for sl in range(GROUP):
            s = g * GROUP + sl
            for b in range(candidate_count):
                c = code_ref[s * candidate_count + b]
                tile = cov_scr[sl * BLK:(sl + 1) * BLK, b * BLK:(b + 1) * BLK] * taper_ref[c]
                tap_scr[sl * BLK:(sl + 1) * BLK, b * BLK:(b + 1) * BLK] = tile.astype(jnp.bfloat16)
        change = jnp.dot(tap_scr[...], it_ref[...], preferred_element_type=jnp.float32)
        if final:
            total = part_ref[...] + change
            out_ref[...] = (ft_ref[...].astype(jnp.float32) + total).astype(jnp.bfloat16)
        else:
            out_ref[...] = change

    row_spec = pl.BlockSpec((rows, members), lambda g, code: (g, 0))
    in_specs = [
        row_spec,
        pl.BlockSpec((members, width), lambda g, code: (0, 0)),
        pl.BlockSpec((width, members), lambda g, code: (0, 0)),
        pl.BlockSpec(tiles.shape, lambda g, code: (0, 0, 0)),
    ]
    operands = [state_t, cand_obs, cand_innov_t, tiles]
    if final:
        in_specs += [row_spec, row_spec]
        operands += [partial, anchor_t]
    grid_spec = pltpu.PrefetchScalarGridSpec(
        num_scalar_prefetch=1,
        grid=(block_count // GROUP,),
        in_specs=in_specs,
        out_specs=row_spec,
        scratch_shapes=[
            pltpu.VMEM((rows, width), jnp.float32),
            pltpu.VMEM((rows, width), jnp.bfloat16),
        ],
    )
    out_type = jnp.bfloat16 if final else jnp.float32
    return pl.pallas_call(
        kernel,
        grid_spec=grid_spec,
        out_shape=jax.ShapeDtypeStruct((cells, members), out_type),
        cost_estimate=pl.CostEstimate(flops=4 * cells * members * width, transcendentals=0, bytes_accessed=8 * cells * members),
    )(code, *operands)


def solution(mesh):
    in_specs = (
        P("wide", None, "lon"),
        P(None, "wide", "lon"),
        P(None, None, "lon"),
        P(None, None, "lon"),
        P("lon", "wide", None),
        P("lon", "wide"),
        P("lon", "wide", None),
    )
    out_specs = P("wide", None, "lon")
    return jax.shard_map(body, mesh=mesh, in_specs=in_specs, out_specs=out_specs, check_vma=False)
```

```python
import math

import jax
import jax.numpy as jnp
from jax import lax
from jax.sharding import PartitionSpec as P
from jax.experimental import pallas as pl
from jax.experimental.pallas import tpu as pltpu

BLK = 128
HALO_BLK = 4


def padded_2(value, sides, width):
    for axis, dim in sides:
        size, length = (lax.axis_size(axis), value.shape[dim])
        up = [(i, (i + 1) % size) for i in range(size)]
        down = [(j, i) for i, j in up]
        last = lax.slice_in_dim(value, length - width, length, axis=dim)
        first = lax.slice_in_dim(value, 0, width, axis=dim)
        before = lax.ppermute(last, axis, up)
        after = lax.ppermute(first, axis, down)
        value = jnp.concatenate([before, value, after], axis=dim)
    return value


def column_halo(value, axis):
    size = lax.axis_size(axis)
    here = lax.axis_index(axis)
    edges = jnp.concatenate([value[..., :1], value[..., -1:]], axis=-1)
    spread = jnp.broadcast_to(edges[None], (size,) + edges.shape)
    got = lax.all_to_all(spread, axis, 0, 0, tiled=False)
    west = lax.dynamic_index_in_dim(got, (here - 1) % size, 0, keepdims=False)[..., 1:2]
    east = lax.dynamic_index_in_dim(got, (here + 1) % size, 0, keepdims=False)[..., 0:1]
    return jnp.concatenate([west, value, east], axis=-1)


def observe_region(state, index, weight):
    members, cells = state.shape
    count = index.shape[1]
    cell_ids = lax.broadcasted_iota(jnp.int32, (cells, count), 0)
    summed = jnp.zeros((members, count), jnp.float32)
    for k in range(4):
        selector = (cell_ids == index[k][None, :]).astype(jnp.bfloat16)
        picked = jnp.dot(state, selector, preferred_element_type=jnp.float32)
        summed = summed + weight[k][None, :] * picked
    return summed.astype(jnp.bfloat16)


def anomaly_from_mean(state_values):
    centred = state_values.astype(jnp.float32)
    return (centred - jnp.mean(centred, axis=-2, keepdims=True)).astype(jnp.bfloat16)


def taper_tiles(classes, in_use, tile_width):
    row_ids = lax.broadcasted_iota(jnp.float32, (tile_width, tile_width), 0)
    col_ids = lax.broadcasted_iota(jnp.float32, (tile_width, tile_width), 1)
    offset = row_ids - col_ids
    length = 8.0 * jnp.exp2(classes.astype(jnp.float32))
    scaled = offset / length[..., None, None]
    return in_use[..., None, None] / (1.0 + scaled * scaled)


def body(background_ensemble, innov, obs_index, obs_weight, obs_list, tile_count, taper_class):
    padded = column_halo(background_ensemble, "lon")
    state_values = background_ensemble.astype(jnp.float32)
    east_neighbour = padded[:, :, 2:].astype(jnp.float32)
    west_neighbour = padded[:, :, :-2].astype(jnp.float32)
    northern = jnp.pad(state_values[:, 1:, :], ((0, 0), (0, 1), (0, 0)))
    southern = jnp.pad(state_values[:, :-1, :], ((0, 0), (1, 0), (0, 0)))
    member_spread = east_neighbour + west_neighbour + northern + southern - 4.0 * state_values
    prediction_increment = (
        state_values + 0.2 * member_spread - 0.3 * (east_neighbour - west_neighbour)
    ).astype(jnp.bfloat16)
    ensemble_lines_here, whole_parallel_set, patch_meridian_lines = prediction_increment.shape
    members = innov.shape[0]
    band_rows = innov.shape[1]
    patch_gridpoints = band_rows * patch_meridian_lines
    region = lax.all_to_all(prediction_increment, "wide", split_axis=1, concat_axis=0, tiled=True)
    region_state = region.reshape(members, patch_gridpoints)
    first_row = lax.axis_index("wide") * band_rows
    local_index = lax.dynamic_slice_in_dim(obs_index, first_row, band_rows, 1).reshape(
        4, patch_gridpoints
    )
    local_index = local_index - first_row * patch_meridian_lines
    local_weight = lax.dynamic_slice_in_dim(obs_weight, first_row, band_rows, 1).reshape(
        4, patch_gridpoints
    )
    halo = HALO_BLK * BLK
    innov_flat = innov.reshape(members, patch_gridpoints)
    edge_index = jnp.concatenate([local_index[:, :halo], local_index[:, -halo:]], axis=1)
    edge_weight = jnp.concatenate([local_weight[:, :halo], local_weight[:, -halo:]], axis=1)
    edge_dev = anomaly_from_mean(observe_region(region_state, edge_index, edge_weight))
    edge_innov = jnp.concatenate([innov_flat[:, :halo], innov_flat[:, -halo:]], axis=1)
    edges = jnp.stack([edge_dev, edge_innov])
    lon_size = lax.axis_size("lon")
    up = [(i, (i + 1) % lon_size) for i in range(lon_size)]
    down = [(j, i) for i, j in up]
    west = lax.ppermute(edges[:, :, halo:], "lon", up)
    east = lax.ppermute(edges[:, :, :halo], "lon", down)
    middle_dev = anomaly_from_mean(
        observe_region(region_state, local_index[:, halo:-halo], local_weight[:, halo:-halo])
    )
    obs_dev = jnp.concatenate([edge_dev[:, :halo], middle_dev, edge_dev[:, halo:]], axis=1)
    model_anomaly = anomaly_from_mean(region_state)
    halo_blocks = halo // BLK
    block_count = patch_gridpoints // BLK
    candidate_count = block_count + 2 * halo_blocks
    code = block_codes(obs_list[0], tile_count[0], taper_class[0], candidate_count)
    own_code = code[:, halo_blocks:halo_blocks + block_count]
    halo_code = jnp.concatenate([code[:, :halo_blocks], code[:, halo_blocks + block_count:]], axis=1)
    tiles = taper_table(BLK, members)
    state_t = model_anomaly.T
    partial = update_call(
        own_code.reshape(-1), state_t, None, None, obs_dev, innov_flat.T, tiles, block_count, block_count
    )
    halo_obs = jnp.concatenate([west[0], east[0]], axis=1)
    halo_innov = jnp.concatenate([west[1], east[1]], axis=1)
    result_t = update_call(
        halo_code.reshape(-1),
        state_t,
        partial,
        region_state.T,
        halo_obs,
        halo_innov.T,
        tiles,
        block_count,
        2 * halo_blocks,
    )
    result = result_t.T
    return lax.all_to_all(
        result.reshape(members, band_rows, patch_meridian_lines),
        "wide",
        split_axis=0,
        concat_axis=1,
        tiled=True,
    )


def block_codes(lists, counts, classes, candidate_count):
    zero_code = 4
    entries = jnp.arange(lists.shape[1], dtype=jnp.int32)
    value = jnp.where(entries[None, :] < counts[:, None], classes, zero_code)
    hit = lists[:, :, None] == jnp.arange(candidate_count, dtype=jnp.int32)[None, None, :]
    code = zero_code + jnp.sum(jnp.where(hit, value[:, :, None] - zero_code, 0), axis=1)
    return jnp.clip(code, 0, zero_code).astype(jnp.int32)


def taper_table(tile_width, members):
    row_ids = lax.broadcasted_iota(jnp.float32, (tile_width, tile_width), 0)
    col_ids = lax.broadcasted_iota(jnp.float32, (tile_width, tile_width), 1)
    offset = row_ids - col_ids
    length = 8.0 * jnp.exp2(jnp.arange(4, dtype=jnp.float32))
    scaled = offset[None] / length[:, None, None]
    tiles = (1.0 / (1.0 + scaled * scaled)) / (members - 1.0)
    return jnp.concatenate([tiles, jnp.zeros((1, tile_width, tile_width), jnp.float32)], axis=0)


GROUP = 4


def update_call(code, state_t, partial, anchor_t, cand_obs, cand_innov_t, tiles, block_count, candidate_count):
    cells, members = state_t.shape
    rows = GROUP * BLK
    width = candidate_count * BLK
    final = anchor_t is not None

    def kernel(code_ref, st_ref, o_ref, it_ref, taper_ref, *rest):
        if final:
            part_ref, ft_ref, out_ref, cov_scr, tap_scr = rest
        else:
            out_ref, cov_scr, tap_scr = rest
        g = pl.program_id(0)
        cov_scr[...] = jnp.dot(st_ref[...], o_ref[...], preferred_element_type=jnp.float32)
        for sl in range(GROUP):
            s = g * GROUP + sl
            for b in range(candidate_count):
                c = code_ref[s * candidate_count + b]
                tile = cov_scr[sl * BLK:(sl + 1) * BLK, b * BLK:(b + 1) * BLK] * taper_ref[c]
                tap_scr[sl * BLK:(sl + 1) * BLK, b * BLK:(b + 1) * BLK] = tile.astype(jnp.bfloat16)
        change = jnp.dot(tap_scr[...], it_ref[...], preferred_element_type=jnp.float32)
        if final:
            total = part_ref[...] + change
            out_ref[...] = (ft_ref[...].astype(jnp.float32) + total).astype(jnp.bfloat16)
        else:
            out_ref[...] = change

    row_spec = pl.BlockSpec((rows, members), lambda g, code: (g, 0))
    in_specs = [
        row_spec,
        pl.BlockSpec((members, width), lambda g, code: (0, 0)),
        pl.BlockSpec((width, members), lambda g, code: (0, 0)),
        pl.BlockSpec(tiles.shape, lambda g, code: (0, 0, 0)),
    ]
    operands = [state_t, cand_obs, cand_innov_t, tiles]
    if final:
        in_specs += [row_spec, row_spec]
        operands += [partial, anchor_t]
    grid_spec = pltpu.PrefetchScalarGridSpec(
        num_scalar_prefetch=1,
        grid=(block_count // GROUP,),
        in_specs=in_specs,
        out_specs=row_spec,
        scratch_shapes=[
            pltpu.VMEM((rows, width), jnp.float32),
            pltpu.VMEM((rows, width), jnp.bfloat16),
        ],
    )
    out_type = jnp.bfloat16 if final else jnp.float32
    return pl.pallas_call(
        kernel,
        grid_spec=grid_spec,
        out_shape=jax.ShapeDtypeStruct((cells, members), out_type),
        cost_estimate=pl.CostEstimate(flops=4 * cells * members * width, transcendentals=0, bytes_accessed=8 * cells * members),
    )(code, *operands)


def solution(mesh):
    in_specs = (
        P("wide", None, "lon"),
        P(None, "wide", "lon"),
        P(None, None, "lon"),
        P(None, None, "lon"),
        P("lon", "wide", None),
        P("lon", "wide"),
        P("lon", "wide", None),
    )
    out_specs = P("wide", None, "lon")
    return jax.shard_map(body, mesh=mesh, in_specs=in_specs, out_specs=out_specs, check_vma=False)
```

```python
import math

import jax
import jax.numpy as jnp
from jax import lax
from jax.sharding import PartitionSpec as P
from jax.experimental import pallas as pl
from jax.experimental.pallas import tpu as pltpu

BLK = 128
HALO_BLK = 4


def padded_2(value, sides, width):
    for axis, dim in sides:
        size, length = (lax.axis_size(axis), value.shape[dim])
        up = [(i, (i + 1) % size) for i in range(size)]
        down = [(j, i) for i, j in up]
        last = lax.slice_in_dim(value, length - width, length, axis=dim)
        first = lax.slice_in_dim(value, 0, width, axis=dim)
        before = lax.ppermute(last, axis, up)
        after = lax.ppermute(first, axis, down)
        value = jnp.concatenate([before, value, after], axis=dim)
    return value


def column_halo(value, axis):
    size = lax.axis_size(axis)
    here = lax.axis_index(axis)
    edges = jnp.concatenate([value[..., :1], value[..., -1:]], axis=-1)
    spread = jnp.broadcast_to(edges[None], (size,) + edges.shape)
    got = lax.all_to_all(spread, axis, 0, 0, tiled=False)
    west = lax.dynamic_index_in_dim(got, (here - 1) % size, 0, keepdims=False)[..., 1:2]
    east = lax.dynamic_index_in_dim(got, (here + 1) % size, 0, keepdims=False)[..., 0:1]
    return west, east


def stencil(state, east, west, northern, southern):
    member_spread = east + west + northern + southern - 4.0 * state
    return (state + 0.2 * member_spread - 0.3 * (east - west)).astype(jnp.bfloat16)


def observe_region(state, index, weight):
    members, cells = state.shape
    count = index.shape[1]
    width = math.gcd(512, count)
    nblocks = count // width
    index_blocks = index.reshape(4, nblocks, width).transpose(1, 0, 2)
    weight_blocks = weight.reshape(4, nblocks, width).transpose(1, 0, 2)
    cell_ids = lax.broadcasted_iota(jnp.int32, (cells, width), 0)

    def observe_one_block(pieces):
        index_here, weight_here = pieces
        summed = jnp.zeros((members, width), jnp.float32)
        for k in range(4):
            selector = (cell_ids == index_here[k][None, :]).astype(jnp.bfloat16)
            picked = jnp.dot(state, selector, preferred_element_type=jnp.float32)
            summed = summed + weight_here[k][None, :] * picked
        return summed.astype(jnp.bfloat16)

    result = lax.map(observe_one_block, (index_blocks, weight_blocks))
    return result.transpose(1, 0, 2).reshape(members, count)


def anomaly_from_mean(state_values):
    centred = state_values.astype(jnp.float32)
    return (centred - jnp.mean(centred, axis=-2, keepdims=True)).astype(jnp.bfloat16)


def taper_tiles(classes, in_use, tile_width):
    row_ids = lax.broadcasted_iota(jnp.float32, (tile_width, tile_width), 0)
    col_ids = lax.broadcasted_iota(jnp.float32, (tile_width, tile_width), 1)
    offset = row_ids - col_ids
    length = 8.0 * jnp.exp2(classes.astype(jnp.float32))
    scaled = offset / length[..., None, None]
    return in_use[..., None, None] / (1.0 + scaled * scaled)


def body(background_ensemble, innov, obs_index, obs_weight, obs_list, tile_count, taper_class):
    state_values = background_ensemble.astype(jnp.float32)
    northern = jnp.pad(state_values[:, 1:, :], ((0, 0), (0, 1), (0, 0)))
    southern = jnp.pad(state_values[:, :-1, :], ((0, 0), (1, 0), (0, 0)))
    inner_east = jnp.pad(state_values[:, :, 1:], ((0, 0), (0, 0), (0, 1)))
    inner_west = jnp.pad(state_values[:, :, :-1], ((0, 0), (0, 0), (1, 0)))
    inner = stencil(state_values, inner_east, inner_west, northern, southern)
    west_col, east_col = column_halo(background_ensemble, "lon")
    first = stencil(
        state_values[..., :1], state_values[..., 1:2], west_col.astype(jnp.float32),
        northern[..., :1], southern[..., :1],
    )
    last = stencil(
        state_values[..., -1:], east_col.astype(jnp.float32), state_values[..., -2:-1],
        northern[..., -1:], southern[..., -1:],
    )
    prediction_increment = jnp.concatenate([first, inner[..., 1:-1], last], axis=-1)
    ensemble_lines_here, whole_parallel_set, patch_meridian_lines = prediction_increment.shape
    members = innov.shape[0]
    band_rows = innov.shape[1]
    patch_gridpoints = band_rows * patch_meridian_lines
    region = lax.all_to_all(prediction_increment, "wide", split_axis=1, concat_axis=0, tiled=True)
    region_state = region.reshape(members, patch_gridpoints)
    first_row = lax.axis_index("wide") * band_rows
    local_index = lax.dynamic_slice_in_dim(obs_index, first_row, band_rows, 1).reshape(
        4, patch_gridpoints
    )
    local_index = local_index - first_row * patch_meridian_lines
    local_weight = lax.dynamic_slice_in_dim(obs_weight, first_row, band_rows, 1).reshape(
        4, patch_gridpoints
    )
    halo = HALO_BLK * BLK
    innov_flat = innov.reshape(members, patch_gridpoints)
    edge_index = jnp.concatenate([local_index[:, :halo], local_index[:, -halo:]], axis=1)
    edge_weight = jnp.concatenate([local_weight[:, :halo], local_weight[:, -halo:]], axis=1)
    edge_dev = anomaly_from_mean(observe_region(region_state, edge_index, edge_weight))
    edge_innov = jnp.concatenate([innov_flat[:, :halo], innov_flat[:, -halo:]], axis=1)
    edges = jnp.stack([edge_dev, edge_innov])
    lon_size = lax.axis_size("lon")
    up = [(i, (i + 1) % lon_size) for i in range(lon_size)]
    down = [(j, i) for i, j in up]
    west = lax.ppermute(edges[:, :, halo:], "lon", up)
    east = lax.ppermute(edges[:, :, :halo], "lon", down)
    middle_dev = anomaly_from_mean(
        observe_region(region_state, local_index[:, halo:-halo], local_weight[:, halo:-halo])
    )
    obs_dev = jnp.concatenate([edge_dev[:, :halo], middle_dev, edge_dev[:, halo:]], axis=1)
    model_anomaly = anomaly_from_mean(region_state)
    halo_blocks = halo // BLK
    block_count = patch_gridpoints // BLK
    candidate_count = block_count + 2 * halo_blocks
    code = block_codes(obs_list[0], tile_count[0], taper_class[0], candidate_count)
    own_code = code[:, halo_blocks:halo_blocks + block_count]
    halo_code = jnp.concatenate([code[:, :halo_blocks], code[:, halo_blocks + block_count:]], axis=1)
    tiles = taper_table(BLK, members)
    state_t = model_anomaly.T
    partial = update_call(
        own_code.reshape(-1), state_t, None, None, obs_dev, innov_flat.T, tiles, block_count, block_count
    )
    halo_obs = jnp.concatenate([west[0], east[0]], axis=1)
    halo_innov = jnp.concatenate([west[1], east[1]], axis=1)
    result_t = update_call(
        halo_code.reshape(-1),
        state_t,
        partial,
        region_state.T,
        halo_obs,
        halo_innov.T,
        tiles,
        block_count,
        2 * halo_blocks,
    )
    result = result_t.T
    return lax.all_to_all(
        result.reshape(members, band_rows, patch_meridian_lines),
        "wide",
        split_axis=0,
        concat_axis=1,
        tiled=True,
    )


def block_codes(lists, counts, classes, candidate_count):
    zero_code = 4
    entries = jnp.arange(lists.shape[1], dtype=jnp.int32)
    value = jnp.where(entries[None, :] < counts[:, None], classes, zero_code)
    hit = lists[:, :, None] == jnp.arange(candidate_count, dtype=jnp.int32)[None, None, :]
    code = zero_code + jnp.sum(jnp.where(hit, value[:, :, None] - zero_code, 0), axis=1)
    return jnp.clip(code, 0, zero_code).astype(jnp.int32)


def taper_table(tile_width, members):
    row_ids = lax.broadcasted_iota(jnp.float32, (tile_width, tile_width), 0)
    col_ids = lax.broadcasted_iota(jnp.float32, (tile_width, tile_width), 1)
    offset = row_ids - col_ids
    length = 8.0 * jnp.exp2(jnp.arange(4, dtype=jnp.float32))
    scaled = offset[None] / length[:, None, None]
    tiles = (1.0 / (1.0 + scaled * scaled)) / (members - 1.0)
    return jnp.concatenate([tiles, jnp.zeros((1, tile_width, tile_width), jnp.float32)], axis=0)


GROUP = 4


def update_call(code, state_t, partial, anchor_t, cand_obs, cand_innov_t, tiles, block_count, candidate_count):
    cells, members = state_t.shape
    rows = GROUP * BLK
    width = candidate_count * BLK
    final = anchor_t is not None

    def kernel(code_ref, st_ref, o_ref, it_ref, taper_ref, *rest):
        if final:
            part_ref, ft_ref, out_ref, cov_scr, tap_scr = rest
        else:
            out_ref, cov_scr, tap_scr = rest
        g = pl.program_id(0)
        cov_scr[...] = jnp.dot(st_ref[...], o_ref[...], preferred_element_type=jnp.float32)
        for sl in range(GROUP):
            s = g * GROUP + sl
            for b in range(candidate_count):
                c = code_ref[s * candidate_count + b]
                tile = cov_scr[sl * BLK:(sl + 1) * BLK, b * BLK:(b + 1) * BLK] * taper_ref[c]
                tap_scr[sl * BLK:(sl + 1) * BLK, b * BLK:(b + 1) * BLK] = tile.astype(jnp.bfloat16)
        change = jnp.dot(tap_scr[...], it_ref[...], preferred_element_type=jnp.float32)
        if final:
            total = part_ref[...] + change
            out_ref[...] = (ft_ref[...].astype(jnp.float32) + total).astype(jnp.bfloat16)
        else:
            out_ref[...] = change

    row_spec = pl.BlockSpec((rows, members), lambda g, code: (g, 0))
    in_specs = [
        row_spec,
        pl.BlockSpec((members, width), lambda g, code: (0, 0)),
        pl.BlockSpec((width, members), lambda g, code: (0, 0)),
        pl.BlockSpec(tiles.shape, lambda g, code: (0, 0, 0)),
    ]
    operands = [state_t, cand_obs, cand_innov_t, tiles]
    if final:
        in_specs += [row_spec, row_spec]
        operands += [partial, anchor_t]
    grid_spec = pltpu.PrefetchScalarGridSpec(
        num_scalar_prefetch=1,
        grid=(block_count // GROUP,),
        in_specs=in_specs,
        out_specs=row_spec,
        scratch_shapes=[
            pltpu.VMEM((rows, width), jnp.float32),
            pltpu.VMEM((rows, width), jnp.bfloat16),
        ],
    )
    out_type = jnp.bfloat16 if final else jnp.float32
    return pl.pallas_call(
        kernel,
        grid_spec=grid_spec,
        out_shape=jax.ShapeDtypeStruct((cells, members), out_type),
        cost_estimate=pl.CostEstimate(flops=4 * cells * members * width, transcendentals=0, bytes_accessed=8 * cells * members),
    )(code, *operands)


def solution(mesh):
    in_specs = (
        P("wide", None, "lon"),
        P(None, "wide", "lon"),
        P(None, None, "lon"),
        P(None, None, "lon"),
        P("lon", "wide", None),
        P("lon", "wide"),
        P("lon", "wide", None),
    )
    out_specs = P("wide", None, "lon")
    return jax.shard_map(body, mesh=mesh, in_specs=in_specs, out_specs=out_specs, check_vma=False)
```

```python
import math

import jax
import jax.numpy as jnp
from jax import lax
from jax.sharding import PartitionSpec as P
from jax.experimental import pallas as pl
from jax.experimental.pallas import tpu as pltpu

BLK = 128
HALO_BLK = 4


def padded_2(value, sides, width):
    for axis, dim in sides:
        size, length = (lax.axis_size(axis), value.shape[dim])
        up = [(i, (i + 1) % size) for i in range(size)]
        down = [(j, i) for i, j in up]
        last = lax.slice_in_dim(value, length - width, length, axis=dim)
        first = lax.slice_in_dim(value, 0, width, axis=dim)
        before = lax.ppermute(last, axis, up)
        after = lax.ppermute(first, axis, down)
        value = jnp.concatenate([before, value, after], axis=dim)
    return value


def column_halo(value, axis):
    size = lax.axis_size(axis)
    here = lax.axis_index(axis)
    edges = jnp.concatenate([value[..., :1], value[..., -1:]], axis=-1)
    spread = jnp.broadcast_to(edges[None], (size,) + edges.shape)
    got = lax.all_to_all(spread, axis, 0, 0, tiled=False)
    west = lax.dynamic_index_in_dim(got, (here - 1) % size, 0, keepdims=False)[..., 1:2]
    east = lax.dynamic_index_in_dim(got, (here + 1) % size, 0, keepdims=False)[..., 0:1]
    return west, east


def forecast_call(state, west, east):
    members, rows, cols = state.shape

    def kernel(x_ref, w_ref, e_ref, o_ref):
        col = lax.broadcasted_iota(jnp.int32, (rows, cols), 1)
        row = lax.broadcasted_iota(jnp.int32, (rows, cols), 0)

        def one(m, carry):
            x = x_ref[m].astype(jnp.float32)
            east_n = jnp.where(col == cols - 1, e_ref[m].astype(jnp.float32), pltpu.roll(x, cols - 1, 1))
            west_n = jnp.where(col == 0, w_ref[m].astype(jnp.float32), pltpu.roll(x, 1, 1))
            north = jnp.where(row == rows - 1, 0.0, pltpu.roll(x, rows - 1, 0))
            south = jnp.where(row == 0, 0.0, pltpu.roll(x, 1, 0))
            spread = east_n + west_n + north + south - 4.0 * x
            o_ref[m] = (x + 0.2 * spread - 0.3 * (east_n - west_n)).astype(jnp.bfloat16)
            return carry

        lax.fori_loop(0, members, one, 0)

    return pl.pallas_call(kernel, out_shape=jax.ShapeDtypeStruct(state.shape, jnp.bfloat16))(state, west, east)


def observe_region(state, index, weight):
    members, cells = state.shape
    count = index.shape[1]
    width = math.gcd(512, count)
    nblocks = count // width
    index_blocks = index.reshape(4, nblocks, width).transpose(1, 0, 2)
    weight_blocks = weight.reshape(4, nblocks, width).transpose(1, 0, 2)
    cell_ids = lax.broadcasted_iota(jnp.int32, (cells, width), 0)

    def observe_one_block(pieces):
        index_here, weight_here = pieces
        summed = jnp.zeros((members, width), jnp.float32)
        for k in range(4):
            selector = (cell_ids == index_here[k][None, :]).astype(jnp.bfloat16)
            picked = jnp.dot(state, selector, preferred_element_type=jnp.float32)
            summed = summed + weight_here[k][None, :] * picked
        return summed.astype(jnp.bfloat16)

    result = lax.map(observe_one_block, (index_blocks, weight_blocks))
    return result.transpose(1, 0, 2).reshape(members, count)


def anomaly_from_mean(state_values):
    centred = state_values.astype(jnp.float32)
    return (centred - jnp.mean(centred, axis=-2, keepdims=True)).astype(jnp.bfloat16)


def taper_tiles(classes, in_use, tile_width):
    row_ids = lax.broadcasted_iota(jnp.float32, (tile_width, tile_width), 0)
    col_ids = lax.broadcasted_iota(jnp.float32, (tile_width, tile_width), 1)
    offset = row_ids - col_ids
    length = 8.0 * jnp.exp2(classes.astype(jnp.float32))
    scaled = offset / length[..., None, None]
    return in_use[..., None, None] / (1.0 + scaled * scaled)


def body(background_ensemble, innov, obs_index, obs_weight, obs_list, tile_count, taper_class):
    west_col, east_col = column_halo(background_ensemble, "lon")
    prediction_increment = forecast_call(background_ensemble, west_col, east_col)
    ensemble_lines_here, whole_parallel_set, patch_meridian_lines = prediction_increment.shape
    members = innov.shape[0]
    band_rows = innov.shape[1]
    patch_gridpoints = band_rows * patch_meridian_lines
    region = lax.all_to_all(prediction_increment, "wide", split_axis=1, concat_axis=0, tiled=True)
    region_state = region.reshape(members, patch_gridpoints)
    first_row = lax.axis_index("wide") * band_rows
    local_index = lax.dynamic_slice_in_dim(obs_index, first_row, band_rows, 1).reshape(
        4, patch_gridpoints
    )
    local_index = local_index - first_row * patch_meridian_lines
    local_weight = lax.dynamic_slice_in_dim(obs_weight, first_row, band_rows, 1).reshape(
        4, patch_gridpoints
    )
    halo = HALO_BLK * BLK
    innov_flat = innov.reshape(members, patch_gridpoints)
    edge_index = jnp.concatenate([local_index[:, :halo], local_index[:, -halo:]], axis=1)
    edge_weight = jnp.concatenate([local_weight[:, :halo], local_weight[:, -halo:]], axis=1)
    edge_dev = anomaly_from_mean(observe_region(region_state, edge_index, edge_weight))
    edge_innov = jnp.concatenate([innov_flat[:, :halo], innov_flat[:, -halo:]], axis=1)
    edges = jnp.stack([edge_dev, edge_innov])
    lon_size = lax.axis_size("lon")
    up = [(i, (i + 1) % lon_size) for i in range(lon_size)]
    down = [(j, i) for i, j in up]
    west = lax.ppermute(edges[:, :, halo:], "lon", up)
    east = lax.ppermute(edges[:, :, :halo], "lon", down)
    middle_dev = anomaly_from_mean(
        observe_region(region_state, local_index[:, halo:-halo], local_weight[:, halo:-halo])
    )
    obs_dev = jnp.concatenate([edge_dev[:, :halo], middle_dev, edge_dev[:, halo:]], axis=1)
    model_anomaly = anomaly_from_mean(region_state)
    halo_blocks = halo // BLK
    block_count = patch_gridpoints // BLK
    candidate_count = block_count + 2 * halo_blocks
    code = block_codes(obs_list[0], tile_count[0], taper_class[0], candidate_count)
    own_code = code[:, halo_blocks:halo_blocks + block_count]
    halo_code = jnp.concatenate([code[:, :halo_blocks], code[:, halo_blocks + block_count:]], axis=1)
    tiles = taper_table(BLK, members)
    state_t = model_anomaly.T
    partial = update_call(
        own_code.reshape(-1), state_t, None, None, obs_dev, innov_flat.T, tiles, block_count, block_count
    )
    halo_obs = jnp.concatenate([west[0], east[0]], axis=1)
    halo_innov = jnp.concatenate([west[1], east[1]], axis=1)
    result_t = update_call(
        halo_code.reshape(-1),
        state_t,
        partial,
        region_state.T,
        halo_obs,
        halo_innov.T,
        tiles,
        block_count,
        2 * halo_blocks,
    )
    result = result_t.T
    return lax.all_to_all(
        result.reshape(members, band_rows, patch_meridian_lines),
        "wide",
        split_axis=0,
        concat_axis=1,
        tiled=True,
    )


def block_codes(lists, counts, classes, candidate_count):
    zero_code = 4
    entries = jnp.arange(lists.shape[1], dtype=jnp.int32)
    value = jnp.where(entries[None, :] < counts[:, None], classes, zero_code)
    hit = lists[:, :, None] == jnp.arange(candidate_count, dtype=jnp.int32)[None, None, :]
    code = zero_code + jnp.sum(jnp.where(hit, value[:, :, None] - zero_code, 0), axis=1)
    return jnp.clip(code, 0, zero_code).astype(jnp.int32)


def taper_table(tile_width, members):
    row_ids = lax.broadcasted_iota(jnp.float32, (tile_width, tile_width), 0)
    col_ids = lax.broadcasted_iota(jnp.float32, (tile_width, tile_width), 1)
    offset = row_ids - col_ids
    length = 8.0 * jnp.exp2(jnp.arange(4, dtype=jnp.float32))
    scaled = offset[None] / length[:, None, None]
    tiles = (1.0 / (1.0 + scaled * scaled)) / (members - 1.0)
    return jnp.concatenate([tiles, jnp.zeros((1, tile_width, tile_width), jnp.float32)], axis=0)


GROUP = 4


def update_call(code, state_t, partial, anchor_t, cand_obs, cand_innov_t, tiles, block_count, candidate_count):
    cells, members = state_t.shape
    rows = GROUP * BLK
    width = candidate_count * BLK
    final = anchor_t is not None

    def kernel(code_ref, st_ref, o_ref, it_ref, taper_ref, *rest):
        if final:
            part_ref, ft_ref, out_ref, cov_scr, tap_scr = rest
        else:
            out_ref, cov_scr, tap_scr = rest
        g = pl.program_id(0)
        cov_scr[...] = jnp.dot(st_ref[...], o_ref[...], preferred_element_type=jnp.float32)
        for sl in range(GROUP):
            s = g * GROUP + sl
            for b in range(candidate_count):
                c = code_ref[s * candidate_count + b]
                tile = cov_scr[sl * BLK:(sl + 1) * BLK, b * BLK:(b + 1) * BLK] * taper_ref[c]
                tap_scr[sl * BLK:(sl + 1) * BLK, b * BLK:(b + 1) * BLK] = tile.astype(jnp.bfloat16)
        change = jnp.dot(tap_scr[...], it_ref[...], preferred_element_type=jnp.float32)
        if final:
            total = part_ref[...] + change
            out_ref[...] = (ft_ref[...].astype(jnp.float32) + total).astype(jnp.bfloat16)
        else:
            out_ref[...] = change

    row_spec = pl.BlockSpec((rows, members), lambda g, code: (g, 0))
    in_specs = [
        row_spec,
        pl.BlockSpec((members, width), lambda g, code: (0, 0)),
        pl.BlockSpec((width, members), lambda g, code: (0, 0)),
        pl.BlockSpec(tiles.shape, lambda g, code: (0, 0, 0)),
    ]
    operands = [state_t, cand_obs, cand_innov_t, tiles]
    if final:
        in_specs += [row_spec, row_spec]
        operands += [partial, anchor_t]
    grid_spec = pltpu.PrefetchScalarGridSpec(
        num_scalar_prefetch=1,
        grid=(block_count // GROUP,),
        in_specs=in_specs,
        out_specs=row_spec,
        scratch_shapes=[
            pltpu.VMEM((rows, width), jnp.float32),
            pltpu.VMEM((rows, width), jnp.bfloat16),
        ],
    )
    out_type = jnp.bfloat16 if final else jnp.float32
    return pl.pallas_call(
        kernel,
        grid_spec=grid_spec,
        out_shape=jax.ShapeDtypeStruct((cells, members), out_type),
        cost_estimate=pl.CostEstimate(flops=4 * cells * members * width, transcendentals=0, bytes_accessed=8 * cells * members),
    )(code, *operands)


def solution(mesh):
    in_specs = (
        P("wide", None, "lon"),
        P(None, "wide", "lon"),
        P(None, None, "lon"),
        P(None, None, "lon"),
        P("lon", "wide", None),
        P("lon", "wide"),
        P("lon", "wide", None),
    )
    out_specs = P("wide", None, "lon")
    return jax.shard_map(body, mesh=mesh, in_specs=in_specs, out_specs=out_specs, check_vma=False)
```

```python
import math

import jax
import jax.numpy as jnp
from jax import lax
from jax.sharding import PartitionSpec as P
from jax.experimental import pallas as pl
from jax.experimental.pallas import tpu as pltpu

BLK = 128
HALO_BLK = 4


def padded_2(value, sides, width):
    for axis, dim in sides:
        size, length = (lax.axis_size(axis), value.shape[dim])
        up = [(i, (i + 1) % size) for i in range(size)]
        down = [(j, i) for i, j in up]
        last = lax.slice_in_dim(value, length - width, length, axis=dim)
        first = lax.slice_in_dim(value, 0, width, axis=dim)
        before = lax.ppermute(last, axis, up)
        after = lax.ppermute(first, axis, down)
        value = jnp.concatenate([before, value, after], axis=dim)
    return value


def column_halo(value, axis):
    size = lax.axis_size(axis)
    here = lax.axis_index(axis)
    edges = jnp.concatenate([value[..., :1], value[..., -1:]], axis=-1)
    spread = jnp.broadcast_to(edges[None], (size,) + edges.shape)
    got = lax.all_to_all(spread, axis, 0, 0, tiled=False)
    west = lax.dynamic_index_in_dim(got, (here - 1) % size, 0, keepdims=False)[..., 1:2]
    east = lax.dynamic_index_in_dim(got, (here + 1) % size, 0, keepdims=False)[..., 0:1]
    return west, east


def forecast_call(state, west, east):
    members, rows, cols = state.shape

    def kernel(x_ref, w_ref, e_ref, o_ref):
        col = lax.broadcasted_iota(jnp.int32, (rows, cols), 1)
        row = lax.broadcasted_iota(jnp.int32, (rows, cols), 0)

        def one(m, carry):
            x = x_ref[m].astype(jnp.float32)
            east_n = jnp.where(col == cols - 1, e_ref[m].astype(jnp.float32), pltpu.roll(x, cols - 1, 1))
            west_n = jnp.where(col == 0, w_ref[m].astype(jnp.float32), pltpu.roll(x, 1, 1))
            north = jnp.where(row == rows - 1, 0.0, pltpu.roll(x, rows - 1, 0))
            south = jnp.where(row == 0, 0.0, pltpu.roll(x, 1, 0))
            spread = east_n + west_n + north + south - 4.0 * x
            o_ref[m] = (x + 0.2 * spread - 0.3 * (east_n - west_n)).astype(jnp.bfloat16)
            return carry

        lax.fori_loop(0, members, one, 0)

    return pl.pallas_call(kernel, out_shape=jax.ShapeDtypeStruct(state.shape, jnp.bfloat16))(state, west, east)


def observe_region(state, index, weight):
    members, cells = state.shape
    count = index.shape[1]
    width = math.gcd(512, count)
    nblocks = count // width
    index_blocks = index.reshape(4, nblocks, width).transpose(1, 0, 2)
    weight_blocks = weight.reshape(4, nblocks, width).transpose(1, 0, 2)
    cell_ids = lax.broadcasted_iota(jnp.int32, (cells, width), 0)

    def observe_one_block(pieces):
        index_here, weight_here = pieces
        summed = jnp.zeros((members, width), jnp.float32)
        for k in range(4):
            selector = (cell_ids == index_here[k][None, :]).astype(jnp.bfloat16)
            picked = jnp.dot(state, selector, preferred_element_type=jnp.float32)
            summed = summed + weight_here[k][None, :] * picked
        return summed.astype(jnp.bfloat16)

    result = lax.map(observe_one_block, (index_blocks, weight_blocks))
    return result.transpose(1, 0, 2).reshape(members, count)


def anomaly_from_mean(state_values):
    centred = state_values.astype(jnp.float32)
    return (centred - jnp.mean(centred, axis=-2, keepdims=True)).astype(jnp.bfloat16)


def taper_tiles(classes, in_use, tile_width):
    row_ids = lax.broadcasted_iota(jnp.float32, (tile_width, tile_width), 0)
    col_ids = lax.broadcasted_iota(jnp.float32, (tile_width, tile_width), 1)
    offset = row_ids - col_ids
    length = 8.0 * jnp.exp2(classes.astype(jnp.float32))
    scaled = offset / length[..., None, None]
    return in_use[..., None, None] / (1.0 + scaled * scaled)


def body(background_ensemble, innov, obs_index, obs_weight, obs_list, tile_count, taper_class):
    west_col, east_col = column_halo(background_ensemble, "lon")
    prediction_increment = forecast_call(background_ensemble, west_col, east_col)
    ensemble_lines_here, whole_parallel_set, patch_meridian_lines = prediction_increment.shape
    members = innov.shape[0]
    band_rows = innov.shape[1]
    patch_gridpoints = band_rows * patch_meridian_lines
    region = lax.all_to_all(prediction_increment, "wide", split_axis=1, concat_axis=0, tiled=True)
    region_state = region.reshape(members, patch_gridpoints)
    first_row = lax.axis_index("wide") * band_rows
    local_index = lax.dynamic_slice_in_dim(obs_index, first_row, band_rows, 1).reshape(
        4, patch_gridpoints
    )
    local_index = local_index - first_row * patch_meridian_lines
    local_weight = lax.dynamic_slice_in_dim(obs_weight, first_row, band_rows, 1).reshape(
        4, patch_gridpoints
    )
    halo = HALO_BLK * BLK
    innov_flat = innov.reshape(members, patch_gridpoints)
    edge_index = jnp.concatenate([local_index[:, :halo], local_index[:, -halo:]], axis=1)
    edge_weight = jnp.concatenate([local_weight[:, :halo], local_weight[:, -halo:]], axis=1)
    edge_dev = anomaly_from_mean(observe_region(region_state, edge_index, edge_weight))
    edge_innov = jnp.concatenate([innov_flat[:, :halo], innov_flat[:, -halo:]], axis=1)
    edges = jnp.stack([edge_dev, edge_innov])
    lon_size = lax.axis_size("lon")
    up = [(i, (i + 1) % lon_size) for i in range(lon_size)]
    down = [(j, i) for i, j in up]
    west = lax.ppermute(edges[:, :, halo:], "lon", up)
    east = lax.ppermute(edges[:, :, :halo], "lon", down)
    middle_dev = anomaly_from_mean(
        observe_region(region_state, local_index[:, halo:-halo], local_weight[:, halo:-halo])
    )
    obs_dev = jnp.concatenate([edge_dev[:, :halo], middle_dev, edge_dev[:, halo:]], axis=1)
    model_anomaly = anomaly_from_mean(region_state)
    halo_blocks = halo // BLK
    block_count = patch_gridpoints // BLK
    candidate_count = block_count + 2 * halo_blocks
    code = block_codes(obs_list[0], tile_count[0], taper_class[0], candidate_count)
    own_code = code[:, halo_blocks:halo_blocks + block_count]
    halo_code = jnp.concatenate([code[:, :halo_blocks], code[:, halo_blocks + block_count:]], axis=1)
    tiles = taper_table(BLK, members)
    partial = update_call(
        own_code.reshape(-1), model_anomaly, None, None, obs_dev, innov_flat, tiles, block_count, block_count
    )
    halo_obs = jnp.concatenate([west[0], east[0]], axis=1)
    halo_innov = jnp.concatenate([west[1], east[1]], axis=1)
    result = update_call(
        halo_code.reshape(-1),
        model_anomaly,
        partial,
        region_state,
        halo_obs,
        halo_innov,
        tiles,
        block_count,
        2 * halo_blocks,
    )
    return lax.all_to_all(
        result.reshape(members, band_rows, patch_meridian_lines),
        "wide",
        split_axis=0,
        concat_axis=1,
        tiled=True,
    )


def block_codes(lists, counts, classes, candidate_count):
    zero_code = 4
    entries = jnp.arange(lists.shape[1], dtype=jnp.int32)
    value = jnp.where(entries[None, :] < counts[:, None], classes, zero_code)
    hit = lists[:, :, None] == jnp.arange(candidate_count, dtype=jnp.int32)[None, None, :]
    code = zero_code + jnp.sum(jnp.where(hit, value[:, :, None] - zero_code, 0), axis=1)
    return jnp.clip(code, 0, zero_code).astype(jnp.int32)


def taper_table(tile_width, members):
    row_ids = lax.broadcasted_iota(jnp.float32, (tile_width, tile_width), 0)
    col_ids = lax.broadcasted_iota(jnp.float32, (tile_width, tile_width), 1)
    offset = row_ids - col_ids
    length = 8.0 * jnp.exp2(jnp.arange(4, dtype=jnp.float32))
    scaled = offset[None] / length[:, None, None]
    tiles = (1.0 / (1.0 + scaled * scaled)) / (members - 1.0)
    return jnp.concatenate([tiles, jnp.zeros((1, tile_width, tile_width), jnp.float32)], axis=0)


GROUP = 4


def update_call(code, state, partial, anchor, cand_obs, cand_innov, tiles, block_count, candidate_count):
    members, cells = state.shape
    rows = GROUP * BLK
    width = candidate_count * BLK
    final = anchor is not None

    def kernel(code_ref, s_ref, o_ref, i_ref, taper_ref, *rest):
        if final:
            part_ref, f_ref, out_ref, cov_scr, tap_scr = rest
        else:
            out_ref, cov_scr, tap_scr = rest
        g = pl.program_id(0)
        cov_scr[...] = lax.dot_general(
            s_ref[...], o_ref[...], (((0,), (0,)), ((), ())), preferred_element_type=jnp.float32
        )
        for sl in range(GROUP):
            s = g * GROUP + sl
            for b in range(candidate_count):
                c = code_ref[s * candidate_count + b]
                tile = cov_scr[sl * BLK:(sl + 1) * BLK, b * BLK:(b + 1) * BLK] * taper_ref[c]
                tap_scr[sl * BLK:(sl + 1) * BLK, b * BLK:(b + 1) * BLK] = tile.astype(jnp.bfloat16)
        change = lax.dot_general(
            i_ref[...], tap_scr[...], (((1,), (1,)), ((), ())), preferred_element_type=jnp.float32
        )
        if final:
            total = part_ref[...] + change
            out_ref[...] = (f_ref[...].astype(jnp.float32) + total).astype(jnp.bfloat16)
        else:
            out_ref[...] = change

    col_spec = pl.BlockSpec((members, rows), lambda g, code: (0, g))
    in_specs = [
        col_spec,
        pl.BlockSpec((members, width), lambda g, code: (0, 0)),
        pl.BlockSpec((members, width), lambda g, code: (0, 0)),
        pl.BlockSpec(tiles.shape, lambda g, code: (0, 0, 0)),
    ]
    operands = [state, cand_obs, cand_innov, tiles]
    if final:
        in_specs += [col_spec, col_spec]
        operands += [partial, anchor]
    grid_spec = pltpu.PrefetchScalarGridSpec(
        num_scalar_prefetch=1,
        grid=(block_count // GROUP,),
        in_specs=in_specs,
        out_specs=col_spec,
        scratch_shapes=[
            pltpu.VMEM((rows, width), jnp.float32),
            pltpu.VMEM((rows, width), jnp.bfloat16),
        ],
    )
    out_type = jnp.bfloat16 if final else jnp.float32
    return pl.pallas_call(
        kernel,
        grid_spec=grid_spec,
        out_shape=jax.ShapeDtypeStruct((members, cells), out_type),
        cost_estimate=pl.CostEstimate(flops=4 * cells * members * width, transcendentals=0, bytes_accessed=8 * cells * members),
    )(code, *operands)


def solution(mesh):
    in_specs = (
        P("wide", None, "lon"),
        P(None, "wide", "lon"),
        P(None, None, "lon"),
        P(None, None, "lon"),
        P("lon", "wide", None),
        P("lon", "wide"),
        P("lon", "wide", None),
    )
    out_specs = P("wide", None, "lon")
    return jax.shard_map(body, mesh=mesh, in_specs=in_specs, out_specs=out_specs, check_vma=False)
```

```python
import math

import jax
import jax.numpy as jnp
from jax import lax
from jax.sharding import PartitionSpec as P
from jax.experimental import pallas as pl
from jax.experimental.pallas import tpu as pltpu

BLK = 128
HALO_BLK = 4


def padded_2(value, sides, width):
    for axis, dim in sides:
        size, length = (lax.axis_size(axis), value.shape[dim])
        up = [(i, (i + 1) % size) for i in range(size)]
        down = [(j, i) for i, j in up]
        last = lax.slice_in_dim(value, length - width, length, axis=dim)
        first = lax.slice_in_dim(value, 0, width, axis=dim)
        before = lax.ppermute(last, axis, up)
        after = lax.ppermute(first, axis, down)
        value = jnp.concatenate([before, value, after], axis=dim)
    return value


def column_halo(value, axis):
    size = lax.axis_size(axis)
    here = lax.axis_index(axis)
    edges = jnp.concatenate([value[..., :1], value[..., -1:]], axis=-1)
    spread = jnp.broadcast_to(edges[None], (size,) + edges.shape)
    got = lax.all_to_all(spread, axis, 0, 0, tiled=False)
    west = lax.dynamic_index_in_dim(got, (here - 1) % size, 0, keepdims=False)[..., 1:2]
    east = lax.dynamic_index_in_dim(got, (here + 1) % size, 0, keepdims=False)[..., 0:1]
    return west, east


def forecast_call(state, west, east):
    members, rows, cols = state.shape

    def kernel(x_ref, w_ref, e_ref, o_ref):
        col = lax.broadcasted_iota(jnp.int32, (rows, cols), 1)
        row = lax.broadcasted_iota(jnp.int32, (rows, cols), 0)

        def one(m, carry):
            x = x_ref[m].astype(jnp.float32)
            east_n = jnp.where(col == cols - 1, e_ref[m].astype(jnp.float32), pltpu.roll(x, cols - 1, 1))
            west_n = jnp.where(col == 0, w_ref[m].astype(jnp.float32), pltpu.roll(x, 1, 1))
            north = jnp.where(row == rows - 1, 0.0, pltpu.roll(x, rows - 1, 0))
            south = jnp.where(row == 0, 0.0, pltpu.roll(x, 1, 0))
            spread = east_n + west_n + north + south - 4.0 * x
            o_ref[m] = (x + 0.2 * spread - 0.3 * (east_n - west_n)).astype(jnp.bfloat16)
            return carry

        lax.fori_loop(0, members, one, 0)

    return pl.pallas_call(kernel, out_shape=jax.ShapeDtypeStruct(state.shape, jnp.bfloat16))(state, west, east)


def observe_region(state, index, weight):
    members, cells = state.shape
    count = index.shape[1]
    width = math.gcd(512, count)
    nblocks = count // width
    index_blocks = index.reshape(4, nblocks, width).transpose(1, 0, 2)
    weight_blocks = weight.reshape(4, nblocks, width).transpose(1, 0, 2)
    cell_ids = lax.broadcasted_iota(jnp.int32, (cells, width), 0)

    def observe_one_block(pieces):
        index_here, weight_here = pieces
        summed = jnp.zeros((members, width), jnp.float32)
        for k in range(4):
            selector = (cell_ids == index_here[k][None, :]).astype(jnp.bfloat16)
            picked = jnp.dot(state, selector, preferred_element_type=jnp.float32)
            summed = summed + weight_here[k][None, :] * picked
        return summed.astype(jnp.bfloat16)

    result = lax.map(observe_one_block, (index_blocks, weight_blocks))
    return result.transpose(1, 0, 2).reshape(members, count)


OBS_STEP = 256
def observe_dev_call(state, index, weight):
    members, cells = state.shape
    count = index.shape[1]
    def kernel(f_ref, i_ref, w_ref, o_ref):
        cell_ids = lax.broadcasted_iota(jnp.int32, (cells, OBS_STEP), 0)
        f = f_ref[...]
        summed = jnp.zeros((members, OBS_STEP), jnp.float32)
        for k in range(4):
            selector = (cell_ids == i_ref[k:k + 1, :]).astype(jnp.bfloat16)
            picked = jnp.dot(f, selector, preferred_element_type=jnp.float32)
            summed = summed + w_ref[k:k + 1, :] * picked
        ens = summed.astype(jnp.bfloat16).astype(jnp.float32)
        mean = jnp.sum(ens, axis=0, keepdims=True) / members
        o_ref[...] = (ens - mean).astype(jnp.bfloat16)
    return pl.pallas_call(
        kernel,
        grid=(count // OBS_STEP,),
        in_specs=[
            pl.BlockSpec((members, cells), lambda j: (0, 0)),
            pl.BlockSpec((4, OBS_STEP), lambda j: (0, j)),
            pl.BlockSpec((4, OBS_STEP), lambda j: (0, j)),
        ],
        out_specs=pl.BlockSpec((members, OBS_STEP), lambda j: (0, j)),
        out_shape=jax.ShapeDtypeStruct((members, count), jnp.bfloat16),
    )(state, index, weight)
def anomaly_from_mean(state_values):
    centred = state_values.astype(jnp.float32)
    return (centred - jnp.mean(centred, axis=-2, keepdims=True)).astype(jnp.bfloat16)


def taper_tiles(classes, in_use, tile_width):
    row_ids = lax.broadcasted_iota(jnp.float32, (tile_width, tile_width), 0)
    col_ids = lax.broadcasted_iota(jnp.float32, (tile_width, tile_width), 1)
    offset = row_ids - col_ids
    length = 8.0 * jnp.exp2(classes.astype(jnp.float32))
    scaled = offset / length[..., None, None]
    return in_use[..., None, None] / (1.0 + scaled * scaled)


def body(background_ensemble, innov, obs_index, obs_weight, obs_list, tile_count, taper_class):
    west_col, east_col = column_halo(background_ensemble, "lon")
    prediction_increment = forecast_call(background_ensemble, west_col, east_col)
    ensemble_lines_here, whole_parallel_set, patch_meridian_lines = prediction_increment.shape
    members = innov.shape[0]
    band_rows = innov.shape[1]
    patch_gridpoints = band_rows * patch_meridian_lines
    region = lax.all_to_all(prediction_increment, "wide", split_axis=1, concat_axis=0, tiled=True)
    region_state = region.reshape(members, patch_gridpoints)
    first_row = lax.axis_index("wide") * band_rows
    local_index = lax.dynamic_slice_in_dim(obs_index, first_row, band_rows, 1).reshape(
        4, patch_gridpoints
    )
    local_index = local_index - first_row * patch_meridian_lines
    local_weight = lax.dynamic_slice_in_dim(obs_weight, first_row, band_rows, 1).reshape(
        4, patch_gridpoints
    )
    halo = HALO_BLK * BLK
    innov_flat = innov.reshape(members, patch_gridpoints)
    edge_index = jnp.concatenate([local_index[:, :halo], local_index[:, -halo:]], axis=1)
    edge_weight = jnp.concatenate([local_weight[:, :halo], local_weight[:, -halo:]], axis=1)
    edge_dev = observe_dev_call(region_state, edge_index, edge_weight)
    edge_innov = jnp.concatenate([innov_flat[:, :halo], innov_flat[:, -halo:]], axis=1)
    edges = jnp.stack([edge_dev, edge_innov])
    lon_size = lax.axis_size("lon")
    up = [(i, (i + 1) % lon_size) for i in range(lon_size)]
    down = [(j, i) for i, j in up]
    west = lax.ppermute(edges[:, :, halo:], "lon", up)
    east = lax.ppermute(edges[:, :, :halo], "lon", down)
    middle_dev = observe_dev_call(region_state, local_index[:, halo:-halo], local_weight[:, halo:-halo])
    obs_dev = jnp.concatenate([edge_dev[:, :halo], middle_dev, edge_dev[:, halo:]], axis=1)
    model_anomaly = anomaly_from_mean(region_state)
    halo_blocks = halo // BLK
    block_count = patch_gridpoints // BLK
    candidate_count = block_count + 2 * halo_blocks
    code = block_codes(obs_list[0], tile_count[0], taper_class[0], candidate_count)
    own_code = code[:, halo_blocks:halo_blocks + block_count]
    halo_code = jnp.concatenate([code[:, :halo_blocks], code[:, halo_blocks + block_count:]], axis=1)
    tiles = taper_table(BLK, members)
    partial = update_call(
        own_code.reshape(-1), model_anomaly, None, None, obs_dev, innov_flat, tiles, block_count, block_count
    )
    halo_obs = jnp.concatenate([west[0], east[0]], axis=1)
    halo_innov = jnp.concatenate([west[1], east[1]], axis=1)
    result = update_call(
        halo_code.reshape(-1),
        model_anomaly,
        partial,
        region_state,
        halo_obs,
        halo_innov,
        tiles,
        block_count,
        2 * halo_blocks,
    )
    return lax.all_to_all(
        result.reshape(members, band_rows, patch_meridian_lines),
        "wide",
        split_axis=0,
        concat_axis=1,
        tiled=True,
    )


def block_codes(lists, counts, classes, candidate_count):
    zero_code = 4
    entries = jnp.arange(lists.shape[1], dtype=jnp.int32)
    value = jnp.where(entries[None, :] < counts[:, None], classes, zero_code)
    hit = lists[:, :, None] == jnp.arange(candidate_count, dtype=jnp.int32)[None, None, :]
    code = zero_code + jnp.sum(jnp.where(hit, value[:, :, None] - zero_code, 0), axis=1)
    return jnp.clip(code, 0, zero_code).astype(jnp.int32)


def taper_table(tile_width, members):
    row_ids = lax.broadcasted_iota(jnp.float32, (tile_width, tile_width), 0)
    col_ids = lax.broadcasted_iota(jnp.float32, (tile_width, tile_width), 1)
    offset = row_ids - col_ids
    length = 8.0 * jnp.exp2(jnp.arange(4, dtype=jnp.float32))
    scaled = offset[None] / length[:, None, None]
    tiles = (1.0 / (1.0 + scaled * scaled)) / (members - 1.0)
    return jnp.concatenate([tiles, jnp.zeros((1, tile_width, tile_width), jnp.float32)], axis=0)


GROUP = 4


def update_call(code, state, partial, anchor, cand_obs, cand_innov, tiles, block_count, candidate_count):
    members, cells = state.shape
    rows = GROUP * BLK
    width = candidate_count * BLK
    final = anchor is not None

    def kernel(code_ref, s_ref, o_ref, i_ref, taper_ref, *rest):
        if final:
            part_ref, f_ref, out_ref, cov_scr, tap_scr = rest
        else:
            out_ref, cov_scr, tap_scr = rest
        g = pl.program_id(0)
        cov_scr[...] = lax.dot_general(
            s_ref[...], o_ref[...], (((0,), (0,)), ((), ())), preferred_element_type=jnp.float32
        )
        for sl in range(GROUP):
            s = g * GROUP + sl
            for b in range(candidate_count):
                c = code_ref[s * candidate_count + b]
                tile = cov_scr[sl * BLK:(sl + 1) * BLK, b * BLK:(b + 1) * BLK] * taper_ref[c]
                tap_scr[sl * BLK:(sl + 1) * BLK, b * BLK:(b + 1) * BLK] = tile.astype(jnp.bfloat16)
        change = lax.dot_general(
            i_ref[...], tap_scr[...], (((1,), (1,)), ((), ())), preferred_element_type=jnp.float32
        )
        if final:
            total = part_ref[...] + change
            out_ref[...] = (f_ref[...].astype(jnp.float32) + total).astype(jnp.bfloat16)
        else:
            out_ref[...] = change

    col_spec = pl.BlockSpec((members, rows), lambda g, code: (0, g))
    in_specs = [
        col_spec,
        pl.BlockSpec((members, width), lambda g, code: (0, 0)),
        pl.BlockSpec((members, width), lambda g, code: (0, 0)),
        pl.BlockSpec(tiles.shape, lambda g, code: (0, 0, 0)),
    ]
    operands = [state, cand_obs, cand_innov, tiles]
    if final:
        in_specs += [col_spec, col_spec]
        operands += [partial, anchor]
    grid_spec = pltpu.PrefetchScalarGridSpec(
        num_scalar_prefetch=1,
        grid=(block_count // GROUP,),
        in_specs=in_specs,
        out_specs=col_spec,
        scratch_shapes=[
            pltpu.VMEM((rows, width), jnp.float32),
            pltpu.VMEM((rows, width), jnp.bfloat16),
        ],
    )
    out_type = jnp.bfloat16 if final else jnp.float32
    return pl.pallas_call(
        kernel,
        grid_spec=grid_spec,
        out_shape=jax.ShapeDtypeStruct((members, cells), out_type),
        cost_estimate=pl.CostEstimate(flops=4 * cells * members * width, transcendentals=0, bytes_accessed=8 * cells * members),
    )(code, *operands)


def solution(mesh):
    in_specs = (
        P("wide", None, "lon"),
        P(None, "wide", "lon"),
        P(None, None, "lon"),
        P(None, None, "lon"),
        P("lon", "wide", None),
        P("lon", "wide"),
        P("lon", "wide", None),
    )
    out_specs = P("wide", None, "lon")
    return jax.shard_map(body, mesh=mesh, in_specs=in_specs, out_specs=out_specs, check_vma=False)
```

```python
import math

import jax
import jax.numpy as jnp
from jax import lax
from jax.sharding import PartitionSpec as P
from jax.experimental import pallas as pl
from jax.experimental.pallas import tpu as pltpu

BLK = 128
HALO_BLK = 4


def padded_2(value, sides, width):
    for axis, dim in sides:
        size, length = (lax.axis_size(axis), value.shape[dim])
        up = [(i, (i + 1) % size) for i in range(size)]
        down = [(j, i) for i, j in up]
        last = lax.slice_in_dim(value, length - width, length, axis=dim)
        first = lax.slice_in_dim(value, 0, width, axis=dim)
        before = lax.ppermute(last, axis, up)
        after = lax.ppermute(first, axis, down)
        value = jnp.concatenate([before, value, after], axis=dim)
    return value


def column_halo(value, axis):
    size = lax.axis_size(axis)
    here = lax.axis_index(axis)
    edges = jnp.concatenate([value[..., :1], value[..., -1:]], axis=-1)
    spread = jnp.broadcast_to(edges[None], (size,) + edges.shape)
    got = lax.all_to_all(spread, axis, 0, 0, tiled=False)
    west = lax.dynamic_index_in_dim(got, (here - 1) % size, 0, keepdims=False)[..., 1:2]
    east = lax.dynamic_index_in_dim(got, (here + 1) % size, 0, keepdims=False)[..., 0:1]
    return west, east


def forecast_call(state, west, east):
    members, rows, cols = state.shape

    def kernel(x_ref, w_ref, e_ref, o_ref):
        col = lax.broadcasted_iota(jnp.int32, (rows, cols), 1)
        row = lax.broadcasted_iota(jnp.int32, (rows, cols), 0)

        def one(m, carry):
            x = x_ref[m].astype(jnp.float32)
            east_n = jnp.where(col == cols - 1, e_ref[m].astype(jnp.float32), pltpu.roll(x, cols - 1, 1))
            west_n = jnp.where(col == 0, w_ref[m].astype(jnp.float32), pltpu.roll(x, 1, 1))
            north = jnp.where(row == rows - 1, 0.0, pltpu.roll(x, rows - 1, 0))
            south = jnp.where(row == 0, 0.0, pltpu.roll(x, 1, 0))
            spread = east_n + west_n + north + south - 4.0 * x
            o_ref[m] = (x + 0.2 * spread - 0.3 * (east_n - west_n)).astype(jnp.bfloat16)
            return carry

        lax.fori_loop(0, members, one, 0, unroll=4)

    return pl.pallas_call(kernel, out_shape=jax.ShapeDtypeStruct(state.shape, jnp.bfloat16))(state, west, east)


def observe_region(state, index, weight):
    members, cells = state.shape
    count = index.shape[1]
    width = math.gcd(512, count)
    nblocks = count // width
    index_blocks = index.reshape(4, nblocks, width).transpose(1, 0, 2)
    weight_blocks = weight.reshape(4, nblocks, width).transpose(1, 0, 2)
    cell_ids = lax.broadcasted_iota(jnp.int32, (cells, width), 0)

    def observe_one_block(pieces):
        index_here, weight_here = pieces
        summed = jnp.zeros((members, width), jnp.float32)
        for k in range(4):
            selector = (cell_ids == index_here[k][None, :]).astype(jnp.bfloat16)
            picked = jnp.dot(state, selector, preferred_element_type=jnp.float32)
            summed = summed + weight_here[k][None, :] * picked
        return summed.astype(jnp.bfloat16)

    result = lax.map(observe_one_block, (index_blocks, weight_blocks))
    return result.transpose(1, 0, 2).reshape(members, count)


OBS_STEP = 256
def observe_dev_call(state, index, weight):
    members, cells = state.shape
    count = index.shape[1]
    def kernel(f_ref, i_ref, w_ref, o_ref):
        cell_ids = lax.broadcasted_iota(jnp.int32, (cells, OBS_STEP), 0)
        f = f_ref[...]
        summed = jnp.zeros((members, OBS_STEP), jnp.float32)
        for k in range(4):
            selector = (cell_ids == i_ref[k:k + 1, :]).astype(jnp.bfloat16)
            picked = jnp.dot(f, selector, preferred_element_type=jnp.float32)
            summed = summed + w_ref[k:k + 1, :] * picked
        ens = summed.astype(jnp.bfloat16).astype(jnp.float32)
        mean = jnp.sum(ens, axis=0, keepdims=True) / members
        o_ref[...] = (ens - mean).astype(jnp.bfloat16)
    return pl.pallas_call(
        kernel,
        grid=(count // OBS_STEP,),
        in_specs=[
            pl.BlockSpec((members, cells), lambda j: (0, 0)),
            pl.BlockSpec((4, OBS_STEP), lambda j: (0, j)),
            pl.BlockSpec((4, OBS_STEP), lambda j: (0, j)),
        ],
        out_specs=pl.BlockSpec((members, OBS_STEP), lambda j: (0, j)),
        out_shape=jax.ShapeDtypeStruct((members, count), jnp.bfloat16),
    )(state, index, weight)
def anomaly_from_mean(state_values):
    centred = state_values.astype(jnp.float32)
    return (centred - jnp.mean(centred, axis=-2, keepdims=True)).astype(jnp.bfloat16)


def taper_tiles(classes, in_use, tile_width):
    row_ids = lax.broadcasted_iota(jnp.float32, (tile_width, tile_width), 0)
    col_ids = lax.broadcasted_iota(jnp.float32, (tile_width, tile_width), 1)
    offset = row_ids - col_ids
    length = 8.0 * jnp.exp2(classes.astype(jnp.float32))
    scaled = offset / length[..., None, None]
    return in_use[..., None, None] / (1.0 + scaled * scaled)


def body(background_ensemble, innov, obs_index, obs_weight, obs_list, tile_count, taper_class):
    west_col, east_col = column_halo(background_ensemble, "lon")
    prediction_increment = forecast_call(background_ensemble, west_col, east_col)
    ensemble_lines_here, whole_parallel_set, patch_meridian_lines = prediction_increment.shape
    members = innov.shape[0]
    band_rows = innov.shape[1]
    patch_gridpoints = band_rows * patch_meridian_lines
    region = lax.all_to_all(prediction_increment, "wide", split_axis=1, concat_axis=0, tiled=True)
    region_state = region.reshape(members, patch_gridpoints)
    first_row = lax.axis_index("wide") * band_rows
    local_index = lax.dynamic_slice_in_dim(obs_index, first_row, band_rows, 1).reshape(
        4, patch_gridpoints
    )
    local_index = local_index - first_row * patch_meridian_lines
    local_weight = lax.dynamic_slice_in_dim(obs_weight, first_row, band_rows, 1).reshape(
        4, patch_gridpoints
    )
    halo = HALO_BLK * BLK
    innov_flat = innov.reshape(members, patch_gridpoints)
    edge_index = jnp.concatenate([local_index[:, :halo], local_index[:, -halo:]], axis=1)
    edge_weight = jnp.concatenate([local_weight[:, :halo], local_weight[:, -halo:]], axis=1)
    edge_dev = observe_dev_call(region_state, edge_index, edge_weight)
    edge_innov = jnp.concatenate([innov_flat[:, :halo], innov_flat[:, -halo:]], axis=1)
    edges = jnp.stack([edge_dev, edge_innov])
    lon_size = lax.axis_size("lon")
    up = [(i, (i + 1) % lon_size) for i in range(lon_size)]
    down = [(j, i) for i, j in up]
    west = lax.ppermute(edges[:, :, halo:], "lon", up)
    east = lax.ppermute(edges[:, :, :halo], "lon", down)
    middle_dev = observe_dev_call(region_state, local_index[:, halo:-halo], local_weight[:, halo:-halo])
    obs_dev = jnp.concatenate([edge_dev[:, :halo], middle_dev, edge_dev[:, halo:]], axis=1)
    model_anomaly = anomaly_from_mean(region_state)
    halo_blocks = halo // BLK
    block_count = patch_gridpoints // BLK
    candidate_count = block_count + 2 * halo_blocks
    code = block_codes(obs_list[0], tile_count[0], taper_class[0], candidate_count)
    own_code = code[:, halo_blocks:halo_blocks + block_count]
    halo_code = jnp.concatenate([code[:, :halo_blocks], code[:, halo_blocks + block_count:]], axis=1)
    tiles = taper_table(BLK, members)
    partial = update_call(
        own_code.reshape(-1), model_anomaly, None, None, obs_dev, innov_flat, tiles, block_count, block_count
    )
    halo_obs = jnp.concatenate([west[0], east[0]], axis=1)
    halo_innov = jnp.concatenate([west[1], east[1]], axis=1)
    result = update_call(
        halo_code.reshape(-1),
        model_anomaly,
        partial,
        region_state,
        halo_obs,
        halo_innov,
        tiles,
        block_count,
        2 * halo_blocks,
    )
    return lax.all_to_all(
        result.reshape(members, band_rows, patch_meridian_lines),
        "wide",
        split_axis=0,
        concat_axis=1,
        tiled=True,
    )


def block_codes(lists, counts, classes, candidate_count):
    zero_code = 4
    entries = jnp.arange(lists.shape[1], dtype=jnp.int32)
    value = jnp.where(entries[None, :] < counts[:, None], classes, zero_code)
    hit = lists[:, :, None] == jnp.arange(candidate_count, dtype=jnp.int32)[None, None, :]
    code = zero_code + jnp.sum(jnp.where(hit, value[:, :, None] - zero_code, 0), axis=1)
    return jnp.clip(code, 0, zero_code).astype(jnp.int32)


def taper_table(tile_width, members):
    row_ids = lax.broadcasted_iota(jnp.float32, (tile_width, tile_width), 0)
    col_ids = lax.broadcasted_iota(jnp.float32, (tile_width, tile_width), 1)
    offset = row_ids - col_ids
    length = 8.0 * jnp.exp2(jnp.arange(4, dtype=jnp.float32))
    scaled = offset[None] / length[:, None, None]
    tiles = (1.0 / (1.0 + scaled * scaled)) / (members - 1.0)
    return jnp.concatenate([tiles, jnp.zeros((1, tile_width, tile_width), jnp.float32)], axis=0)


GROUP = 4


def update_call(code, state, partial, anchor, cand_obs, cand_innov, tiles, block_count, candidate_count):
    members, cells = state.shape
    rows = GROUP * BLK
    width = candidate_count * BLK
    final = anchor is not None

    def kernel(code_ref, s_ref, o_ref, i_ref, taper_ref, *rest):
        if final:
            part_ref, f_ref, out_ref, cov_scr, tap_scr = rest
        else:
            out_ref, cov_scr, tap_scr = rest
        g = pl.program_id(0)
        cov_scr[...] = lax.dot_general(
            s_ref[...], o_ref[...], (((0,), (0,)), ((), ())), preferred_element_type=jnp.float32
        )
        for sl in range(GROUP):
            s = g * GROUP + sl
            for b in range(candidate_count):
                c = code_ref[s * candidate_count + b]
                tile = cov_scr[sl * BLK:(sl + 1) * BLK, b * BLK:(b + 1) * BLK] * taper_ref[c]
                tap_scr[sl * BLK:(sl + 1) * BLK, b * BLK:(b + 1) * BLK] = tile.astype(jnp.bfloat16)
        change = lax.dot_general(
            i_ref[...], tap_scr[...], (((1,), (1,)), ((), ())), preferred_element_type=jnp.float32
        )
        if final:
            total = part_ref[...] + change
            out_ref[...] = (f_ref[...].astype(jnp.float32) + total).astype(jnp.bfloat16)
        else:
            out_ref[...] = change

    col_spec = pl.BlockSpec((members, rows), lambda g, code: (0, g))
    in_specs = [
        col_spec,
        pl.BlockSpec((members, width), lambda g, code: (0, 0)),
        pl.BlockSpec((members, width), lambda g, code: (0, 0)),
        pl.BlockSpec(tiles.shape, lambda g, code: (0, 0, 0)),
    ]
    operands = [state, cand_obs, cand_innov, tiles]
    if final:
        in_specs += [col_spec, col_spec]
        operands += [partial, anchor]
    grid_spec = pltpu.PrefetchScalarGridSpec(
        num_scalar_prefetch=1,
        grid=(block_count // GROUP,),
        in_specs=in_specs,
        out_specs=col_spec,
        scratch_shapes=[
            pltpu.VMEM((rows, width), jnp.float32),
            pltpu.VMEM((rows, width), jnp.bfloat16),
        ],
    )
    out_type = jnp.bfloat16 if final else jnp.float32
    return pl.pallas_call(
        kernel,
        grid_spec=grid_spec,
        out_shape=jax.ShapeDtypeStruct((members, cells), out_type),
        cost_estimate=pl.CostEstimate(flops=4 * cells * members * width, transcendentals=0, bytes_accessed=8 * cells * members),
    )(code, *operands)


def solution(mesh):
    in_specs = (
        P("wide", None, "lon"),
        P(None, "wide", "lon"),
        P(None, None, "lon"),
        P(None, None, "lon"),
        P("lon", "wide", None),
        P("lon", "wide"),
        P("lon", "wide", None),
    )
    out_specs = P("wide", None, "lon")
    return jax.shard_map(body, mesh=mesh, in_specs=in_specs, out_specs=out_specs, check_vma=False)
```

```python
import math

import jax
import jax.numpy as jnp
from jax import lax
from jax.sharding import PartitionSpec as P
from jax.experimental import pallas as pl
from jax.experimental.pallas import tpu as pltpu

BLK = 128
HALO_BLK = 4


def padded_2(value, sides, width):
    for axis, dim in sides:
        size, length = (lax.axis_size(axis), value.shape[dim])
        up = [(i, (i + 1) % size) for i in range(size)]
        down = [(j, i) for i, j in up]
        last = lax.slice_in_dim(value, length - width, length, axis=dim)
        first = lax.slice_in_dim(value, 0, width, axis=dim)
        before = lax.ppermute(last, axis, up)
        after = lax.ppermute(first, axis, down)
        value = jnp.concatenate([before, value, after], axis=dim)
    return value


def column_halo(value, axis):
    size = lax.axis_size(axis)
    here = lax.axis_index(axis)
    edges = jnp.concatenate([value[..., :1], value[..., -1:]], axis=-1)
    spread = jnp.broadcast_to(edges[None], (size,) + edges.shape)
    got = lax.all_to_all(spread, axis, 0, 0, tiled=False)
    west = lax.dynamic_index_in_dim(got, (here - 1) % size, 0, keepdims=False)[..., 1:2]
    east = lax.dynamic_index_in_dim(got, (here + 1) % size, 0, keepdims=False)[..., 0:1]
    return west, east


def forecast_call(state, west, east):
    members, rows, cols = state.shape

    def kernel(x_ref, w_ref, e_ref, o_ref):
        col = lax.broadcasted_iota(jnp.int32, (rows, cols), 1)
        row = lax.broadcasted_iota(jnp.int32, (rows, cols), 0)

        def one(m, carry):
            x = x_ref[m].astype(jnp.float32)
            east_n = jnp.where(col == cols - 1, e_ref[m].astype(jnp.float32), pltpu.roll(x, cols - 1, 1))
            west_n = jnp.where(col == 0, w_ref[m].astype(jnp.float32), pltpu.roll(x, 1, 1))
            north = jnp.where(row == rows - 1, 0.0, pltpu.roll(x, rows - 1, 0))
            south = jnp.where(row == 0, 0.0, pltpu.roll(x, 1, 0))
            spread = east_n + west_n + north + south - 4.0 * x
            o_ref[m] = (x + 0.2 * spread - 0.3 * (east_n - west_n)).astype(jnp.bfloat16)
            return carry

        lax.fori_loop(0, members, one, 0, unroll=4)

    return pl.pallas_call(kernel, out_shape=jax.ShapeDtypeStruct(state.shape, jnp.bfloat16))(state, west, east)


def observe_region(state, index, weight):
    members, cells = state.shape
    count = index.shape[1]
    width = math.gcd(512, count)
    nblocks = count // width
    index_blocks = index.reshape(4, nblocks, width).transpose(1, 0, 2)
    weight_blocks = weight.reshape(4, nblocks, width).transpose(1, 0, 2)
    cell_ids = lax.broadcasted_iota(jnp.int32, (cells, width), 0)

    def observe_one_block(pieces):
        index_here, weight_here = pieces
        summed = jnp.zeros((members, width), jnp.float32)
        for k in range(4):
            selector = (cell_ids == index_here[k][None, :]).astype(jnp.bfloat16)
            picked = jnp.dot(state, selector, preferred_element_type=jnp.float32)
            summed = summed + weight_here[k][None, :] * picked
        return summed.astype(jnp.bfloat16)

    result = lax.map(observe_one_block, (index_blocks, weight_blocks))
    return result.transpose(1, 0, 2).reshape(members, count)


OBS_STEP = 256
def observe_dev_call(state, index, weight):
    members, cells = state.shape
    count = index.shape[1]
    def kernel(f_ref, i_ref, w_ref, o_ref):
        cell_ids = lax.broadcasted_iota(jnp.int32, (cells, OBS_STEP), 0)
        f = f_ref[...]
        summed = jnp.zeros((members, OBS_STEP), jnp.float32)
        for k in range(4):
            selector = (cell_ids == i_ref[k:k + 1, :]).astype(jnp.bfloat16)
            picked = jnp.dot(f, selector, preferred_element_type=jnp.float32)
            summed = summed + w_ref[k:k + 1, :] * picked
        ens = summed.astype(jnp.bfloat16).astype(jnp.float32)
        mean = jnp.sum(ens, axis=0, keepdims=True) / members
        o_ref[...] = (ens - mean).astype(jnp.bfloat16)
    return pl.pallas_call(
        kernel,
        grid=(count // OBS_STEP,),
        in_specs=[
            pl.BlockSpec((members, cells), lambda j: (0, 0)),
            pl.BlockSpec((4, OBS_STEP), lambda j: (0, j)),
            pl.BlockSpec((4, OBS_STEP), lambda j: (0, j)),
        ],
        out_specs=pl.BlockSpec((members, OBS_STEP), lambda j: (0, j)),
        out_shape=jax.ShapeDtypeStruct((members, count), jnp.bfloat16),
    )(state, index, weight)
def anomaly_from_mean(state_values):
    centred = state_values.astype(jnp.float32)
    return (centred - jnp.mean(centred, axis=-2, keepdims=True)).astype(jnp.bfloat16)


def taper_tiles(classes, in_use, tile_width):
    row_ids = lax.broadcasted_iota(jnp.float32, (tile_width, tile_width), 0)
    col_ids = lax.broadcasted_iota(jnp.float32, (tile_width, tile_width), 1)
    offset = row_ids - col_ids
    length = 8.0 * jnp.exp2(classes.astype(jnp.float32))
    scaled = offset / length[..., None, None]
    return in_use[..., None, None] / (1.0 + scaled * scaled)


def body(background_ensemble, innov, obs_index, obs_weight, obs_list, tile_count, taper_class):
    west_col, east_col = column_halo(background_ensemble, "lon")
    prediction_increment = forecast_call(background_ensemble, west_col, east_col)
    ensemble_lines_here, whole_parallel_set, patch_meridian_lines = prediction_increment.shape
    members = innov.shape[0]
    band_rows = innov.shape[1]
    patch_gridpoints = band_rows * patch_meridian_lines
    region = lax.all_to_all(prediction_increment, "wide", split_axis=1, concat_axis=0, tiled=True)
    region_state = region.reshape(members, patch_gridpoints)
    first_row = lax.axis_index("wide") * band_rows
    local_index = lax.dynamic_slice_in_dim(obs_index, first_row, band_rows, 1).reshape(
        4, patch_gridpoints
    )
    local_index = local_index - first_row * patch_meridian_lines
    local_weight = lax.dynamic_slice_in_dim(obs_weight, first_row, band_rows, 1).reshape(
        4, patch_gridpoints
    )
    halo = HALO_BLK * BLK
    innov_flat = innov.reshape(members, patch_gridpoints)
    edge_index = jnp.concatenate([local_index[:, :halo], local_index[:, -halo:]], axis=1)
    edge_weight = jnp.concatenate([local_weight[:, :halo], local_weight[:, -halo:]], axis=1)
    edge_dev = observe_dev_call(region_state, edge_index, edge_weight)
    edge_innov = jnp.concatenate([innov_flat[:, :halo], innov_flat[:, -halo:]], axis=1)
    edges = jnp.stack([edge_dev, edge_innov])
    lon_size = lax.axis_size("lon")
    up = [(i, (i + 1) % lon_size) for i in range(lon_size)]
    down = [(j, i) for i, j in up]
    west = lax.ppermute(edges[:, :, halo:], "lon", up)
    east = lax.ppermute(edges[:, :, :halo], "lon", down)
    middle_dev = observe_dev_call(region_state, local_index[:, halo:-halo], local_weight[:, halo:-halo])
    obs_dev = jnp.concatenate([edge_dev[:, :halo], middle_dev, edge_dev[:, halo:]], axis=1)
    model_anomaly = anomaly_from_mean(region_state)
    halo_blocks = halo // BLK
    block_count = patch_gridpoints // BLK
    candidate_count = block_count + 2 * halo_blocks
    code = block_codes(obs_list[0], tile_count[0], taper_class[0], candidate_count)
    own_code = code[:, halo_blocks:halo_blocks + block_count]
    halo_code = jnp.concatenate([code[:, :halo_blocks], code[:, halo_blocks + block_count:]], axis=1)
    tiles = taper_table(BLK, members)
    partial = update_call(
        own_code.reshape(-1), model_anomaly, None, None, obs_dev, innov_flat, tiles, block_count, block_count
    )
    halo_obs = jnp.concatenate([west[0], east[0]], axis=1)
    halo_innov = jnp.concatenate([west[1], east[1]], axis=1)
    result = update_call(
        halo_code.reshape(-1),
        model_anomaly,
        partial,
        region_state,
        halo_obs,
        halo_innov,
        tiles,
        block_count,
        2 * halo_blocks,
        group=8,
    )
    return lax.all_to_all(
        result.reshape(members, band_rows, patch_meridian_lines),
        "wide",
        split_axis=0,
        concat_axis=1,
        tiled=True,
    )


def block_codes(lists, counts, classes, candidate_count):
    zero_code = 4
    entries = jnp.arange(lists.shape[1], dtype=jnp.int32)
    value = jnp.where(entries[None, :] < counts[:, None], classes, zero_code)
    hit = lists[:, :, None] == jnp.arange(candidate_count, dtype=jnp.int32)[None, None, :]
    code = zero_code + jnp.sum(jnp.where(hit, value[:, :, None] - zero_code, 0), axis=1)
    return jnp.clip(code, 0, zero_code).astype(jnp.int32)


def taper_table(tile_width, members):
    row_ids = lax.broadcasted_iota(jnp.float32, (tile_width, tile_width), 0)
    col_ids = lax.broadcasted_iota(jnp.float32, (tile_width, tile_width), 1)
    offset = row_ids - col_ids
    length = 8.0 * jnp.exp2(jnp.arange(4, dtype=jnp.float32))
    scaled = offset[None] / length[:, None, None]
    tiles = (1.0 / (1.0 + scaled * scaled)) / (members - 1.0)
    return jnp.concatenate([tiles, jnp.zeros((1, tile_width, tile_width), jnp.float32)], axis=0)


GROUP = 4


def update_call(code, state, partial, anchor, cand_obs, cand_innov, tiles, block_count, candidate_count, group=GROUP):
    members, cells = state.shape
    rows = group * BLK
    width = candidate_count * BLK
    final = anchor is not None

    def kernel(code_ref, s_ref, o_ref, i_ref, taper_ref, *rest):
        if final:
            part_ref, f_ref, out_ref, cov_scr, tap_scr = rest
        else:
            out_ref, cov_scr, tap_scr = rest
        g = pl.program_id(0)
        cov_scr[...] = lax.dot_general(
            s_ref[...], o_ref[...], (((0,), (0,)), ((), ())), preferred_element_type=jnp.float32
        )
        for sl in range(group):
            s = g * group + sl
            for b in range(candidate_count):
                c = code_ref[s * candidate_count + b]
                tile = cov_scr[sl * BLK:(sl + 1) * BLK, b * BLK:(b + 1) * BLK] * taper_ref[c]
                tap_scr[sl * BLK:(sl + 1) * BLK, b * BLK:(b + 1) * BLK] = tile.astype(jnp.bfloat16)
        change = lax.dot_general(
            i_ref[...], tap_scr[...], (((1,), (1,)), ((), ())), preferred_element_type=jnp.float32
        )
        if final:
            total = part_ref[...] + change
            out_ref[...] = (f_ref[...].astype(jnp.float32) + total).astype(jnp.bfloat16)
        else:
            out_ref[...] = change

    col_spec = pl.BlockSpec((members, rows), lambda g, code: (0, g))
    in_specs = [
        col_spec,
        pl.BlockSpec((members, width), lambda g, code: (0, 0)),
        pl.BlockSpec((members, width), lambda g, code: (0, 0)),
        pl.BlockSpec(tiles.shape, lambda g, code: (0, 0, 0)),
    ]
    operands = [state, cand_obs, cand_innov, tiles]
    if final:
        in_specs += [col_spec, col_spec]
        operands += [partial, anchor]
    grid_spec = pltpu.PrefetchScalarGridSpec(
        num_scalar_prefetch=1,
        grid=(block_count // group,),
        in_specs=in_specs,
        out_specs=col_spec,
        scratch_shapes=[
            pltpu.VMEM((rows, width), jnp.float32),
            pltpu.VMEM((rows, width), jnp.bfloat16),
        ],
    )
    out_type = jnp.bfloat16 if final else jnp.float32
    return pl.pallas_call(
        kernel,
        grid_spec=grid_spec,
        out_shape=jax.ShapeDtypeStruct((members, cells), out_type),
        cost_estimate=pl.CostEstimate(flops=4 * cells * members * width, transcendentals=0, bytes_accessed=8 * cells * members),
    )(code, *operands)


def solution(mesh):
    in_specs = (
        P("wide", None, "lon"),
        P(None, "wide", "lon"),
        P(None, None, "lon"),
        P(None, None, "lon"),
        P("lon", "wide", None),
        P("lon", "wide"),
        P("lon", "wide", None),
    )
    out_specs = P("wide", None, "lon")
    return jax.shard_map(body, mesh=mesh, in_specs=in_specs, out_specs=out_specs, check_vma=False)
```

```python
import math

import jax
import jax.numpy as jnp
from jax import lax
from jax.sharding import PartitionSpec as P
from jax.experimental import pallas as pl
from jax.experimental.pallas import tpu as pltpu

BLK = 128
HALO_BLK = 4


def padded_2(value, sides, width):
    for axis, dim in sides:
        size, length = (lax.axis_size(axis), value.shape[dim])
        up = [(i, (i + 1) % size) for i in range(size)]
        down = [(j, i) for i, j in up]
        last = lax.slice_in_dim(value, length - width, length, axis=dim)
        first = lax.slice_in_dim(value, 0, width, axis=dim)
        before = lax.ppermute(last, axis, up)
        after = lax.ppermute(first, axis, down)
        value = jnp.concatenate([before, value, after], axis=dim)
    return value


def column_halo(value, axis):
    size = lax.axis_size(axis)
    here = lax.axis_index(axis)
    edges = jnp.concatenate([value[..., :1], value[..., -1:]], axis=-1)
    spread = jnp.broadcast_to(edges[None], (size,) + edges.shape)
    got = lax.all_to_all(spread, axis, 0, 0, tiled=False)
    west = lax.dynamic_index_in_dim(got, (here - 1) % size, 0, keepdims=False)[..., 1:2]
    east = lax.dynamic_index_in_dim(got, (here + 1) % size, 0, keepdims=False)[..., 0:1]
    return west, east


def stencil(state, east, west, northern, southern):
    member_spread = east + west + northern + southern - 4.0 * state
    return (state + 0.2 * member_spread - 0.3 * (east - west)).astype(jnp.bfloat16)


def rows_beside(column):
    northern = jnp.pad(column[:, 1:, :], ((0, 0), (0, 1), (0, 0)))
    southern = jnp.pad(column[:, :-1, :], ((0, 0), (1, 0), (0, 0)))
    return northern, southern


def forecast_call(state):
    members, rows, cols = state.shape

    def kernel(x_ref, o_ref):
        row = lax.broadcasted_iota(jnp.int32, (rows, cols), 0)

        def one(m, carry):
            x = x_ref[m].astype(jnp.float32)
            east_n = pltpu.roll(x, cols - 1, 1)
            west_n = pltpu.roll(x, 1, 1)
            north = jnp.where(row == rows - 1, 0.0, pltpu.roll(x, rows - 1, 0))
            south = jnp.where(row == 0, 0.0, pltpu.roll(x, 1, 0))
            spread = east_n + west_n + north + south - 4.0 * x
            o_ref[m] = (x + 0.2 * spread - 0.3 * (east_n - west_n)).astype(jnp.bfloat16)
            return carry

        lax.fori_loop(0, members, one, 0, unroll=4)

    return pl.pallas_call(kernel, out_shape=jax.ShapeDtypeStruct(state.shape, jnp.bfloat16))(state)


def observe_region(state, index, weight):
    members, cells = state.shape
    count = index.shape[1]
    width = math.gcd(512, count)
    nblocks = count // width
    index_blocks = index.reshape(4, nblocks, width).transpose(1, 0, 2)
    weight_blocks = weight.reshape(4, nblocks, width).transpose(1, 0, 2)
    cell_ids = lax.broadcasted_iota(jnp.int32, (cells, width), 0)

    def observe_one_block(pieces):
        index_here, weight_here = pieces
        summed = jnp.zeros((members, width), jnp.float32)
        for k in range(4):
            selector = (cell_ids == index_here[k][None, :]).astype(jnp.bfloat16)
            picked = jnp.dot(state, selector, preferred_element_type=jnp.float32)
            summed = summed + weight_here[k][None, :] * picked
        return summed.astype(jnp.bfloat16)

    result = lax.map(observe_one_block, (index_blocks, weight_blocks))
    return result.transpose(1, 0, 2).reshape(members, count)


OBS_STEP = 256
def observe_dev_call(state, index, weight):
    members, cells = state.shape
    count = index.shape[1]
    def kernel(f_ref, i_ref, w_ref, o_ref):
        cell_ids = lax.broadcasted_iota(jnp.int32, (cells, OBS_STEP), 0)
        f = f_ref[...]
        summed = jnp.zeros((members, OBS_STEP), jnp.float32)
        for k in range(4):
            selector = (cell_ids == i_ref[k:k + 1, :]).astype(jnp.bfloat16)
            picked = jnp.dot(f, selector, preferred_element_type=jnp.float32)
            summed = summed + w_ref[k:k + 1, :] * picked
        ens = summed.astype(jnp.bfloat16).astype(jnp.float32)
        mean = jnp.sum(ens, axis=0, keepdims=True) / members
        o_ref[...] = (ens - mean).astype(jnp.bfloat16)
    return pl.pallas_call(
        kernel,
        grid=(count // OBS_STEP,),
        in_specs=[
            pl.BlockSpec((members, cells), lambda j: (0, 0)),
            pl.BlockSpec((4, OBS_STEP), lambda j: (0, j)),
            pl.BlockSpec((4, OBS_STEP), lambda j: (0, j)),
        ],
        out_specs=pl.BlockSpec((members, OBS_STEP), lambda j: (0, j)),
        out_shape=jax.ShapeDtypeStruct((members, count), jnp.bfloat16),
    )(state, index, weight)
def anomaly_from_mean(state_values):
    centred = state_values.astype(jnp.float32)
    return (centred - jnp.mean(centred, axis=-2, keepdims=True)).astype(jnp.bfloat16)


def taper_tiles(classes, in_use, tile_width):
    row_ids = lax.broadcasted_iota(jnp.float32, (tile_width, tile_width), 0)
    col_ids = lax.broadcasted_iota(jnp.float32, (tile_width, tile_width), 1)
    offset = row_ids - col_ids
    length = 8.0 * jnp.exp2(classes.astype(jnp.float32))
    scaled = offset / length[..., None, None]
    return in_use[..., None, None] / (1.0 + scaled * scaled)


def body(background_ensemble, innov, obs_index, obs_weight, obs_list, tile_count, taper_class):
    inner = forecast_call(background_ensemble)
    west_col, east_col = column_halo(background_ensemble, "lon")
    near = background_ensemble[..., :2].astype(jnp.float32)
    far = background_ensemble[..., -2:].astype(jnp.float32)
    first = stencil(near[..., :1], near[..., 1:2], west_col.astype(jnp.float32), *rows_beside(near[..., :1]))
    last = stencil(far[..., 1:], east_col.astype(jnp.float32), far[..., :1], *rows_beside(far[..., 1:]))
    prediction_increment = jnp.concatenate([first, inner[..., 1:-1], last], axis=-1)
    ensemble_lines_here, whole_parallel_set, patch_meridian_lines = prediction_increment.shape
    members = innov.shape[0]
    band_rows = innov.shape[1]
    patch_gridpoints = band_rows * patch_meridian_lines
    region = lax.all_to_all(prediction_increment, "wide", split_axis=1, concat_axis=0, tiled=True)
    region_state = region.reshape(members, patch_gridpoints)
    first_row = lax.axis_index("wide") * band_rows
    local_index = lax.dynamic_slice_in_dim(obs_index, first_row, band_rows, 1).reshape(
        4, patch_gridpoints
    )
    local_index = local_index - first_row * patch_meridian_lines
    local_weight = lax.dynamic_slice_in_dim(obs_weight, first_row, band_rows, 1).reshape(
        4, patch_gridpoints
    )
    halo = HALO_BLK * BLK
    innov_flat = innov.reshape(members, patch_gridpoints)
    edge_index = jnp.concatenate([local_index[:, :halo], local_index[:, -halo:]], axis=1)
    edge_weight = jnp.concatenate([local_weight[:, :halo], local_weight[:, -halo:]], axis=1)
    edge_dev = observe_dev_call(region_state, edge_index, edge_weight)
    edge_innov = jnp.concatenate([innov_flat[:, :halo], innov_flat[:, -halo:]], axis=1)
    edges = jnp.stack([edge_dev, edge_innov])
    lon_size = lax.axis_size("lon")
    up = [(i, (i + 1) % lon_size) for i in range(lon_size)]
    down = [(j, i) for i, j in up]
    west = lax.ppermute(edges[:, :, halo:], "lon", up)
    east = lax.ppermute(edges[:, :, :halo], "lon", down)
    middle_dev = observe_dev_call(region_state, local_index[:, halo:-halo], local_weight[:, halo:-halo])
    obs_dev = jnp.concatenate([edge_dev[:, :halo], middle_dev, edge_dev[:, halo:]], axis=1)
    model_anomaly = anomaly_from_mean(region_state)
    halo_blocks = halo // BLK
    block_count = patch_gridpoints // BLK
    candidate_count = block_count + 2 * halo_blocks
    code = block_codes(obs_list[0], tile_count[0], taper_class[0], candidate_count)
    own_code = code[:, halo_blocks:halo_blocks + block_count]
    halo_code = jnp.concatenate([code[:, :halo_blocks], code[:, halo_blocks + block_count:]], axis=1)
    tiles = taper_table(BLK, members)
    partial = update_call(
        own_code.reshape(-1), model_anomaly, None, None, obs_dev, innov_flat, tiles, block_count, block_count
    )
    halo_obs = jnp.concatenate([west[0], east[0]], axis=1)
    halo_innov = jnp.concatenate([west[1], east[1]], axis=1)
    result = update_call(
        halo_code.reshape(-1),
        model_anomaly,
        partial,
        region_state,
        halo_obs,
        halo_innov,
        tiles,
        block_count,
        2 * halo_blocks,
        group=8,
    )
    return lax.all_to_all(
        result.reshape(members, band_rows, patch_meridian_lines),
        "wide",
        split_axis=0,
        concat_axis=1,
        tiled=True,
    )


def block_codes(lists, counts, classes, candidate_count):
    zero_code = 4
    entries = jnp.arange(lists.shape[1], dtype=jnp.int32)
    value = jnp.where(entries[None, :] < counts[:, None], classes, zero_code)
    hit = lists[:, :, None] == jnp.arange(candidate_count, dtype=jnp.int32)[None, None, :]
    code = zero_code + jnp.sum(jnp.where(hit, value[:, :, None] - zero_code, 0), axis=1)
    return jnp.clip(code, 0, zero_code).astype(jnp.int32)


def taper_table(tile_width, members):
    row_ids = lax.broadcasted_iota(jnp.float32, (tile_width, tile_width), 0)
    col_ids = lax.broadcasted_iota(jnp.float32, (tile_width, tile_width), 1)
    offset = row_ids - col_ids
    length = 8.0 * jnp.exp2(jnp.arange(4, dtype=jnp.float32))
    scaled = offset[None] / length[:, None, None]
    tiles = (1.0 / (1.0 + scaled * scaled)) / (members - 1.0)
    return jnp.concatenate([tiles, jnp.zeros((1, tile_width, tile_width), jnp.float32)], axis=0)


GROUP = 4


def update_call(code, state, partial, anchor, cand_obs, cand_innov, tiles, block_count, candidate_count, group=GROUP):
    members, cells = state.shape
    rows = group * BLK
    width = candidate_count * BLK
    final = anchor is not None

    def kernel(code_ref, s_ref, o_ref, i_ref, taper_ref, *rest):
        if final:
            part_ref, f_ref, out_ref, cov_scr, tap_scr = rest
        else:
            out_ref, cov_scr, tap_scr = rest
        g = pl.program_id(0)
        cov_scr[...] = lax.dot_general(
            s_ref[...], o_ref[...], (((0,), (0,)), ((), ())), preferred_element_type=jnp.float32
        )
        for sl in range(group):
            s = g * group + sl
            for b in range(candidate_count):
                c = code_ref[s * candidate_count + b]
                tile = cov_scr[sl * BLK:(sl + 1) * BLK, b * BLK:(b + 1) * BLK] * taper_ref[c]
                tap_scr[sl * BLK:(sl + 1) * BLK, b * BLK:(b + 1) * BLK] = tile.astype(jnp.bfloat16)
        change = lax.dot_general(
            i_ref[...], tap_scr[...], (((1,), (1,)), ((), ())), preferred_element_type=jnp.float32
        )
        if final:
            total = part_ref[...] + change
            out_ref[...] = (f_ref[...].astype(jnp.float32) + total).astype(jnp.bfloat16)
        else:
            out_ref[...] = change

    col_spec = pl.BlockSpec((members, rows), lambda g, code: (0, g))
    in_specs = [
        col_spec,
        pl.BlockSpec((members, width), lambda g, code: (0, 0)),
        pl.BlockSpec((members, width), lambda g, code: (0, 0)),
        pl.BlockSpec(tiles.shape, lambda g, code: (0, 0, 0)),
    ]
    operands = [state, cand_obs, cand_innov, tiles]
    if final:
        in_specs += [col_spec, col_spec]
        operands += [partial, anchor]
    grid_spec = pltpu.PrefetchScalarGridSpec(
        num_scalar_prefetch=1,
        grid=(block_count // group,),
        in_specs=in_specs,
        out_specs=col_spec,
        scratch_shapes=[
            pltpu.VMEM((rows, width), jnp.float32),
            pltpu.VMEM((rows, width), jnp.bfloat16),
        ],
    )
    out_type = jnp.bfloat16 if final else jnp.float32
    return pl.pallas_call(
        kernel,
        grid_spec=grid_spec,
        out_shape=jax.ShapeDtypeStruct((members, cells), out_type),
        cost_estimate=pl.CostEstimate(flops=4 * cells * members * width, transcendentals=0, bytes_accessed=8 * cells * members),
    )(code, *operands)


def solution(mesh):
    in_specs = (
        P("wide", None, "lon"),
        P(None, "wide", "lon"),
        P(None, None, "lon"),
        P(None, None, "lon"),
        P("lon", "wide", None),
        P("lon", "wide"),
        P("lon", "wide", None),
    )
    out_specs = P("wide", None, "lon")
    return jax.shard_map(body, mesh=mesh, in_specs=in_specs, out_specs=out_specs, check_vma=False)
```

```python
import math

import jax
import jax.numpy as jnp
from jax import lax
from jax.sharding import PartitionSpec as P
from jax.experimental import pallas as pl
from jax.experimental.pallas import tpu as pltpu

BLK = 128
HALO_BLK = 4


def padded_2(value, sides, width):
    for axis, dim in sides:
        size, length = (lax.axis_size(axis), value.shape[dim])
        up = [(i, (i + 1) % size) for i in range(size)]
        down = [(j, i) for i, j in up]
        last = lax.slice_in_dim(value, length - width, length, axis=dim)
        first = lax.slice_in_dim(value, 0, width, axis=dim)
        before = lax.ppermute(last, axis, up)
        after = lax.ppermute(first, axis, down)
        value = jnp.concatenate([before, value, after], axis=dim)
    return value


def column_halo(value, axis):
    size = lax.axis_size(axis)
    here = lax.axis_index(axis)
    edges = jnp.concatenate([value[..., :1], value[..., -1:]], axis=-1)
    spread = jnp.broadcast_to(edges[None], (size,) + edges.shape)
    got = lax.all_to_all(spread, axis, 0, 0, tiled=False)
    west = lax.dynamic_index_in_dim(got, (here - 1) % size, 0, keepdims=False)[..., 1:2]
    east = lax.dynamic_index_in_dim(got, (here + 1) % size, 0, keepdims=False)[..., 0:1]
    return west, east


def forecast_call(state, west, east):
    members, rows, cols = state.shape

    def kernel(x_ref, w_ref, e_ref, o_ref):
        col = lax.broadcasted_iota(jnp.int32, (rows, cols), 1)
        row = lax.broadcasted_iota(jnp.int32, (rows, cols), 0)

        def one(m, carry):
            x = x_ref[m].astype(jnp.float32)
            east_n = jnp.where(col == cols - 1, e_ref[m].astype(jnp.float32), pltpu.roll(x, cols - 1, 1))
            west_n = jnp.where(col == 0, w_ref[m].astype(jnp.float32), pltpu.roll(x, 1, 1))
            north = jnp.where(row == rows - 1, 0.0, pltpu.roll(x, rows - 1, 0))
            south = jnp.where(row == 0, 0.0, pltpu.roll(x, 1, 0))
            spread = east_n + west_n + north + south - 4.0 * x
            o_ref[m] = (x + 0.2 * spread - 0.3 * (east_n - west_n)).astype(jnp.bfloat16)
            return carry

        lax.fori_loop(0, members, one, 0, unroll=4)

    return pl.pallas_call(kernel, out_shape=jax.ShapeDtypeStruct(state.shape, jnp.bfloat16))(state, west, east)


def observe_region(state, index, weight):
    members, cells = state.shape
    count = index.shape[1]
    width = math.gcd(512, count)
    nblocks = count // width
    index_blocks = index.reshape(4, nblocks, width).transpose(1, 0, 2)
    weight_blocks = weight.reshape(4, nblocks, width).transpose(1, 0, 2)
    cell_ids = lax.broadcasted_iota(jnp.int32, (cells, width), 0)

    def observe_one_block(pieces):
        index_here, weight_here = pieces
        summed = jnp.zeros((members, width), jnp.float32)
        for k in range(4):
            selector = (cell_ids == index_here[k][None, :]).astype(jnp.bfloat16)
            picked = jnp.dot(state, selector, preferred_element_type=jnp.float32)
            summed = summed + weight_here[k][None, :] * picked
        return summed.astype(jnp.bfloat16)

    result = lax.map(observe_one_block, (index_blocks, weight_blocks))
    return result.transpose(1, 0, 2).reshape(members, count)


OBS_STEP = 256
def observe_dev_call(state, index, weight, extra=None):
    members, cells = state.shape
    count = index.shape[1]
    carry = extra is not None

    def kernel(f_ref, i_ref, w_ref, *rest):
        if carry:
            x_ref, o_ref = rest
        else:
            (o_ref,) = rest
        cell_ids = lax.broadcasted_iota(jnp.int32, (cells, OBS_STEP), 0)
        f = f_ref[...]
        summed = jnp.zeros((members, OBS_STEP), jnp.float32)
        for k in range(4):
            selector = (cell_ids == i_ref[k:k + 1, :]).astype(jnp.bfloat16)
            picked = jnp.dot(f, selector, preferred_element_type=jnp.float32)
            summed = summed + w_ref[k:k + 1, :] * picked
        ens = summed.astype(jnp.bfloat16).astype(jnp.float32)
        mean = jnp.sum(ens, axis=0, keepdims=True) / members
        dev = (ens - mean).astype(jnp.bfloat16)
        if carry:
            o_ref[0] = dev
            o_ref[1] = x_ref[...]
        else:
            o_ref[...] = dev

    in_specs = [
        pl.BlockSpec((members, cells), lambda j: (0, 0)),
        pl.BlockSpec((4, OBS_STEP), lambda j: (0, j)),
        pl.BlockSpec((4, OBS_STEP), lambda j: (0, j)),
    ]
    operands = [state, index, weight]
    if carry:
        in_specs.append(pl.BlockSpec((members, OBS_STEP), lambda j: (0, j)))
        operands.append(extra)
        out_spec = pl.BlockSpec((2, members, OBS_STEP), lambda j: (0, 0, j))
        out_shape = jax.ShapeDtypeStruct((2, members, count), jnp.bfloat16)
    else:
        out_spec = pl.BlockSpec((members, OBS_STEP), lambda j: (0, j))
        out_shape = jax.ShapeDtypeStruct((members, count), jnp.bfloat16)
    return pl.pallas_call(
        kernel,
        grid=(count // OBS_STEP,),
        in_specs=in_specs,
        out_specs=out_spec,
        out_shape=out_shape,
    )(*operands)


def anomaly_from_mean(state_values):
    centred = state_values.astype(jnp.float32)
    return (centred - jnp.mean(centred, axis=-2, keepdims=True)).astype(jnp.bfloat16)


def taper_tiles(classes, in_use, tile_width):
    row_ids = lax.broadcasted_iota(jnp.float32, (tile_width, tile_width), 0)
    col_ids = lax.broadcasted_iota(jnp.float32, (tile_width, tile_width), 1)
    offset = row_ids - col_ids
    length = 8.0 * jnp.exp2(classes.astype(jnp.float32))
    scaled = offset / length[..., None, None]
    return in_use[..., None, None] / (1.0 + scaled * scaled)


def body(background_ensemble, innov, obs_index, obs_weight, obs_list, tile_count, taper_class):
    west_col, east_col = column_halo(background_ensemble, "lon")
    prediction_increment = forecast_call(background_ensemble, west_col, east_col)
    ensemble_lines_here, whole_parallel_set, patch_meridian_lines = prediction_increment.shape
    members = innov.shape[0]
    band_rows = innov.shape[1]
    patch_gridpoints = band_rows * patch_meridian_lines
    region = lax.all_to_all(prediction_increment, "wide", split_axis=1, concat_axis=0, tiled=True)
    region_state = region.reshape(members, patch_gridpoints)
    first_row = lax.axis_index("wide") * band_rows
    local_index = lax.dynamic_slice_in_dim(obs_index, first_row, band_rows, 1).reshape(
        4, patch_gridpoints
    )
    local_index = local_index - first_row * patch_meridian_lines
    local_weight = lax.dynamic_slice_in_dim(obs_weight, first_row, band_rows, 1).reshape(
        4, patch_gridpoints
    )
    halo = HALO_BLK * BLK
    innov_flat = innov.reshape(members, patch_gridpoints)
    lon_size = lax.axis_size("lon")
    up = [(i, (i + 1) % lon_size) for i in range(lon_size)]
    down = [(j, i) for i, j in up]
    last_edge = observe_dev_call(
        region_state, local_index[:, -halo:], local_weight[:, -halo:], innov_flat[:, -halo:]
    )
    west = lax.ppermute(last_edge, "lon", up)
    first_edge = observe_dev_call(
        region_state, local_index[:, :halo], local_weight[:, :halo], innov_flat[:, :halo]
    )
    east = lax.ppermute(first_edge, "lon", down)
    middle_dev = observe_dev_call(region_state, local_index[:, halo:-halo], local_weight[:, halo:-halo])
    obs_dev = jnp.concatenate([first_edge[0], middle_dev, last_edge[0]], axis=1)
    model_anomaly = anomaly_from_mean(region_state)
    halo_blocks = halo // BLK
    block_count = patch_gridpoints // BLK
    candidate_count = block_count + 2 * halo_blocks
    code = block_codes(obs_list[0], tile_count[0], taper_class[0], candidate_count)
    own_code = code[:, halo_blocks:halo_blocks + block_count]
    halo_code = jnp.concatenate([code[:, :halo_blocks], code[:, halo_blocks + block_count:]], axis=1)
    tiles = taper_table(BLK, members)
    partial = update_call(
        own_code.reshape(-1), model_anomaly, None, None, obs_dev, innov_flat, tiles, block_count, block_count
    )
    halo_obs = jnp.concatenate([west[0], east[0]], axis=1)
    halo_innov = jnp.concatenate([west[1], east[1]], axis=1)
    result = update_call(
        halo_code.reshape(-1),
        model_anomaly,
        partial,
        region_state,
        halo_obs,
        halo_innov,
        tiles,
        block_count,
        2 * halo_blocks,
        group=8,
    )
    return lax.all_to_all(
        result.reshape(members, band_rows, patch_meridian_lines),
        "wide",
        split_axis=0,
        concat_axis=1,
        tiled=True,
    )


def block_codes(lists, counts, classes, candidate_count):
    zero_code = 4
    entries = jnp.arange(lists.shape[1], dtype=jnp.int32)
    value = jnp.where(entries[None, :] < counts[:, None], classes, zero_code)
    hit = lists[:, :, None] == jnp.arange(candidate_count, dtype=jnp.int32)[None, None, :]
    code = zero_code + jnp.sum(jnp.where(hit, value[:, :, None] - zero_code, 0), axis=1)
    return jnp.clip(code, 0, zero_code).astype(jnp.int32)


def taper_table(tile_width, members):
    row_ids = lax.broadcasted_iota(jnp.float32, (tile_width, tile_width), 0)
    col_ids = lax.broadcasted_iota(jnp.float32, (tile_width, tile_width), 1)
    offset = row_ids - col_ids
    length = 8.0 * jnp.exp2(jnp.arange(4, dtype=jnp.float32))
    scaled = offset[None] / length[:, None, None]
    tiles = (1.0 / (1.0 + scaled * scaled)) / (members - 1.0)
    return jnp.concatenate([tiles, jnp.zeros((1, tile_width, tile_width), jnp.float32)], axis=0)


GROUP = 4


def update_call(code, state, partial, anchor, cand_obs, cand_innov, tiles, block_count, candidate_count, group=GROUP):
    members, cells = state.shape
    rows = group * BLK
    width = candidate_count * BLK
    final = anchor is not None

    def kernel(code_ref, s_ref, o_ref, i_ref, taper_ref, *rest):
        if final:
            part_ref, f_ref, out_ref, cov_scr, tap_scr = rest
        else:
            out_ref, cov_scr, tap_scr = rest
        g = pl.program_id(0)
        cov_scr[...] = lax.dot_general(
            s_ref[...], o_ref[...], (((0,), (0,)), ((), ())), preferred_element_type=jnp.float32
        )
        for sl in range(group):
            s = g * group + sl
            for b in range(candidate_count):
                c = code_ref[s * candidate_count + b]
                tile = cov_scr[sl * BLK:(sl + 1) * BLK, b * BLK:(b + 1) * BLK] * taper_ref[c]
                tap_scr[sl * BLK:(sl + 1) * BLK, b * BLK:(b + 1) * BLK] = tile.astype(jnp.bfloat16)
        change = lax.dot_general(
            i_ref[...], tap_scr[...], (((1,), (1,)), ((), ())), preferred_element_type=jnp.float32
        )
        if final:
            total = part_ref[...] + change
            out_ref[...] = (f_ref[...].astype(jnp.float32) + total).astype(jnp.bfloat16)
        else:
            out_ref[...] = change

    col_spec = pl.BlockSpec((members, rows), lambda g, code: (0, g))
    in_specs = [
        col_spec,
        pl.BlockSpec((members, width), lambda g, code: (0, 0)),
        pl.BlockSpec((members, width), lambda g, code: (0, 0)),
        pl.BlockSpec(tiles.shape, lambda g, code: (0, 0, 0)),
    ]
    operands = [state, cand_obs, cand_innov, tiles]
    if final:
        in_specs += [col_spec, col_spec]
        operands += [partial, anchor]
    grid_spec = pltpu.PrefetchScalarGridSpec(
        num_scalar_prefetch=1,
        grid=(block_count // group,),
        in_specs=in_specs,
        out_specs=col_spec,
        scratch_shapes=[
            pltpu.VMEM((rows, width), jnp.float32),
            pltpu.VMEM((rows, width), jnp.bfloat16),
        ],
    )
    out_type = jnp.bfloat16 if final else jnp.float32
    return pl.pallas_call(
        kernel,
        grid_spec=grid_spec,
        out_shape=jax.ShapeDtypeStruct((members, cells), out_type),
        cost_estimate=pl.CostEstimate(flops=4 * cells * members * width, transcendentals=0, bytes_accessed=8 * cells * members),
    )(code, *operands)


def solution(mesh):
    in_specs = (
        P("wide", None, "lon"),
        P(None, "wide", "lon"),
        P(None, None, "lon"),
        P(None, None, "lon"),
        P("lon", "wide", None),
        P("lon", "wide"),
        P("lon", "wide", None),
    )
    out_specs = P("wide", None, "lon")
    return jax.shard_map(body, mesh=mesh, in_specs=in_specs, out_specs=out_specs, check_vma=False)
```

```python
import math

import jax
import jax.numpy as jnp
from jax import lax
from jax.sharding import PartitionSpec as P
from jax.experimental import pallas as pl
from jax.experimental.pallas import tpu as pltpu

BLK = 128
HALO_BLK = 4


def padded_2(value, sides, width):
    for axis, dim in sides:
        size, length = (lax.axis_size(axis), value.shape[dim])
        up = [(i, (i + 1) % size) for i in range(size)]
        down = [(j, i) for i, j in up]
        last = lax.slice_in_dim(value, length - width, length, axis=dim)
        first = lax.slice_in_dim(value, 0, width, axis=dim)
        before = lax.ppermute(last, axis, up)
        after = lax.ppermute(first, axis, down)
        value = jnp.concatenate([before, value, after], axis=dim)
    return value


def column_halo(value, axis):
    size = lax.axis_size(axis)
    here = lax.axis_index(axis)
    edges = jnp.concatenate([value[..., :1], value[..., -1:]], axis=-1)
    spread = jnp.broadcast_to(edges[None], (size,) + edges.shape)
    got = lax.all_to_all(spread, axis, 0, 0, tiled=False)
    west = lax.dynamic_index_in_dim(got, (here - 1) % size, 0, keepdims=False)[..., 1:2]
    east = lax.dynamic_index_in_dim(got, (here + 1) % size, 0, keepdims=False)[..., 0:1]
    return west, east


def forecast_call(state, west, east):
    members, rows, cols = state.shape

    def kernel(x_ref, w_ref, e_ref, o_ref):
        col = lax.broadcasted_iota(jnp.int32, (rows, cols), 1)
        row = lax.broadcasted_iota(jnp.int32, (rows, cols), 0)

        def one(m, carry):
            x = x_ref[m].astype(jnp.float32)
            east_n = jnp.where(col == cols - 1, e_ref[m].astype(jnp.float32), pltpu.roll(x, cols - 1, 1))
            west_n = jnp.where(col == 0, w_ref[m].astype(jnp.float32), pltpu.roll(x, 1, 1))
            north = jnp.where(row == rows - 1, 0.0, pltpu.roll(x, rows - 1, 0))
            south = jnp.where(row == 0, 0.0, pltpu.roll(x, 1, 0))
            spread = east_n + west_n + north + south - 4.0 * x
            o_ref[m] = (x + 0.2 * spread - 0.3 * (east_n - west_n)).astype(jnp.bfloat16)
            return carry

        lax.fori_loop(0, members, one, 0, unroll=4)

    return pl.pallas_call(kernel, out_shape=jax.ShapeDtypeStruct(state.shape, jnp.bfloat16))(state, west, east)


def observe_region(state, index, weight):
    members, cells = state.shape
    count = index.shape[1]
    width = math.gcd(512, count)
    nblocks = count // width
    index_blocks = index.reshape(4, nblocks, width).transpose(1, 0, 2)
    weight_blocks = weight.reshape(4, nblocks, width).transpose(1, 0, 2)
    cell_ids = lax.broadcasted_iota(jnp.int32, (cells, width), 0)

    def observe_one_block(pieces):
        index_here, weight_here = pieces
        summed = jnp.zeros((members, width), jnp.float32)
        for k in range(4):
            selector = (cell_ids == index_here[k][None, :]).astype(jnp.bfloat16)
            picked = jnp.dot(state, selector, preferred_element_type=jnp.float32)
            summed = summed + weight_here[k][None, :] * picked
        return summed.astype(jnp.bfloat16)

    result = lax.map(observe_one_block, (index_blocks, weight_blocks))
    return result.transpose(1, 0, 2).reshape(members, count)


OBS_STEP = 256
def observe_dev_call(state, index, weight, extra=None):
    members, cells = state.shape
    count = index.shape[1]
    carry = extra is not None

    def kernel(f_ref, i_ref, w_ref, *rest):
        if carry:
            x_ref, o_ref = rest
        else:
            (o_ref,) = rest
        cell_ids = lax.broadcasted_iota(jnp.int32, (cells, OBS_STEP), 0)
        f = f_ref[...]
        summed = jnp.zeros((members, OBS_STEP), jnp.float32)
        for k in range(4):
            selector = (cell_ids == i_ref[k:k + 1, :]).astype(jnp.bfloat16)
            picked = jnp.dot(f, selector, preferred_element_type=jnp.float32)
            summed = summed + w_ref[k:k + 1, :] * picked
        ens = summed.astype(jnp.bfloat16).astype(jnp.float32)
        mean = jnp.sum(ens, axis=0, keepdims=True) / members
        dev = (ens - mean).astype(jnp.bfloat16)
        if carry:
            o_ref[0] = dev
            o_ref[1] = x_ref[...]
        else:
            o_ref[...] = dev

    in_specs = [
        pl.BlockSpec((members, cells), lambda j: (0, 0)),
        pl.BlockSpec((4, OBS_STEP), lambda j: (0, j)),
        pl.BlockSpec((4, OBS_STEP), lambda j: (0, j)),
    ]
    operands = [state, index, weight]
    if carry:
        in_specs.append(pl.BlockSpec((members, OBS_STEP), lambda j: (0, j)))
        operands.append(extra)
        out_spec = pl.BlockSpec((2, members, OBS_STEP), lambda j: (0, 0, j))
        out_shape = jax.ShapeDtypeStruct((2, members, count), jnp.bfloat16)
    else:
        out_spec = pl.BlockSpec((members, OBS_STEP), lambda j: (0, j))
        out_shape = jax.ShapeDtypeStruct((members, count), jnp.bfloat16)
    return pl.pallas_call(
        kernel,
        grid=(count // OBS_STEP,),
        in_specs=in_specs,
        out_specs=out_spec,
        out_shape=out_shape,
    )(*operands)


def anomaly_from_mean(state_values):
    centred = state_values.astype(jnp.float32)
    return (centred - jnp.mean(centred, axis=-2, keepdims=True)).astype(jnp.bfloat16)


def taper_tiles(classes, in_use, tile_width):
    row_ids = lax.broadcasted_iota(jnp.float32, (tile_width, tile_width), 0)
    col_ids = lax.broadcasted_iota(jnp.float32, (tile_width, tile_width), 1)
    offset = row_ids - col_ids
    length = 8.0 * jnp.exp2(classes.astype(jnp.float32))
    scaled = offset / length[..., None, None]
    return in_use[..., None, None] / (1.0 + scaled * scaled)


def body(background_ensemble, innov, obs_index, obs_weight, obs_list, tile_count, taper_class):
    west_col, east_col = column_halo(background_ensemble, "lon")
    prediction_increment = forecast_call(background_ensemble, west_col, east_col)
    ensemble_lines_here, whole_parallel_set, patch_meridian_lines = prediction_increment.shape
    members = innov.shape[0]
    band_rows = innov.shape[1]
    patch_gridpoints = band_rows * patch_meridian_lines
    region = lax.all_to_all(prediction_increment, "wide", split_axis=1, concat_axis=0, tiled=True)
    region_state = region.reshape(members, patch_gridpoints)
    first_row = lax.axis_index("wide") * band_rows
    local_index = lax.dynamic_slice_in_dim(obs_index, first_row, band_rows, 1).reshape(
        4, patch_gridpoints
    )
    local_index = local_index - first_row * patch_meridian_lines
    local_weight = lax.dynamic_slice_in_dim(obs_weight, first_row, band_rows, 1).reshape(
        4, patch_gridpoints
    )
    halo = HALO_BLK * BLK
    innov_flat = innov.reshape(members, patch_gridpoints)
    lon_size = lax.axis_size("lon")
    up = [(i, (i + 1) % lon_size) for i in range(lon_size)]
    down = [(j, i) for i, j in up]
    last_edge = observe_dev_call(
        region_state, local_index[:, -halo:], local_weight[:, -halo:], innov_flat[:, -halo:]
    )
    west = lax.ppermute(last_edge, "lon", up)
    first_edge = observe_dev_call(
        region_state, local_index[:, :halo], local_weight[:, :halo], innov_flat[:, :halo]
    )
    east = lax.ppermute(first_edge, "lon", down)
    middle_dev = observe_dev_call(region_state, local_index[:, halo:-halo], local_weight[:, halo:-halo])
    obs_dev = jnp.concatenate([first_edge[0], middle_dev, last_edge[0]], axis=1)
    halo_blocks = halo // BLK
    block_count = patch_gridpoints // BLK
    candidate_count = block_count + 2 * halo_blocks
    code = block_codes(obs_list[0], tile_count[0], taper_class[0], candidate_count)
    own_code = code[:, halo_blocks:halo_blocks + block_count]
    halo_code = jnp.concatenate([code[:, :halo_blocks], code[:, halo_blocks + block_count:]], axis=1)
    tiles = taper_table(BLK, members)
    partial = update_call(
        own_code.reshape(-1),
        region_state,
        None,
        [(first_edge, 0), (middle_dev, None), (last_edge, 0)],
        [(innov_flat, None)],
        tiles,
        block_count,
        block_count,
    )
    result = update_call(
        halo_code.reshape(-1),
        region_state,
        partial,
        [(west, 0), (east, 0)],
        [(west, 1), (east, 1)],
        tiles,
        block_count,
        2 * halo_blocks,
        group=8,
    )
    return lax.all_to_all(
        result.reshape(members, band_rows, patch_meridian_lines),
        "wide",
        split_axis=0,
        concat_axis=1,
        tiled=True,
    )


def block_codes(lists, counts, classes, candidate_count):
    zero_code = 4
    entries = jnp.arange(lists.shape[1], dtype=jnp.int32)
    value = jnp.where(entries[None, :] < counts[:, None], classes, zero_code)
    hit = lists[:, :, None] == jnp.arange(candidate_count, dtype=jnp.int32)[None, None, :]
    code = zero_code + jnp.sum(jnp.where(hit, value[:, :, None] - zero_code, 0), axis=1)
    return jnp.clip(code, 0, zero_code).astype(jnp.int32)


def taper_table(tile_width, members):
    row_ids = lax.broadcasted_iota(jnp.float32, (tile_width, tile_width), 0)
    col_ids = lax.broadcasted_iota(jnp.float32, (tile_width, tile_width), 1)
    offset = row_ids - col_ids
    length = 8.0 * jnp.exp2(jnp.arange(4, dtype=jnp.float32))
    scaled = offset[None] / length[:, None, None]
    tiles = (1.0 / (1.0 + scaled * scaled)) / (members - 1.0)
    return jnp.concatenate([tiles, jnp.zeros((1, tile_width, tile_width), jnp.float32)], axis=0)


GROUP = 4


def piece_spec(array):
    if array.ndim == 3:
        return pl.BlockSpec(array.shape, lambda g, code: (0, 0, 0))
    return pl.BlockSpec(array.shape, lambda g, code: (0, 0))


def piece_value(ref, pick):
    return ref[...] if pick is None else ref[pick]


def update_call(code, forecast, partial, obs_pieces, innov_pieces, tiles, block_count, candidate_count, group=GROUP):
    members, cells = forecast.shape
    rows = group * BLK
    width = candidate_count * BLK
    final = partial is not None
    obs_arrays = [a for a, _ in obs_pieces]
    innov_arrays = [a for a, _ in innov_pieces]
    n_obs = len(obs_pieces)
    n_innov = len(innov_pieces)

    def kernel(code_ref, f_ref, taper_ref, *rest):
        obs_refs = rest[:n_obs]
        innov_refs = rest[n_obs:n_obs + n_innov]
        rest = rest[n_obs + n_innov:]
        if final:
            part_ref, out_ref, cov_scr, tap_scr = rest
        else:
            out_ref, cov_scr, tap_scr = rest
        g = pl.program_id(0)
        forecast_block = f_ref[...].astype(jnp.float32)
        mean = jnp.sum(forecast_block, axis=0, keepdims=True) / members
        state = (forecast_block - mean).astype(jnp.bfloat16)
        offset = 0
        for ref, (_, pick) in zip(obs_refs, obs_pieces):
            piece = piece_value(ref, pick)
            span = piece.shape[1]
            cov_scr[:, offset:offset + span] = lax.dot_general(
                state, piece, (((0,), (0,)), ((), ())), preferred_element_type=jnp.float32
            )
            offset += span
        for sl in range(group):
            s = g * group + sl
            for b in range(candidate_count):
                c = code_ref[s * candidate_count + b]
                tile = cov_scr[sl * BLK:(sl + 1) * BLK, b * BLK:(b + 1) * BLK] * taper_ref[c]
                tap_scr[sl * BLK:(sl + 1) * BLK, b * BLK:(b + 1) * BLK] = tile.astype(jnp.bfloat16)
        change = None
        offset = 0
        for ref, (_, pick) in zip(innov_refs, innov_pieces):
            piece = piece_value(ref, pick)
            span = piece.shape[1]
            term = lax.dot_general(
                piece, tap_scr[:, offset:offset + span], (((1,), (1,)), ((), ())),
                preferred_element_type=jnp.float32,
            )
            change = term if change is None else change + term
            offset += span
        if final:
            total = part_ref[...] + change
            out_ref[...] = (forecast_block + total).astype(jnp.bfloat16)
        else:
            out_ref[...] = change

    col_spec = pl.BlockSpec((members, rows), lambda g, code: (0, g))
    in_specs = [col_spec, pl.BlockSpec(tiles.shape, lambda g, code: (0, 0, 0))]
    in_specs += [piece_spec(a) for a in obs_arrays] + [piece_spec(a) for a in innov_arrays]
    operands = [forecast, tiles] + obs_arrays + innov_arrays
    if final:
        in_specs.append(col_spec)
        operands.append(partial)
    grid_spec = pltpu.PrefetchScalarGridSpec(
        num_scalar_prefetch=1,
        grid=(block_count // group,),
        in_specs=in_specs,
        out_specs=col_spec,
        scratch_shapes=[
            pltpu.VMEM((rows, width), jnp.float32),
            pltpu.VMEM((rows, width), jnp.bfloat16),
        ],
    )
    out_type = jnp.bfloat16 if final else jnp.float32
    return pl.pallas_call(
        kernel,
        grid_spec=grid_spec,
        out_shape=jax.ShapeDtypeStruct((members, cells), out_type),
        cost_estimate=pl.CostEstimate(flops=4 * cells * members * width, transcendentals=0, bytes_accessed=8 * cells * members),
    )(code, *operands)


def solution(mesh):
    in_specs = (
        P("wide", None, "lon"),
        P(None, "wide", "lon"),
        P(None, None, "lon"),
        P(None, None, "lon"),
        P("lon", "wide", None),
        P("lon", "wide"),
        P("lon", "wide", None),
    )
    out_specs = P("wide", None, "lon")
    return jax.shard_map(body, mesh=mesh, in_specs=in_specs, out_specs=out_specs, check_vma=False)
```

```python
import math

import jax
import jax.numpy as jnp
from jax import lax
from jax.sharding import PartitionSpec as P
from jax.experimental import pallas as pl
from jax.experimental.pallas import tpu as pltpu

BLK = 128
HALO_BLK = 4


def padded_2(value, sides, width):
    for axis, dim in sides:
        size, length = (lax.axis_size(axis), value.shape[dim])
        up = [(i, (i + 1) % size) for i in range(size)]
        down = [(j, i) for i, j in up]
        last = lax.slice_in_dim(value, length - width, length, axis=dim)
        first = lax.slice_in_dim(value, 0, width, axis=dim)
        before = lax.ppermute(last, axis, up)
        after = lax.ppermute(first, axis, down)
        value = jnp.concatenate([before, value, after], axis=dim)
    return value


def column_halo(value, axis):
    size = lax.axis_size(axis)
    edges = jnp.concatenate([value[..., :1], value[..., -1:]], axis=-1)
    spread = jnp.broadcast_to(edges[None], (size,) + edges.shape)
    return lax.all_to_all(spread, axis, 0, 0, tiled=False)


def forecast_call(state, received, here):
    members, rows, cols = state.shape
    size = received.shape[0]
    position = jnp.reshape(here, (1,)).astype(jnp.int32)

    def kernel(pos_ref, x_ref, h_ref, o_ref):
        col = lax.broadcasted_iota(jnp.int32, (rows, cols), 1)
        row = lax.broadcasted_iota(jnp.int32, (rows, cols), 0)
        t = pos_ref[0]
        west_from = (t + size - 1) % size
        east_from = (t + 1) % size

        def one(m, carry):
            x = x_ref[m].astype(jnp.float32)
            west_col = h_ref[west_from, m][:, 1:2].astype(jnp.float32)
            east_col = h_ref[east_from, m][:, 0:1].astype(jnp.float32)
            east_n = jnp.where(col == cols - 1, east_col, pltpu.roll(x, cols - 1, 1))
            west_n = jnp.where(col == 0, west_col, pltpu.roll(x, 1, 1))
            north = jnp.where(row == rows - 1, 0.0, pltpu.roll(x, rows - 1, 0))
            south = jnp.where(row == 0, 0.0, pltpu.roll(x, 1, 0))
            spread = east_n + west_n + north + south - 4.0 * x
            o_ref[m] = (x + 0.2 * spread - 0.3 * (east_n - west_n)).astype(jnp.bfloat16)
            return carry

        lax.fori_loop(0, members, one, 0, unroll=4)

    grid_spec = pltpu.PrefetchScalarGridSpec(
        num_scalar_prefetch=1,
        grid=(1,),
        in_specs=[
            pl.BlockSpec(state.shape, lambda i, p: (0, 0, 0)),
            pl.BlockSpec(received.shape, lambda i, p: (0, 0, 0, 0)),
        ],
        out_specs=pl.BlockSpec(state.shape, lambda i, p: (0, 0, 0)),
    )
    return pl.pallas_call(
        kernel, grid_spec=grid_spec, out_shape=jax.ShapeDtypeStruct(state.shape, jnp.bfloat16)
    )(position, state, received)


def observe_region(state, index, weight):
    members, cells = state.shape
    count = index.shape[1]
    width = math.gcd(512, count)
    nblocks = count // width
    index_blocks = index.reshape(4, nblocks, width).transpose(1, 0, 2)
    weight_blocks = weight.reshape(4, nblocks, width).transpose(1, 0, 2)
    cell_ids = lax.broadcasted_iota(jnp.int32, (cells, width), 0)

    def observe_one_block(pieces):
        index_here, weight_here = pieces
        summed = jnp.zeros((members, width), jnp.float32)
        for k in range(4):
            selector = (cell_ids == index_here[k][None, :]).astype(jnp.bfloat16)
            picked = jnp.dot(state, selector, preferred_element_type=jnp.float32)
            summed = summed + weight_here[k][None, :] * picked
        return summed.astype(jnp.bfloat16)

    result = lax.map(observe_one_block, (index_blocks, weight_blocks))
    return result.transpose(1, 0, 2).reshape(members, count)


OBS_STEP = 256
def observe_dev_call(state, index, weight, extra=None):
    members, cells = state.shape
    count = index.shape[1]
    carry = extra is not None

    def kernel(f_ref, i_ref, w_ref, *rest):
        if carry:
            x_ref, o_ref = rest
        else:
            (o_ref,) = rest
        cell_ids = lax.broadcasted_iota(jnp.int32, (cells, OBS_STEP), 0)
        f = f_ref[...]
        summed = jnp.zeros((members, OBS_STEP), jnp.float32)
        for k in range(4):
            selector = (cell_ids == i_ref[k:k + 1, :]).astype(jnp.bfloat16)
            picked = jnp.dot(f, selector, preferred_element_type=jnp.float32)
            summed = summed + w_ref[k:k + 1, :] * picked
        ens = summed.astype(jnp.bfloat16).astype(jnp.float32)
        mean = jnp.sum(ens, axis=0, keepdims=True) / members
        dev = (ens - mean).astype(jnp.bfloat16)
        if carry:
            o_ref[0] = dev
            o_ref[1] = x_ref[...]
        else:
            o_ref[...] = dev

    in_specs = [
        pl.BlockSpec((members, cells), lambda j: (0, 0)),
        pl.BlockSpec((4, OBS_STEP), lambda j: (0, j)),
        pl.BlockSpec((4, OBS_STEP), lambda j: (0, j)),
    ]
    operands = [state, index, weight]
    if carry:
        in_specs.append(pl.BlockSpec((members, OBS_STEP), lambda j: (0, j)))
        operands.append(extra)
        out_spec = pl.BlockSpec((2, members, OBS_STEP), lambda j: (0, 0, j))
        out_shape = jax.ShapeDtypeStruct((2, members, count), jnp.bfloat16)
    else:
        out_spec = pl.BlockSpec((members, OBS_STEP), lambda j: (0, j))
        out_shape = jax.ShapeDtypeStruct((members, count), jnp.bfloat16)
    return pl.pallas_call(
        kernel,
        grid=(count // OBS_STEP,),
        in_specs=in_specs,
        out_specs=out_spec,
        out_shape=out_shape,
    )(*operands)


def anomaly_from_mean(state_values):
    centred = state_values.astype(jnp.float32)
    return (centred - jnp.mean(centred, axis=-2, keepdims=True)).astype(jnp.bfloat16)


def taper_tiles(classes, in_use, tile_width):
    row_ids = lax.broadcasted_iota(jnp.float32, (tile_width, tile_width), 0)
    col_ids = lax.broadcasted_iota(jnp.float32, (tile_width, tile_width), 1)
    offset = row_ids - col_ids
    length = 8.0 * jnp.exp2(classes.astype(jnp.float32))
    scaled = offset / length[..., None, None]
    return in_use[..., None, None] / (1.0 + scaled * scaled)


def body(background_ensemble, innov, obs_index, obs_weight, obs_list, tile_count, taper_class):
    received = column_halo(background_ensemble, "lon")
    prediction_increment = forecast_call(background_ensemble, received, lax.axis_index("lon"))
    ensemble_lines_here, whole_parallel_set, patch_meridian_lines = prediction_increment.shape
    members = innov.shape[0]
    band_rows = innov.shape[1]
    patch_gridpoints = band_rows * patch_meridian_lines
    region = lax.all_to_all(prediction_increment, "wide", split_axis=1, concat_axis=0, tiled=True)
    region_state = region.reshape(members, patch_gridpoints)
    first_row = lax.axis_index("wide") * band_rows
    local_index = lax.dynamic_slice_in_dim(obs_index, first_row, band_rows, 1).reshape(
        4, patch_gridpoints
    )
    local_index = local_index - first_row * patch_meridian_lines
    local_weight = lax.dynamic_slice_in_dim(obs_weight, first_row, band_rows, 1).reshape(
        4, patch_gridpoints
    )
    halo = HALO_BLK * BLK
    innov_flat = innov.reshape(members, patch_gridpoints)
    lon_size = lax.axis_size("lon")
    up = [(i, (i + 1) % lon_size) for i in range(lon_size)]
    down = [(j, i) for i, j in up]
    last_edge = observe_dev_call(
        region_state, local_index[:, -halo:], local_weight[:, -halo:], innov_flat[:, -halo:]
    )
    west = lax.ppermute(last_edge, "lon", up)
    first_edge = observe_dev_call(
        region_state, local_index[:, :halo], local_weight[:, :halo], innov_flat[:, :halo]
    )
    east = lax.ppermute(first_edge, "lon", down)
    middle_dev = observe_dev_call(region_state, local_index[:, halo:-halo], local_weight[:, halo:-halo])
    obs_dev = jnp.concatenate([first_edge[0], middle_dev, last_edge[0]], axis=1)
    halo_blocks = halo // BLK
    block_count = patch_gridpoints // BLK
    candidate_count = block_count + 2 * halo_blocks
    code = block_codes(obs_list[0], tile_count[0], taper_class[0], candidate_count)
    own_code = code[:, halo_blocks:halo_blocks + block_count]
    halo_code = jnp.concatenate([code[:, :halo_blocks], code[:, halo_blocks + block_count:]], axis=1)
    tiles = taper_table(BLK, members)
    partial = update_call(
        own_code.reshape(-1),
        region_state,
        None,
        [(first_edge, 0), (middle_dev, None), (last_edge, 0)],
        [(innov_flat, None)],
        tiles,
        block_count,
        block_count,
    )
    result = update_call(
        halo_code.reshape(-1),
        region_state,
        partial,
        [(west, 0), (east, 0)],
        [(west, 1), (east, 1)],
        tiles,
        block_count,
        2 * halo_blocks,
        group=8,
    )
    return lax.all_to_all(
        result.reshape(members, band_rows, patch_meridian_lines),
        "wide",
        split_axis=0,
        concat_axis=1,
        tiled=True,
    )


def block_codes(lists, counts, classes, candidate_count):
    zero_code = 4
    entries = jnp.arange(lists.shape[1], dtype=jnp.int32)
    value = jnp.where(entries[None, :] < counts[:, None], classes, zero_code)
    hit = lists[:, :, None] == jnp.arange(candidate_count, dtype=jnp.int32)[None, None, :]
    code = zero_code + jnp.sum(jnp.where(hit, value[:, :, None] - zero_code, 0), axis=1)
    return jnp.clip(code, 0, zero_code).astype(jnp.int32)


def taper_table(tile_width, members):
    row_ids = lax.broadcasted_iota(jnp.float32, (tile_width, tile_width), 0)
    col_ids = lax.broadcasted_iota(jnp.float32, (tile_width, tile_width), 1)
    offset = row_ids - col_ids
    length = 8.0 * jnp.exp2(jnp.arange(4, dtype=jnp.float32))
    scaled = offset[None] / length[:, None, None]
    tiles = (1.0 / (1.0 + scaled * scaled)) / (members - 1.0)
    return jnp.concatenate([tiles, jnp.zeros((1, tile_width, tile_width), jnp.float32)], axis=0)


GROUP = 4


def piece_spec(array):
    if array.ndim == 3:
        return pl.BlockSpec(array.shape, lambda g, code: (0, 0, 0))
    return pl.BlockSpec(array.shape, lambda g, code: (0, 0))


def piece_value(ref, pick):
    return ref[...] if pick is None else ref[pick]


def update_call(code, forecast, partial, obs_pieces, innov_pieces, tiles, block_count, candidate_count, group=GROUP):
    members, cells = forecast.shape
    rows = group * BLK
    width = candidate_count * BLK
    final = partial is not None
    obs_arrays = [a for a, _ in obs_pieces]
    innov_arrays = [a for a, _ in innov_pieces]
    n_obs = len(obs_pieces)
    n_innov = len(innov_pieces)

    def kernel(code_ref, f_ref, taper_ref, *rest):
        obs_refs = rest[:n_obs]
        innov_refs = rest[n_obs:n_obs + n_innov]
        rest = rest[n_obs + n_innov:]
        if final:
            part_ref, out_ref, cov_scr, tap_scr = rest
        else:
            out_ref, cov_scr, tap_scr = rest
        g = pl.program_id(0)
        forecast_block = f_ref[...].astype(jnp.float32)
        mean = jnp.sum(forecast_block, axis=0, keepdims=True) / members
        state = (forecast_block - mean).astype(jnp.bfloat16)
        offset = 0
        for ref, (_, pick) in zip(obs_refs, obs_pieces):
            piece = piece_value(ref, pick)
            span = piece.shape[1]
            cov_scr[:, offset:offset + span] = lax.dot_general(
                state, piece, (((0,), (0,)), ((), ())), preferred_element_type=jnp.float32
            )
            offset += span
        for sl in range(group):
            s = g * group + sl
            for b in range(candidate_count):
                c = code_ref[s * candidate_count + b]
                tile = cov_scr[sl * BLK:(sl + 1) * BLK, b * BLK:(b + 1) * BLK] * taper_ref[c]
                tap_scr[sl * BLK:(sl + 1) * BLK, b * BLK:(b + 1) * BLK] = tile.astype(jnp.bfloat16)
        change = None
        offset = 0
        for ref, (_, pick) in zip(innov_refs, innov_pieces):
            piece = piece_value(ref, pick)
            span = piece.shape[1]
            term = lax.dot_general(
                piece, tap_scr[:, offset:offset + span], (((1,), (1,)), ((), ())),
                preferred_element_type=jnp.float32,
            )
            change = term if change is None else change + term
            offset += span
        if final:
            total = part_ref[...] + change
            out_ref[...] = (forecast_block + total).astype(jnp.bfloat16)
        else:
            out_ref[...] = change

    col_spec = pl.BlockSpec((members, rows), lambda g, code: (0, g))
    in_specs = [col_spec, pl.BlockSpec(tiles.shape, lambda g, code: (0, 0, 0))]
    in_specs += [piece_spec(a) for a in obs_arrays] + [piece_spec(a) for a in innov_arrays]
    operands = [forecast, tiles] + obs_arrays + innov_arrays
    if final:
        in_specs.append(col_spec)
        operands.append(partial)
    grid_spec = pltpu.PrefetchScalarGridSpec(
        num_scalar_prefetch=1,
        grid=(block_count // group,),
        in_specs=in_specs,
        out_specs=col_spec,
        scratch_shapes=[
            pltpu.VMEM((rows, width), jnp.float32),
            pltpu.VMEM((rows, width), jnp.bfloat16),
        ],
    )
    out_type = jnp.bfloat16 if final else jnp.float32
    return pl.pallas_call(
        kernel,
        grid_spec=grid_spec,
        out_shape=jax.ShapeDtypeStruct((members, cells), out_type),
        cost_estimate=pl.CostEstimate(flops=4 * cells * members * width, transcendentals=0, bytes_accessed=8 * cells * members),
    )(code, *operands)


def solution(mesh):
    in_specs = (
        P("wide", None, "lon"),
        P(None, "wide", "lon"),
        P(None, None, "lon"),
        P(None, None, "lon"),
        P("lon", "wide", None),
        P("lon", "wide"),
        P("lon", "wide", None),
    )
    out_specs = P("wide", None, "lon")
    return jax.shard_map(body, mesh=mesh, in_specs=in_specs, out_specs=out_specs, check_vma=False)
```

```python
import math

import jax
import jax.numpy as jnp
from jax import lax
from jax.sharding import PartitionSpec as P
from jax.experimental import pallas as pl
from jax.experimental.pallas import tpu as pltpu

BLK = 128
HALO_BLK = 4


def padded_2(value, sides, width):
    for axis, dim in sides:
        size, length = (lax.axis_size(axis), value.shape[dim])
        up = [(i, (i + 1) % size) for i in range(size)]
        down = [(j, i) for i, j in up]
        last = lax.slice_in_dim(value, length - width, length, axis=dim)
        first = lax.slice_in_dim(value, 0, width, axis=dim)
        before = lax.ppermute(last, axis, up)
        after = lax.ppermute(first, axis, down)
        value = jnp.concatenate([before, value, after], axis=dim)
    return value


def column_halo(value, axis):
    size = lax.axis_size(axis)
    edges = jnp.concatenate([value[..., :1], value[..., -1:]], axis=-1)
    spread = jnp.broadcast_to(edges[None], (size,) + edges.shape)
    return lax.all_to_all(spread, axis, 0, 0, tiled=False)


def forecast_call(state, received, here):
    members, rows, cols = state.shape
    size = received.shape[0]
    position = jnp.reshape(here, (1,)).astype(jnp.int32)

    def kernel(pos_ref, x_ref, h_ref, o_ref):
        col = lax.broadcasted_iota(jnp.int32, (rows, cols), 1)
        row = lax.broadcasted_iota(jnp.int32, (rows, cols), 0)
        t = pos_ref[0]
        west_from = (t + size - 1) % size
        east_from = (t + 1) % size

        def one(m, carry):
            x = x_ref[m].astype(jnp.float32)
            west_col = h_ref[west_from, m][:, 1:2].astype(jnp.float32)
            east_col = h_ref[east_from, m][:, 0:1].astype(jnp.float32)
            east_n = jnp.where(col == cols - 1, east_col, pltpu.roll(x, cols - 1, 1))
            west_n = jnp.where(col == 0, west_col, pltpu.roll(x, 1, 1))
            north = jnp.where(row == rows - 1, 0.0, pltpu.roll(x, rows - 1, 0))
            south = jnp.where(row == 0, 0.0, pltpu.roll(x, 1, 0))
            spread = east_n + west_n + north + south - 4.0 * x
            o_ref[:, m, :] = (x + 0.2 * spread - 0.3 * (east_n - west_n)).astype(jnp.bfloat16)
            return carry

        for m in range(members):
            one(m, 0)

    grid_spec = pltpu.PrefetchScalarGridSpec(
        num_scalar_prefetch=1,
        grid=(1,),
        in_specs=[
            pl.BlockSpec(state.shape, lambda i, p: (0, 0, 0)),
            pl.BlockSpec(received.shape, lambda i, p: (0, 0, 0, 0)),
        ],
        out_specs=pl.BlockSpec((rows, members, cols), lambda i, p: (0, 0, 0)),
    )
    return pl.pallas_call(
        kernel, grid_spec=grid_spec, out_shape=jax.ShapeDtypeStruct((rows, members, cols), jnp.bfloat16)
    )(position, state, received)


def observe_region(state, index, weight):
    members, cells = state.shape
    count = index.shape[1]
    width = math.gcd(512, count)
    nblocks = count // width
    index_blocks = index.reshape(4, nblocks, width).transpose(1, 0, 2)
    weight_blocks = weight.reshape(4, nblocks, width).transpose(1, 0, 2)
    cell_ids = lax.broadcasted_iota(jnp.int32, (cells, width), 0)

    def observe_one_block(pieces):
        index_here, weight_here = pieces
        summed = jnp.zeros((members, width), jnp.float32)
        for k in range(4):
            selector = (cell_ids == index_here[k][None, :]).astype(jnp.bfloat16)
            picked = jnp.dot(state, selector, preferred_element_type=jnp.float32)
            summed = summed + weight_here[k][None, :] * picked
        return summed.astype(jnp.bfloat16)

    result = lax.map(observe_one_block, (index_blocks, weight_blocks))
    return result.transpose(1, 0, 2).reshape(members, count)


OBS_STEP = 256
def observe_dev_call(state, index, weight, extra=None):
    members, cells = state.shape
    count = index.shape[1]
    carry = extra is not None

    def kernel(f_ref, i_ref, w_ref, *rest):
        if carry:
            x_ref, o_ref = rest
        else:
            (o_ref,) = rest
        cell_ids = lax.broadcasted_iota(jnp.int32, (cells, OBS_STEP), 0)
        f = f_ref[...]
        summed = jnp.zeros((members, OBS_STEP), jnp.float32)
        for k in range(4):
            selector = (cell_ids == i_ref[k:k + 1, :]).astype(jnp.bfloat16)
            picked = jnp.dot(f, selector, preferred_element_type=jnp.float32)
            summed = summed + w_ref[k:k + 1, :] * picked
        ens = summed.astype(jnp.bfloat16).astype(jnp.float32)
        mean = jnp.sum(ens, axis=0, keepdims=True) / members
        dev = (ens - mean).astype(jnp.bfloat16)
        if carry:
            o_ref[0] = dev
            o_ref[1] = x_ref[...]
        else:
            o_ref[...] = dev

    in_specs = [
        pl.BlockSpec((members, cells), lambda j: (0, 0)),
        pl.BlockSpec((4, OBS_STEP), lambda j: (0, j)),
        pl.BlockSpec((4, OBS_STEP), lambda j: (0, j)),
    ]
    operands = [state, index, weight]
    if carry:
        in_specs.append(pl.BlockSpec((members, OBS_STEP), lambda j: (0, j)))
        operands.append(extra)
        out_spec = pl.BlockSpec((2, members, OBS_STEP), lambda j: (0, 0, j))
        out_shape = jax.ShapeDtypeStruct((2, members, count), jnp.bfloat16)
    else:
        out_spec = pl.BlockSpec((members, OBS_STEP), lambda j: (0, j))
        out_shape = jax.ShapeDtypeStruct((members, count), jnp.bfloat16)
    return pl.pallas_call(
        kernel,
        grid=(count // OBS_STEP,),
        in_specs=in_specs,
        out_specs=out_spec,
        out_shape=out_shape,
    )(*operands)


def anomaly_from_mean(state_values):
    centred = state_values.astype(jnp.float32)
    return (centred - jnp.mean(centred, axis=-2, keepdims=True)).astype(jnp.bfloat16)


def taper_tiles(classes, in_use, tile_width):
    row_ids = lax.broadcasted_iota(jnp.float32, (tile_width, tile_width), 0)
    col_ids = lax.broadcasted_iota(jnp.float32, (tile_width, tile_width), 1)
    offset = row_ids - col_ids
    length = 8.0 * jnp.exp2(classes.astype(jnp.float32))
    scaled = offset / length[..., None, None]
    return in_use[..., None, None] / (1.0 + scaled * scaled)


def body(background_ensemble, innov, obs_index, obs_weight, obs_list, tile_count, taper_class):
    received = column_halo(background_ensemble, "lon")
    prediction_increment = forecast_call(background_ensemble, received, lax.axis_index("lon"))
    whole_parallel_set, ensemble_lines_here, patch_meridian_lines = prediction_increment.shape
    members = innov.shape[0]
    band_rows = innov.shape[1]
    patch_gridpoints = band_rows * patch_meridian_lines
    region = lax.all_to_all(prediction_increment, "wide", split_axis=0, concat_axis=1, tiled=True)
    region_state = region.transpose(1, 0, 2).reshape(members, patch_gridpoints)
    first_row = lax.axis_index("wide") * band_rows
    local_index = lax.dynamic_slice_in_dim(obs_index, first_row, band_rows, 1).reshape(
        4, patch_gridpoints
    )
    local_index = local_index - first_row * patch_meridian_lines
    local_weight = lax.dynamic_slice_in_dim(obs_weight, first_row, band_rows, 1).reshape(
        4, patch_gridpoints
    )
    halo = HALO_BLK * BLK
    innov_flat = innov.reshape(members, patch_gridpoints)
    lon_size = lax.axis_size("lon")
    up = [(i, (i + 1) % lon_size) for i in range(lon_size)]
    down = [(j, i) for i, j in up]
    last_edge = observe_dev_call(
        region_state, local_index[:, -halo:], local_weight[:, -halo:], innov_flat[:, -halo:]
    )
    west = lax.ppermute(last_edge, "lon", up)
    first_edge = observe_dev_call(
        region_state, local_index[:, :halo], local_weight[:, :halo], innov_flat[:, :halo]
    )
    east = lax.ppermute(first_edge, "lon", down)
    middle_dev = observe_dev_call(region_state, local_index[:, halo:-halo], local_weight[:, halo:-halo])
    obs_dev = jnp.concatenate([first_edge[0], middle_dev, last_edge[0]], axis=1)
    halo_blocks = halo // BLK
    block_count = patch_gridpoints // BLK
    candidate_count = block_count + 2 * halo_blocks
    code = block_codes(obs_list[0], tile_count[0], taper_class[0], candidate_count)
    own_code = code[:, halo_blocks:halo_blocks + block_count]
    halo_code = jnp.concatenate([code[:, :halo_blocks], code[:, halo_blocks + block_count:]], axis=1)
    tiles = taper_table(BLK, members)
    partial = update_call(
        own_code.reshape(-1),
        region_state,
        None,
        [(first_edge, 0), (middle_dev, None), (last_edge, 0)],
        [(innov_flat, None)],
        tiles,
        block_count,
        block_count,
    )
    result = update_call(
        halo_code.reshape(-1),
        region_state,
        partial,
        [(west, 0), (east, 0)],
        [(west, 1), (east, 1)],
        tiles,
        block_count,
        2 * halo_blocks,
        group=8,
    )
    return lax.all_to_all(
        result.reshape(members, band_rows, patch_meridian_lines),
        "wide",
        split_axis=0,
        concat_axis=1,
        tiled=True,
    )


def block_codes(lists, counts, classes, candidate_count):
    zero_code = 4
    entries = jnp.arange(lists.shape[1], dtype=jnp.int32)
    value = jnp.where(entries[None, :] < counts[:, None], classes, zero_code)
    hit = lists[:, :, None] == jnp.arange(candidate_count, dtype=jnp.int32)[None, None, :]
    code = zero_code + jnp.sum(jnp.where(hit, value[:, :, None] - zero_code, 0), axis=1)
    return jnp.clip(code, 0, zero_code).astype(jnp.int32)


def taper_table(tile_width, members):
    row_ids = lax.broadcasted_iota(jnp.float32, (tile_width, tile_width), 0)
    col_ids = lax.broadcasted_iota(jnp.float32, (tile_width, tile_width), 1)
    offset = row_ids - col_ids
    length = 8.0 * jnp.exp2(jnp.arange(4, dtype=jnp.float32))
    scaled = offset[None] / length[:, None, None]
    tiles = (1.0 / (1.0 + scaled * scaled)) / (members - 1.0)
    return jnp.concatenate([tiles, jnp.zeros((1, tile_width, tile_width), jnp.float32)], axis=0)


GROUP = 4


def piece_spec(array):
    if array.ndim == 3:
        return pl.BlockSpec(array.shape, lambda g, code: (0, 0, 0))
    return pl.BlockSpec(array.shape, lambda g, code: (0, 0))


def piece_value(ref, pick):
    return ref[...] if pick is None else ref[pick]


def update_call(code, forecast, partial, obs_pieces, innov_pieces, tiles, block_count, candidate_count, group=GROUP):
    members, cells = forecast.shape
    rows = group * BLK
    width = candidate_count * BLK
    final = partial is not None
    obs_arrays = [a for a, _ in obs_pieces]
    innov_arrays = [a for a, _ in innov_pieces]
    n_obs = len(obs_pieces)
    n_innov = len(innov_pieces)

    def kernel(code_ref, f_ref, taper_ref, *rest):
        obs_refs = rest[:n_obs]
        innov_refs = rest[n_obs:n_obs + n_innov]
        rest = rest[n_obs + n_innov:]
        if final:
            part_ref, out_ref, cov_scr, tap_scr = rest
        else:
            out_ref, cov_scr, tap_scr = rest
        g = pl.program_id(0)
        forecast_block = f_ref[...].astype(jnp.float32)
        mean = jnp.sum(forecast_block, axis=0, keepdims=True) / members
        state = (forecast_block - mean).astype(jnp.bfloat16)
        offset = 0
        for ref, (_, pick) in zip(obs_refs, obs_pieces):
            piece = piece_value(ref, pick)
            span = piece.shape[1]
            cov_scr[:, offset:offset + span] = lax.dot_general(
                state, piece, (((0,), (0,)), ((), ())), preferred_element_type=jnp.float32
            )
            offset += span
        for sl in range(group):
            s = g * group + sl
            for b in range(candidate_count):
                c = code_ref[s * candidate_count + b]
                tile = cov_scr[sl * BLK:(sl + 1) * BLK, b * BLK:(b + 1) * BLK] * taper_ref[c]
                tap_scr[sl * BLK:(sl + 1) * BLK, b * BLK:(b + 1) * BLK] = tile.astype(jnp.bfloat16)
        change = None
        offset = 0
        for ref, (_, pick) in zip(innov_refs, innov_pieces):
            piece = piece_value(ref, pick)
            span = piece.shape[1]
            term = lax.dot_general(
                piece, tap_scr[:, offset:offset + span], (((1,), (1,)), ((), ())),
                preferred_element_type=jnp.float32,
            )
            change = term if change is None else change + term
            offset += span
        if final:
            total = part_ref[...] + change
            out_ref[...] = (forecast_block + total).astype(jnp.bfloat16)
        else:
            out_ref[...] = change

    col_spec = pl.BlockSpec((members, rows), lambda g, code: (0, g))
    in_specs = [col_spec, pl.BlockSpec(tiles.shape, lambda g, code: (0, 0, 0))]
    in_specs += [piece_spec(a) for a in obs_arrays] + [piece_spec(a) for a in innov_arrays]
    operands = [forecast, tiles] + obs_arrays + innov_arrays
    if final:
        in_specs.append(col_spec)
        operands.append(partial)
    grid_spec = pltpu.PrefetchScalarGridSpec(
        num_scalar_prefetch=1,
        grid=(block_count // group,),
        in_specs=in_specs,
        out_specs=col_spec,
        scratch_shapes=[
            pltpu.VMEM((rows, width), jnp.float32),
            pltpu.VMEM((rows, width), jnp.bfloat16),
        ],
    )
    out_type = jnp.bfloat16 if final else jnp.float32
    return pl.pallas_call(
        kernel,
        grid_spec=grid_spec,
        out_shape=jax.ShapeDtypeStruct((members, cells), out_type),
        cost_estimate=pl.CostEstimate(flops=4 * cells * members * width, transcendentals=0, bytes_accessed=8 * cells * members),
    )(code, *operands)


def solution(mesh):
    in_specs = (
        P("wide", None, "lon"),
        P(None, "wide", "lon"),
        P(None, None, "lon"),
        P(None, None, "lon"),
        P("lon", "wide", None),
        P("lon", "wide"),
        P("lon", "wide", None),
    )
    out_specs = P("wide", None, "lon")
    return jax.shard_map(body, mesh=mesh, in_specs=in_specs, out_specs=out_specs, check_vma=False)
```

```python
import math

import jax
import jax.numpy as jnp
from jax import lax
from jax.sharding import PartitionSpec as P
from jax.experimental import pallas as pl
from jax.experimental.pallas import tpu as pltpu

BLK = 128
HALO_BLK = 4


def padded_2(value, sides, width):
    for axis, dim in sides:
        size, length = (lax.axis_size(axis), value.shape[dim])
        up = [(i, (i + 1) % size) for i in range(size)]
        down = [(j, i) for i, j in up]
        last = lax.slice_in_dim(value, length - width, length, axis=dim)
        first = lax.slice_in_dim(value, 0, width, axis=dim)
        before = lax.ppermute(last, axis, up)
        after = lax.ppermute(first, axis, down)
        value = jnp.concatenate([before, value, after], axis=dim)
    return value


def column_halo(value, axis):
    size = lax.axis_size(axis)
    edges = jnp.concatenate([value[..., :1], value[..., -1:]], axis=-1)
    spread = jnp.broadcast_to(edges[None], (size,) + edges.shape)
    return lax.all_to_all(spread, axis, 0, 0, tiled=False)


def forecast_call(state, received, here):
    members, rows, cols = state.shape
    size = received.shape[0]
    position = jnp.reshape(here, (1,)).astype(jnp.int32)

    def kernel(pos_ref, x_ref, h_ref, o_ref):
        col = lax.broadcasted_iota(jnp.int32, (rows, cols), 1)
        row = lax.broadcasted_iota(jnp.int32, (rows, cols), 0)
        t = pos_ref[0]
        west_from = (t + size - 1) % size
        east_from = (t + 1) % size

        def one(m, carry):
            x = x_ref[m].astype(jnp.float32)
            west_col = h_ref[west_from, m][:, 1:2].astype(jnp.float32)
            east_col = h_ref[east_from, m][:, 0:1].astype(jnp.float32)
            east_n = jnp.where(col == cols - 1, east_col, pltpu.roll(x, cols - 1, 1))
            west_n = jnp.where(col == 0, west_col, pltpu.roll(x, 1, 1))
            north = jnp.where(row == rows - 1, 0.0, pltpu.roll(x, rows - 1, 0))
            south = jnp.where(row == 0, 0.0, pltpu.roll(x, 1, 0))
            spread = east_n + west_n + north + south - 4.0 * x
            o_ref[:, m, :] = (x + 0.2 * spread - 0.3 * (east_n - west_n)).astype(jnp.bfloat16)
            return carry

        for m in range(members):
            one(m, 0)

    grid_spec = pltpu.PrefetchScalarGridSpec(
        num_scalar_prefetch=1,
        grid=(1,),
        in_specs=[
            pl.BlockSpec(state.shape, lambda i, p: (0, 0, 0)),
            pl.BlockSpec(received.shape, lambda i, p: (0, 0, 0, 0)),
        ],
        out_specs=pl.BlockSpec((rows, members, cols), lambda i, p: (0, 0, 0)),
    )
    return pl.pallas_call(
        kernel, grid_spec=grid_spec, out_shape=jax.ShapeDtypeStruct((rows, members, cols), jnp.bfloat16)
    )(position, state, received)


def observe_region(state, index, weight):
    members, cells = state.shape
    count = index.shape[1]
    width = math.gcd(512, count)
    nblocks = count // width
    index_blocks = index.reshape(4, nblocks, width).transpose(1, 0, 2)
    weight_blocks = weight.reshape(4, nblocks, width).transpose(1, 0, 2)
    cell_ids = lax.broadcasted_iota(jnp.int32, (cells, width), 0)

    def observe_one_block(pieces):
        index_here, weight_here = pieces
        summed = jnp.zeros((members, width), jnp.float32)
        for k in range(4):
            selector = (cell_ids == index_here[k][None, :]).astype(jnp.bfloat16)
            picked = jnp.dot(state, selector, preferred_element_type=jnp.float32)
            summed = summed + weight_here[k][None, :] * picked
        return summed.astype(jnp.bfloat16)

    result = lax.map(observe_one_block, (index_blocks, weight_blocks))
    return result.transpose(1, 0, 2).reshape(members, count)


OBS_STEP = 256
def observe_dev_call(state, index, weight, extra=None):
    members, cells = state.shape
    count = index.shape[1]
    carry = extra is not None

    def kernel(f_ref, i_ref, w_ref, *rest):
        if carry:
            x_ref, o_ref = rest
        else:
            (o_ref,) = rest
        cell_ids = lax.broadcasted_iota(jnp.int32, (cells, OBS_STEP), 0)
        f = f_ref[...]
        summed = jnp.zeros((members, OBS_STEP), jnp.float32)
        for k in range(4):
            selector = (cell_ids == i_ref[k:k + 1, :]).astype(jnp.bfloat16)
            picked = jnp.dot(f, selector, preferred_element_type=jnp.float32)
            summed = summed + w_ref[k:k + 1, :] * picked
        ens = summed.astype(jnp.bfloat16).astype(jnp.float32)
        mean = jnp.sum(ens, axis=0, keepdims=True) / members
        dev = (ens - mean).astype(jnp.bfloat16)
        if carry:
            o_ref[0] = dev
            o_ref[1] = x_ref[...]
        else:
            o_ref[...] = dev

    in_specs = [
        pl.BlockSpec((members, cells), lambda j: (0, 0)),
        pl.BlockSpec((4, OBS_STEP), lambda j: (0, j)),
        pl.BlockSpec((4, OBS_STEP), lambda j: (0, j)),
    ]
    operands = [state, index, weight]
    if carry:
        in_specs.append(pl.BlockSpec((members, OBS_STEP), lambda j: (0, j)))
        operands.append(extra)
        out_spec = pl.BlockSpec((2, members, OBS_STEP), lambda j: (0, 0, j))
        out_shape = jax.ShapeDtypeStruct((2, members, count), jnp.bfloat16)
    else:
        out_spec = pl.BlockSpec((members, OBS_STEP), lambda j: (0, j))
        out_shape = jax.ShapeDtypeStruct((members, count), jnp.bfloat16)
    return pl.pallas_call(
        kernel,
        grid=(count // OBS_STEP,),
        in_specs=in_specs,
        out_specs=out_spec,
        out_shape=out_shape,
    )(*operands)


def anomaly_from_mean(state_values):
    centred = state_values.astype(jnp.float32)
    return (centred - jnp.mean(centred, axis=-2, keepdims=True)).astype(jnp.bfloat16)


def taper_tiles(classes, in_use, tile_width):
    row_ids = lax.broadcasted_iota(jnp.float32, (tile_width, tile_width), 0)
    col_ids = lax.broadcasted_iota(jnp.float32, (tile_width, tile_width), 1)
    offset = row_ids - col_ids
    length = 8.0 * jnp.exp2(classes.astype(jnp.float32))
    scaled = offset / length[..., None, None]
    return in_use[..., None, None] / (1.0 + scaled * scaled)


def body(background_ensemble, innov, obs_index, obs_weight, obs_list, tile_count, taper_class):
    received = column_halo(background_ensemble, "lon")
    prediction_increment = forecast_call(background_ensemble, received, lax.axis_index("lon"))
    whole_parallel_set, ensemble_lines_here, patch_meridian_lines = prediction_increment.shape
    members = innov.shape[0]
    band_rows = innov.shape[1]
    patch_gridpoints = band_rows * patch_meridian_lines
    region = lax.all_to_all(prediction_increment, "wide", split_axis=0, concat_axis=1, tiled=True)
    region_state = region.transpose(1, 0, 2).reshape(members, patch_gridpoints)
    first_row = lax.axis_index("wide") * band_rows
    local_index = lax.dynamic_slice_in_dim(obs_index, first_row, band_rows, 1).reshape(
        4, patch_gridpoints
    )
    local_index = local_index - first_row * patch_meridian_lines
    local_weight = lax.dynamic_slice_in_dim(obs_weight, first_row, band_rows, 1).reshape(
        4, patch_gridpoints
    )
    halo = HALO_BLK * BLK
    innov_flat = innov.reshape(members, patch_gridpoints)
    lon_size = lax.axis_size("lon")
    up = [(i, (i + 1) % lon_size) for i in range(lon_size)]
    down = [(j, i) for i, j in up]
    last_edge = observe_dev_call(
        region_state, local_index[:, -halo:], local_weight[:, -halo:], innov_flat[:, -halo:]
    )
    west = lax.ppermute(last_edge, "lon", up)
    first_edge = observe_dev_call(
        region_state, local_index[:, :halo], local_weight[:, :halo], innov_flat[:, :halo]
    )
    east = lax.ppermute(first_edge, "lon", down)
    middle_dev = observe_dev_call(region_state, local_index[:, halo:-halo], local_weight[:, halo:-halo])
    obs_dev = jnp.concatenate([first_edge[0], middle_dev, last_edge[0]], axis=1)
    halo_blocks = halo // BLK
    block_count = patch_gridpoints // BLK
    candidate_count = block_count + 2 * halo_blocks
    code = block_codes(obs_list[0], tile_count[0], taper_class[0], candidate_count)
    own_code = code[:, halo_blocks:halo_blocks + block_count]
    halo_code = jnp.concatenate([code[:, :halo_blocks], code[:, halo_blocks + block_count:]], axis=1)
    tiles = taper_table(BLK, members)
    partial = update_call(
        own_code.reshape(-1),
        region_state,
        None,
        [(first_edge, 0), (middle_dev, None), (last_edge, 0)],
        [(innov_flat, None)],
        tiles,
        block_count,
        block_count,
        group=8,
    )
    result = update_call(
        halo_code.reshape(-1),
        region_state,
        partial,
        [(west, 0), (east, 0)],
        [(west, 1), (east, 1)],
        tiles,
        block_count,
        2 * halo_blocks,
        group=8,
    )
    return lax.all_to_all(
        result.reshape(members, band_rows, patch_meridian_lines),
        "wide",
        split_axis=0,
        concat_axis=1,
        tiled=True,
    )


def block_codes(lists, counts, classes, candidate_count):
    zero_code = 4
    entries = jnp.arange(lists.shape[1], dtype=jnp.int32)
    value = jnp.where(entries[None, :] < counts[:, None], classes, zero_code)
    hit = lists[:, :, None] == jnp.arange(candidate_count, dtype=jnp.int32)[None, None, :]
    code = zero_code + jnp.sum(jnp.where(hit, value[:, :, None] - zero_code, 0), axis=1)
    return jnp.clip(code, 0, zero_code).astype(jnp.int32)


def taper_table(tile_width, members):
    row_ids = lax.broadcasted_iota(jnp.float32, (tile_width, tile_width), 0)
    col_ids = lax.broadcasted_iota(jnp.float32, (tile_width, tile_width), 1)
    offset = row_ids - col_ids
    length = 8.0 * jnp.exp2(jnp.arange(4, dtype=jnp.float32))
    scaled = offset[None] / length[:, None, None]
    tiles = (1.0 / (1.0 + scaled * scaled)) / (members - 1.0)
    return jnp.concatenate([tiles, jnp.zeros((1, tile_width, tile_width), jnp.float32)], axis=0)


GROUP = 4


def piece_spec(array):
    if array.ndim == 3:
        return pl.BlockSpec(array.shape, lambda g, code: (0, 0, 0))
    return pl.BlockSpec(array.shape, lambda g, code: (0, 0))


def piece_value(ref, pick):
    return ref[...] if pick is None else ref[pick]


def update_call(code, forecast, partial, obs_pieces, innov_pieces, tiles, block_count, candidate_count, group=GROUP):
    members, cells = forecast.shape
    rows = group * BLK
    width = candidate_count * BLK
    final = partial is not None
    obs_arrays = [a for a, _ in obs_pieces]
    innov_arrays = [a for a, _ in innov_pieces]
    n_obs = len(obs_pieces)
    n_innov = len(innov_pieces)

    def kernel(code_ref, f_ref, taper_ref, *rest):
        obs_refs = rest[:n_obs]
        innov_refs = rest[n_obs:n_obs + n_innov]
        rest = rest[n_obs + n_innov:]
        if final:
            part_ref, out_ref, cov_scr, tap_scr = rest
        else:
            out_ref, cov_scr, tap_scr = rest
        g = pl.program_id(0)
        forecast_block = f_ref[...].astype(jnp.float32)
        mean = jnp.sum(forecast_block, axis=0, keepdims=True) / members
        state = (forecast_block - mean).astype(jnp.bfloat16)
        offset = 0
        for ref, (_, pick) in zip(obs_refs, obs_pieces):
            piece = piece_value(ref, pick)
            span = piece.shape[1]
            cov_scr[:, offset:offset + span] = lax.dot_general(
                state, piece, (((0,), (0,)), ((), ())), preferred_element_type=jnp.float32
            )
            offset += span
        for sl in range(group):
            s = g * group + sl
            for b in range(candidate_count):
                c = code_ref[s * candidate_count + b]
                tile = cov_scr[sl * BLK:(sl + 1) * BLK, b * BLK:(b + 1) * BLK] * taper_ref[c]
                tap_scr[sl * BLK:(sl + 1) * BLK, b * BLK:(b + 1) * BLK] = tile.astype(jnp.bfloat16)
        change = None
        offset = 0
        for ref, (_, pick) in zip(innov_refs, innov_pieces):
            piece = piece_value(ref, pick)
            span = piece.shape[1]
            term = lax.dot_general(
                piece, tap_scr[:, offset:offset + span], (((1,), (1,)), ((), ())),
                preferred_element_type=jnp.float32,
            )
            change = term if change is None else change + term
            offset += span
        if final:
            total = part_ref[...] + change
            out_ref[...] = (forecast_block + total).astype(jnp.bfloat16)
        else:
            out_ref[...] = change

    col_spec = pl.BlockSpec((members, rows), lambda g, code: (0, g))
    in_specs = [col_spec, pl.BlockSpec(tiles.shape, lambda g, code: (0, 0, 0))]
    in_specs += [piece_spec(a) for a in obs_arrays] + [piece_spec(a) for a in innov_arrays]
    operands = [forecast, tiles] + obs_arrays + innov_arrays
    if final:
        in_specs.append(col_spec)
        operands.append(partial)
    grid_spec = pltpu.PrefetchScalarGridSpec(
        num_scalar_prefetch=1,
        grid=(block_count // group,),
        in_specs=in_specs,
        out_specs=col_spec,
        scratch_shapes=[
            pltpu.VMEM((rows, width), jnp.float32),
            pltpu.VMEM((rows, width), jnp.bfloat16),
        ],
    )
    out_type = jnp.bfloat16 if final else jnp.float32
    return pl.pallas_call(
        kernel,
        grid_spec=grid_spec,
        out_shape=jax.ShapeDtypeStruct((members, cells), out_type),
        cost_estimate=pl.CostEstimate(flops=4 * cells * members * width, transcendentals=0, bytes_accessed=8 * cells * members),
    )(code, *operands)


def solution(mesh):
    in_specs = (
        P("wide", None, "lon"),
        P(None, "wide", "lon"),
        P(None, None, "lon"),
        P(None, None, "lon"),
        P("lon", "wide", None),
        P("lon", "wide"),
        P("lon", "wide", None),
    )
    out_specs = P("wide", None, "lon")
    return jax.shard_map(body, mesh=mesh, in_specs=in_specs, out_specs=out_specs, check_vma=False)
```

```python
import math

import numpy as np

import jax
import jax.numpy as jnp
from jax import lax
from jax.sharding import PartitionSpec as P
from jax.experimental import pallas as pl
from jax.experimental.pallas import tpu as pltpu

BLK = 128
HALO_BLK = 4


def padded_2(value, sides, width):
    for axis, dim in sides:
        size, length = (lax.axis_size(axis), value.shape[dim])
        up = [(i, (i + 1) % size) for i in range(size)]
        down = [(j, i) for i, j in up]
        last = lax.slice_in_dim(value, length - width, length, axis=dim)
        first = lax.slice_in_dim(value, 0, width, axis=dim)
        before = lax.ppermute(last, axis, up)
        after = lax.ppermute(first, axis, down)
        value = jnp.concatenate([before, value, after], axis=dim)
    return value


def column_halo(value, axis):
    size = lax.axis_size(axis)
    edges = jnp.concatenate([value[..., :1], value[..., -1:]], axis=-1)
    spread = jnp.broadcast_to(edges[None], (size,) + edges.shape)
    return lax.all_to_all(spread, axis, 0, 0, tiled=False)


def forecast_call(state, received, here):
    members, rows, cols = state.shape
    size = received.shape[0]
    position = jnp.reshape(here, (1,)).astype(jnp.int32)

    def kernel(pos_ref, x_ref, h_ref, o_ref):
        col = lax.broadcasted_iota(jnp.int32, (rows, cols), 1)
        row = lax.broadcasted_iota(jnp.int32, (rows, cols), 0)
        t = pos_ref[0]
        west_from = (t + size - 1) % size
        east_from = (t + 1) % size

        def one(m, carry):
            x = x_ref[m].astype(jnp.float32)
            west_col = h_ref[west_from, m][:, 1:2].astype(jnp.float32)
            east_col = h_ref[east_from, m][:, 0:1].astype(jnp.float32)
            east_n = jnp.where(col == cols - 1, east_col, pltpu.roll(x, cols - 1, 1))
            west_n = jnp.where(col == 0, west_col, pltpu.roll(x, 1, 1))
            north = jnp.where(row == rows - 1, 0.0, pltpu.roll(x, rows - 1, 0))
            south = jnp.where(row == 0, 0.0, pltpu.roll(x, 1, 0))
            spread = east_n + west_n + north + south - 4.0 * x
            o_ref[:, m, :] = (x + 0.2 * spread - 0.3 * (east_n - west_n)).astype(jnp.bfloat16)
            return carry

        for m in range(members):
            one(m, 0)

    grid_spec = pltpu.PrefetchScalarGridSpec(
        num_scalar_prefetch=1,
        grid=(1,),
        in_specs=[
            pl.BlockSpec(state.shape, lambda i, p: (0, 0, 0)),
            pl.BlockSpec(received.shape, lambda i, p: (0, 0, 0, 0)),
        ],
        out_specs=pl.BlockSpec((rows, members, cols), lambda i, p: (0, 0, 0)),
    )
    return pl.pallas_call(
        kernel, grid_spec=grid_spec, out_shape=jax.ShapeDtypeStruct((rows, members, cols), jnp.bfloat16)
    )(position, state, received)


def observe_region(state, index, weight):
    members, cells = state.shape
    count = index.shape[1]
    width = math.gcd(512, count)
    nblocks = count // width
    index_blocks = index.reshape(4, nblocks, width).transpose(1, 0, 2)
    weight_blocks = weight.reshape(4, nblocks, width).transpose(1, 0, 2)
    cell_ids = lax.broadcasted_iota(jnp.int32, (cells, width), 0)

    def observe_one_block(pieces):
        index_here, weight_here = pieces
        summed = jnp.zeros((members, width), jnp.float32)
        for k in range(4):
            selector = (cell_ids == index_here[k][None, :]).astype(jnp.bfloat16)
            picked = jnp.dot(state, selector, preferred_element_type=jnp.float32)
            summed = summed + weight_here[k][None, :] * picked
        return summed.astype(jnp.bfloat16)

    result = lax.map(observe_one_block, (index_blocks, weight_blocks))
    return result.transpose(1, 0, 2).reshape(members, count)


OBS_STEP = 256
def observe_dev_call(state, index, weight, extra=None):
    members, cells = state.shape
    count = index.shape[1]
    carry = extra is not None

    def kernel(f_ref, i_ref, w_ref, *rest):
        if carry:
            x_ref, o_ref = rest
        else:
            (o_ref,) = rest
        cell_ids = lax.broadcasted_iota(jnp.int32, (cells, OBS_STEP), 0)
        f = f_ref[...]
        summed = jnp.zeros((members, OBS_STEP), jnp.float32)
        for k in range(4):
            selector = (cell_ids == i_ref[k:k + 1, :]).astype(jnp.bfloat16)
            picked = jnp.dot(f, selector, preferred_element_type=jnp.float32)
            summed = summed + w_ref[k:k + 1, :] * picked
        ens = summed.astype(jnp.bfloat16).astype(jnp.float32)
        mean = jnp.sum(ens, axis=0, keepdims=True) / members
        dev = (ens - mean).astype(jnp.bfloat16)
        if carry:
            o_ref[0] = dev
            o_ref[1] = x_ref[...]
        else:
            o_ref[...] = dev

    in_specs = [
        pl.BlockSpec((members, cells), lambda j: (0, 0)),
        pl.BlockSpec((4, OBS_STEP), lambda j: (0, j)),
        pl.BlockSpec((4, OBS_STEP), lambda j: (0, j)),
    ]
    operands = [state, index, weight]
    if carry:
        in_specs.append(pl.BlockSpec((members, OBS_STEP), lambda j: (0, j)))
        operands.append(extra)
        out_spec = pl.BlockSpec((2, members, OBS_STEP), lambda j: (0, 0, j))
        out_shape = jax.ShapeDtypeStruct((2, members, count), jnp.bfloat16)
    else:
        out_spec = pl.BlockSpec((members, OBS_STEP), lambda j: (0, j))
        out_shape = jax.ShapeDtypeStruct((members, count), jnp.bfloat16)
    return pl.pallas_call(
        kernel,
        grid=(count // OBS_STEP,),
        in_specs=in_specs,
        out_specs=out_spec,
        out_shape=out_shape,
    )(*operands)


def anomaly_from_mean(state_values):
    centred = state_values.astype(jnp.float32)
    return (centred - jnp.mean(centred, axis=-2, keepdims=True)).astype(jnp.bfloat16)


def taper_tiles(classes, in_use, tile_width):
    row_ids = lax.broadcasted_iota(jnp.float32, (tile_width, tile_width), 0)
    col_ids = lax.broadcasted_iota(jnp.float32, (tile_width, tile_width), 1)
    offset = row_ids - col_ids
    length = 8.0 * jnp.exp2(classes.astype(jnp.float32))
    scaled = offset / length[..., None, None]
    return in_use[..., None, None] / (1.0 + scaled * scaled)


def body(background_ensemble, innov, obs_index, obs_weight, obs_list, tile_count, taper_class):
    received = column_halo(background_ensemble, "lon")
    prediction_increment = forecast_call(background_ensemble, received, lax.axis_index("lon"))
    whole_parallel_set, ensemble_lines_here, patch_meridian_lines = prediction_increment.shape
    members = innov.shape[0]
    band_rows = innov.shape[1]
    patch_gridpoints = band_rows * patch_meridian_lines
    region = lax.all_to_all(prediction_increment, "wide", split_axis=0, concat_axis=1, tiled=True)
    region_state = region.transpose(1, 0, 2).reshape(members, patch_gridpoints)
    first_row = lax.axis_index("wide") * band_rows
    local_index = lax.dynamic_slice_in_dim(obs_index, first_row, band_rows, 1).reshape(
        4, patch_gridpoints
    )
    local_index = local_index - first_row * patch_meridian_lines
    local_weight = lax.dynamic_slice_in_dim(obs_weight, first_row, band_rows, 1).reshape(
        4, patch_gridpoints
    )
    halo = HALO_BLK * BLK
    innov_flat = innov.reshape(members, patch_gridpoints)
    lon_size = lax.axis_size("lon")
    up = [(i, (i + 1) % lon_size) for i in range(lon_size)]
    down = [(j, i) for i, j in up]
    last_edge = observe_dev_call(
        region_state, local_index[:, -halo:], local_weight[:, -halo:], innov_flat[:, -halo:]
    )
    west = lax.ppermute(last_edge, "lon", up)
    first_edge = observe_dev_call(
        region_state, local_index[:, :halo], local_weight[:, :halo], innov_flat[:, :halo]
    )
    east = lax.ppermute(first_edge, "lon", down)
    middle_dev = observe_dev_call(region_state, local_index[:, halo:-halo], local_weight[:, halo:-halo])
    obs_dev = jnp.concatenate([first_edge[0], middle_dev, last_edge[0]], axis=1)
    halo_blocks = halo // BLK
    block_count = patch_gridpoints // BLK
    candidate_count = block_count + 2 * halo_blocks
    code = block_codes(obs_list[0], tile_count[0], taper_class[0], candidate_count)
    own_code = code[:, halo_blocks:halo_blocks + block_count]
    halo_code = jnp.concatenate([code[:, :halo_blocks], code[:, halo_blocks + block_count:]], axis=1)
    tiles = taper_table(BLK, members)
    partial = update_call(
        own_code.reshape(-1),
        region_state,
        None,
        [(first_edge, 0), (middle_dev, None), (last_edge, 0)],
        [(innov_flat, None)],
        tiles,
        block_count,
        block_count,
        group=8,
    )
    result = update_call(
        halo_code.reshape(-1),
        region_state,
        partial,
        [(west, 0), (east, 0)],
        [(west, 1), (east, 1)],
        tiles,
        block_count,
        2 * halo_blocks,
        group=8,
    )
    return lax.all_to_all(
        result.reshape(members, band_rows, patch_meridian_lines),
        "wide",
        split_axis=0,
        concat_axis=1,
        tiled=True,
    )


def block_codes(lists, counts, classes, candidate_count):
    zero_code = 4
    entries = jnp.arange(lists.shape[1], dtype=jnp.int32)
    value = jnp.where(entries[None, :] < counts[:, None], classes, zero_code)
    hit = lists[:, :, None] == jnp.arange(candidate_count, dtype=jnp.int32)[None, None, :]
    code = zero_code + jnp.sum(jnp.where(hit, value[:, :, None] - zero_code, 0), axis=1)
    return jnp.clip(code, 0, zero_code).astype(jnp.int32)


def taper_table(tile_width, members):
    offset = np.arange(tile_width, dtype=np.float32)[:, None] - np.arange(tile_width, dtype=np.float32)[None, :]
    length = np.float32(8.0) * np.exp2(np.arange(4, dtype=np.float32))
    scaled = offset[None] / length[:, None, None]
    one = np.float32(1.0)
    tiles = (one / (one + scaled * scaled)) / np.float32(members - 1.0)
    zero = np.zeros((1, tile_width, tile_width), np.float32)
    return jnp.asarray(np.concatenate([tiles, zero], axis=0).astype(np.float32))


GROUP = 4


def piece_spec(array):
    if array.ndim == 3:
        return pl.BlockSpec(array.shape, lambda g, code: (0, 0, 0))
    return pl.BlockSpec(array.shape, lambda g, code: (0, 0))


def piece_value(ref, pick):
    return ref[...] if pick is None else ref[pick]


def update_call(code, forecast, partial, obs_pieces, innov_pieces, tiles, block_count, candidate_count, group=GROUP):
    members, cells = forecast.shape
    rows = group * BLK
    width = candidate_count * BLK
    final = partial is not None
    obs_arrays = [a for a, _ in obs_pieces]
    innov_arrays = [a for a, _ in innov_pieces]
    n_obs = len(obs_pieces)
    n_innov = len(innov_pieces)

    def kernel(code_ref, f_ref, taper_ref, *rest):
        obs_refs = rest[:n_obs]
        innov_refs = rest[n_obs:n_obs + n_innov]
        rest = rest[n_obs + n_innov:]
        if final:
            part_ref, out_ref, cov_scr, tap_scr = rest
        else:
            out_ref, cov_scr, tap_scr = rest
        g = pl.program_id(0)
        forecast_block = f_ref[...].astype(jnp.float32)
        mean = jnp.sum(forecast_block, axis=0, keepdims=True) / members
        state = (forecast_block - mean).astype(jnp.bfloat16)
        offset = 0
        for ref, (_, pick) in zip(obs_refs, obs_pieces):
            piece = piece_value(ref, pick)
            span = piece.shape[1]
            cov_scr[:, offset:offset + span] = lax.dot_general(
                state, piece, (((0,), (0,)), ((), ())), preferred_element_type=jnp.float32
            )
            offset += span
        for sl in range(group):
            s = g * group + sl
            for b in range(candidate_count):
                c = code_ref[s * candidate_count + b]
                tile = cov_scr[sl * BLK:(sl + 1) * BLK, b * BLK:(b + 1) * BLK] * taper_ref[c]
                tap_scr[sl * BLK:(sl + 1) * BLK, b * BLK:(b + 1) * BLK] = tile.astype(jnp.bfloat16)
        change = None
        offset = 0
        for ref, (_, pick) in zip(innov_refs, innov_pieces):
            piece = piece_value(ref, pick)
            span = piece.shape[1]
            term = lax.dot_general(
                piece, tap_scr[:, offset:offset + span], (((1,), (1,)), ((), ())),
                preferred_element_type=jnp.float32,
            )
            change = term if change is None else change + term
            offset += span
        if final:
            total = part_ref[...] + change
            out_ref[...] = (forecast_block + total).astype(jnp.bfloat16)
        else:
            out_ref[...] = change

    col_spec = pl.BlockSpec((members, rows), lambda g, code: (0, g))
    in_specs = [col_spec, pl.BlockSpec(tiles.shape, lambda g, code: (0, 0, 0))]
    in_specs += [piece_spec(a) for a in obs_arrays] + [piece_spec(a) for a in innov_arrays]
    operands = [forecast, tiles] + obs_arrays + innov_arrays
    if final:
        in_specs.append(col_spec)
        operands.append(partial)
    grid_spec = pltpu.PrefetchScalarGridSpec(
        num_scalar_prefetch=1,
        grid=(block_count // group,),
        in_specs=in_specs,
        out_specs=col_spec,
        scratch_shapes=[
            pltpu.VMEM((rows, width), jnp.float32),
            pltpu.VMEM((rows, width), jnp.bfloat16),
        ],
    )
    out_type = jnp.bfloat16 if final else jnp.float32
    return pl.pallas_call(
        kernel,
        grid_spec=grid_spec,
        out_shape=jax.ShapeDtypeStruct((members, cells), out_type),
        cost_estimate=pl.CostEstimate(flops=4 * cells * members * width, transcendentals=0, bytes_accessed=8 * cells * members),
    )(code, *operands)


def solution(mesh):
    in_specs = (
        P("wide", None, "lon"),
        P(None, "wide", "lon"),
        P(None, None, "lon"),
        P(None, None, "lon"),
        P("lon", "wide", None),
        P("lon", "wide"),
        P("lon", "wide", None),
    )
    out_specs = P("wide", None, "lon")
    return jax.shard_map(body, mesh=mesh, in_specs=in_specs, out_specs=out_specs, check_vma=False)
```

```python
import math

import jax
import jax.numpy as jnp
from jax import lax
from jax.sharding import PartitionSpec as P
from jax.experimental import pallas as pl
from jax.experimental.pallas import tpu as pltpu

BLK = 128
HALO_BLK = 4


def padded_2(value, sides, width):
    for axis, dim in sides:
        size, length = (lax.axis_size(axis), value.shape[dim])
        up = [(i, (i + 1) % size) for i in range(size)]
        down = [(j, i) for i, j in up]
        last = lax.slice_in_dim(value, length - width, length, axis=dim)
        first = lax.slice_in_dim(value, 0, width, axis=dim)
        before = lax.ppermute(last, axis, up)
        after = lax.ppermute(first, axis, down)
        value = jnp.concatenate([before, value, after], axis=dim)
    return value


def column_halo(value, axis):
    size = lax.axis_size(axis)
    edges = jnp.concatenate([value[..., :1], value[..., -1:]], axis=-1)
    spread = jnp.broadcast_to(edges[None], (size,) + edges.shape)
    return lax.all_to_all(spread, axis, 0, 0, tiled=False)


def forecast_call(state, received, here):
    members, rows, cols = state.shape
    size = received.shape[0]
    position = jnp.reshape(here, (1,)).astype(jnp.int32)

    def kernel(pos_ref, x_ref, h_ref, o_ref):
        col = lax.broadcasted_iota(jnp.int32, (rows, cols), 1)
        row = lax.broadcasted_iota(jnp.int32, (rows, cols), 0)
        t = pos_ref[0]
        west_from = (t + size - 1) % size
        east_from = (t + 1) % size

        def one(m):
            x = x_ref[m].astype(jnp.float32)
            west_col = h_ref[west_from, m][:, 1:2].astype(jnp.float32)
            east_col = h_ref[east_from, m][:, 0:1].astype(jnp.float32)
            east_n = jnp.where(col == cols - 1, east_col, pltpu.roll(x, cols - 1, 1))
            west_n = jnp.where(col == 0, west_col, pltpu.roll(x, 1, 1))
            north = jnp.where(row == rows - 1, 0.0, pltpu.roll(x, rows - 1, 0))
            south = jnp.where(row == 0, 0.0, pltpu.roll(x, 1, 0))
            spread = east_n + west_n + north + south - 4.0 * x
            return (x + 0.2 * spread - 0.3 * (east_n - west_n)).astype(jnp.bfloat16)

        def group(i, carry):
            base = pl.multiple_of(i * 8, 8)
            values = jnp.stack([one(base + j) for j in range(8)], axis=1)
            o_ref[:, pl.ds(base, 8), :] = values
            return carry

        lax.fori_loop(0, members // 8, group, 0)

    grid_spec = pltpu.PrefetchScalarGridSpec(
        num_scalar_prefetch=1,
        grid=(1,),
        in_specs=[
            pl.BlockSpec(state.shape, lambda i, p: (0, 0, 0)),
            pl.BlockSpec(received.shape, lambda i, p: (0, 0, 0, 0)),
        ],
        out_specs=pl.BlockSpec((rows, members, cols), lambda i, p: (0, 0, 0)),
    )
    return pl.pallas_call(
        kernel, grid_spec=grid_spec, out_shape=jax.ShapeDtypeStruct((rows, members, cols), jnp.bfloat16)
    )(position, state, received)


def observe_region(state, index, weight):
    members, cells = state.shape
    count = index.shape[1]
    width = math.gcd(512, count)
    nblocks = count // width
    index_blocks = index.reshape(4, nblocks, width).transpose(1, 0, 2)
    weight_blocks = weight.reshape(4, nblocks, width).transpose(1, 0, 2)
    cell_ids = lax.broadcasted_iota(jnp.int32, (cells, width), 0)

    def observe_one_block(pieces):
        index_here, weight_here = pieces
        summed = jnp.zeros((members, width), jnp.float32)
        for k in range(4):
            selector = (cell_ids == index_here[k][None, :]).astype(jnp.bfloat16)
            picked = jnp.dot(state, selector, preferred_element_type=jnp.float32)
            summed = summed + weight_here[k][None, :] * picked
        return summed.astype(jnp.bfloat16)

    result = lax.map(observe_one_block, (index_blocks, weight_blocks))
    return result.transpose(1, 0, 2).reshape(members, count)


OBS_STEP = 256
def observe_dev_call(state, index, weight, extra=None):
    members, cells = state.shape
    count = index.shape[1]
    carry = extra is not None

    def kernel(f_ref, i_ref, w_ref, *rest):
        if carry:
            x_ref, o_ref = rest
        else:
            (o_ref,) = rest
        cell_ids = lax.broadcasted_iota(jnp.int32, (cells, OBS_STEP), 0)
        f = f_ref[...]
        summed = jnp.zeros((members, OBS_STEP), jnp.float32)
        for k in range(4):
            selector = (cell_ids == i_ref[k:k + 1, :]).astype(jnp.bfloat16)
            picked = jnp.dot(f, selector, preferred_element_type=jnp.float32)
            summed = summed + w_ref[k:k + 1, :] * picked
        ens = summed.astype(jnp.bfloat16).astype(jnp.float32)
        mean = jnp.sum(ens, axis=0, keepdims=True) / members
        dev = (ens - mean).astype(jnp.bfloat16)
        if carry:
            o_ref[0] = dev
            o_ref[1] = x_ref[...]
        else:
            o_ref[...] = dev

    in_specs = [
        pl.BlockSpec((members, cells), lambda j: (0, 0)),
        pl.BlockSpec((4, OBS_STEP), lambda j: (0, j)),
        pl.BlockSpec((4, OBS_STEP), lambda j: (0, j)),
    ]
    operands = [state, index, weight]
    if carry:
        in_specs.append(pl.BlockSpec((members, OBS_STEP), lambda j: (0, j)))
        operands.append(extra)
        out_spec = pl.BlockSpec((2, members, OBS_STEP), lambda j: (0, 0, j))
        out_shape = jax.ShapeDtypeStruct((2, members, count), jnp.bfloat16)
    else:
        out_spec = pl.BlockSpec((members, OBS_STEP), lambda j: (0, j))
        out_shape = jax.ShapeDtypeStruct((members, count), jnp.bfloat16)
    return pl.pallas_call(
        kernel,
        grid=(count // OBS_STEP,),
        in_specs=in_specs,
        out_specs=out_spec,
        out_shape=out_shape,
    )(*operands)


def anomaly_from_mean(state_values):
    centred = state_values.astype(jnp.float32)
    return (centred - jnp.mean(centred, axis=-2, keepdims=True)).astype(jnp.bfloat16)


def taper_tiles(classes, in_use, tile_width):
    row_ids = lax.broadcasted_iota(jnp.float32, (tile_width, tile_width), 0)
    col_ids = lax.broadcasted_iota(jnp.float32, (tile_width, tile_width), 1)
    offset = row_ids - col_ids
    length = 8.0 * jnp.exp2(classes.astype(jnp.float32))
    scaled = offset / length[..., None, None]
    return in_use[..., None, None] / (1.0 + scaled * scaled)


def body(background_ensemble, innov, obs_index, obs_weight, obs_list, tile_count, taper_class):
    received = column_halo(background_ensemble, "lon")
    prediction_increment = forecast_call(background_ensemble, received, lax.axis_index("lon"))
    whole_parallel_set, ensemble_lines_here, patch_meridian_lines = prediction_increment.shape
    members = innov.shape[0]
    band_rows = innov.shape[1]
    patch_gridpoints = band_rows * patch_meridian_lines
    region = lax.all_to_all(prediction_increment, "wide", split_axis=0, concat_axis=1, tiled=True)
    region_state = region.transpose(1, 0, 2).reshape(members, patch_gridpoints)
    first_row = lax.axis_index("wide") * band_rows
    local_index = lax.dynamic_slice_in_dim(obs_index, first_row, band_rows, 1).reshape(
        4, patch_gridpoints
    )
    local_index = local_index - first_row * patch_meridian_lines
    local_weight = lax.dynamic_slice_in_dim(obs_weight, first_row, band_rows, 1).reshape(
        4, patch_gridpoints
    )
    halo = HALO_BLK * BLK
    innov_flat = innov.reshape(members, patch_gridpoints)
    lon_size = lax.axis_size("lon")
    up = [(i, (i + 1) % lon_size) for i in range(lon_size)]
    down = [(j, i) for i, j in up]
    last_edge = observe_dev_call(
        region_state, local_index[:, -halo:], local_weight[:, -halo:], innov_flat[:, -halo:]
    )
    west = lax.ppermute(last_edge, "lon", up)
    first_edge = observe_dev_call(
        region_state, local_index[:, :halo], local_weight[:, :halo], innov_flat[:, :halo]
    )
    east = lax.ppermute(first_edge, "lon", down)
    middle_dev = observe_dev_call(region_state, local_index[:, halo:-halo], local_weight[:, halo:-halo])
    obs_dev = jnp.concatenate([first_edge[0], middle_dev, last_edge[0]], axis=1)
    halo_blocks = halo // BLK
    block_count = patch_gridpoints // BLK
    candidate_count = block_count + 2 * halo_blocks
    code = block_codes(obs_list[0], tile_count[0], taper_class[0], candidate_count)
    own_code = code[:, halo_blocks:halo_blocks + block_count]
    halo_code = jnp.concatenate([code[:, :halo_blocks], code[:, halo_blocks + block_count:]], axis=1)
    tiles = taper_table(BLK, members)
    partial = update_call(
        own_code.reshape(-1),
        region_state,
        None,
        [(first_edge, 0), (middle_dev, None), (last_edge, 0)],
        [(innov_flat, None)],
        tiles,
        block_count,
        block_count,
        group=8,
    )
    result = update_call(
        halo_code.reshape(-1),
        region_state,
        partial,
        [(west, 0), (east, 0)],
        [(west, 1), (east, 1)],
        tiles,
        block_count,
        2 * halo_blocks,
        group=8,
    )
    return lax.all_to_all(
        result.reshape(members, band_rows, patch_meridian_lines),
        "wide",
        split_axis=0,
        concat_axis=1,
        tiled=True,
    )


def block_codes(lists, counts, classes, candidate_count):
    zero_code = 4
    entries = jnp.arange(lists.shape[1], dtype=jnp.int32)
    value = jnp.where(entries[None, :] < counts[:, None], classes, zero_code)
    hit = lists[:, :, None] == jnp.arange(candidate_count, dtype=jnp.int32)[None, None, :]
    code = zero_code + jnp.sum(jnp.where(hit, value[:, :, None] - zero_code, 0), axis=1)
    return jnp.clip(code, 0, zero_code).astype(jnp.int32)


def taper_table(tile_width, members):
    row_ids = lax.broadcasted_iota(jnp.float32, (tile_width, tile_width), 0)
    col_ids = lax.broadcasted_iota(jnp.float32, (tile_width, tile_width), 1)
    offset = row_ids - col_ids
    length = 8.0 * jnp.exp2(jnp.arange(4, dtype=jnp.float32))
    scaled = offset[None] / length[:, None, None]
    tiles = (1.0 / (1.0 + scaled * scaled)) / (members - 1.0)
    return jnp.concatenate([tiles, jnp.zeros((1, tile_width, tile_width), jnp.float32)], axis=0)


GROUP = 4


def piece_spec(array):
    if array.ndim == 3:
        return pl.BlockSpec(array.shape, lambda g, code: (0, 0, 0))
    return pl.BlockSpec(array.shape, lambda g, code: (0, 0))


def piece_value(ref, pick):
    return ref[...] if pick is None else ref[pick]


def update_call(code, forecast, partial, obs_pieces, innov_pieces, tiles, block_count, candidate_count, group=GROUP):
    members, cells = forecast.shape
    rows = group * BLK
    width = candidate_count * BLK
    final = partial is not None
    obs_arrays = [a for a, _ in obs_pieces]
    innov_arrays = [a for a, _ in innov_pieces]
    n_obs = len(obs_pieces)
    n_innov = len(innov_pieces)

    def kernel(code_ref, f_ref, taper_ref, *rest):
        obs_refs = rest[:n_obs]
        innov_refs = rest[n_obs:n_obs + n_innov]
        rest = rest[n_obs + n_innov:]
        if final:
            part_ref, out_ref, cov_scr, tap_scr = rest
        else:
            out_ref, cov_scr, tap_scr = rest
        g = pl.program_id(0)
        forecast_block = f_ref[...].astype(jnp.float32)
        mean = jnp.sum(forecast_block, axis=0, keepdims=True) / members
        state = (forecast_block - mean).astype(jnp.bfloat16)
        offset = 0
        for ref, (_, pick) in zip(obs_refs, obs_pieces):
            piece = piece_value(ref, pick)
            span = piece.shape[1]
            cov_scr[:, offset:offset + span] = lax.dot_general(
                state, piece, (((0,), (0,)), ((), ())), preferred_element_type=jnp.float32
            )
            offset += span
        for sl in range(group):
            s = g * group + sl
            for b in range(candidate_count):
                c = code_ref[s * candidate_count + b]
                tile = cov_scr[sl * BLK:(sl + 1) * BLK, b * BLK:(b + 1) * BLK] * taper_ref[c]
                tap_scr[sl * BLK:(sl + 1) * BLK, b * BLK:(b + 1) * BLK] = tile.astype(jnp.bfloat16)
        change = None
        offset = 0
        for ref, (_, pick) in zip(innov_refs, innov_pieces):
            piece = piece_value(ref, pick)
            span = piece.shape[1]
            term = lax.dot_general(
                piece, tap_scr[:, offset:offset + span], (((1,), (1,)), ((), ())),
                preferred_element_type=jnp.float32,
            )
            change = term if change is None else change + term
            offset += span
        if final:
            total = part_ref[...] + change
            out_ref[...] = (forecast_block + total).astype(jnp.bfloat16)
        else:
            out_ref[...] = change

    col_spec = pl.BlockSpec((members, rows), lambda g, code: (0, g))
    in_specs = [col_spec, pl.BlockSpec(tiles.shape, lambda g, code: (0, 0, 0))]
    in_specs += [piece_spec(a) for a in obs_arrays] + [piece_spec(a) for a in innov_arrays]
    operands = [forecast, tiles] + obs_arrays + innov_arrays
    if final:
        in_specs.append(col_spec)
        operands.append(partial)
    grid_spec = pltpu.PrefetchScalarGridSpec(
        num_scalar_prefetch=1,
        grid=(block_count // group,),
        in_specs=in_specs,
        out_specs=col_spec,
        scratch_shapes=[
            pltpu.VMEM((rows, width), jnp.float32),
            pltpu.VMEM((rows, width), jnp.bfloat16),
        ],
    )
    out_type = jnp.bfloat16 if final else jnp.float32
    return pl.pallas_call(
        kernel,
        grid_spec=grid_spec,
        out_shape=jax.ShapeDtypeStruct((members, cells), out_type),
        cost_estimate=pl.CostEstimate(flops=4 * cells * members * width, transcendentals=0, bytes_accessed=8 * cells * members),
    )(code, *operands)


def solution(mesh):
    in_specs = (
        P("wide", None, "lon"),
        P(None, "wide", "lon"),
        P(None, None, "lon"),
        P(None, None, "lon"),
        P("lon", "wide", None),
        P("lon", "wide"),
        P("lon", "wide", None),
    )
    out_specs = P("wide", None, "lon")
    return jax.shard_map(body, mesh=mesh, in_specs=in_specs, out_specs=out_specs, check_vma=False)
```

```python
import math

import jax
import jax.numpy as jnp
from jax import lax
from jax.sharding import PartitionSpec as P
from jax.experimental import pallas as pl
from jax.experimental.pallas import tpu as pltpu

BLK = 128
HALO_BLK = 4


def padded_2(value, sides, width):
    for axis, dim in sides:
        size, length = (lax.axis_size(axis), value.shape[dim])
        up = [(i, (i + 1) % size) for i in range(size)]
        down = [(j, i) for i, j in up]
        last = lax.slice_in_dim(value, length - width, length, axis=dim)
        first = lax.slice_in_dim(value, 0, width, axis=dim)
        before = lax.ppermute(last, axis, up)
        after = lax.ppermute(first, axis, down)
        value = jnp.concatenate([before, value, after], axis=dim)
    return value


def column_halo(value, axis):
    size = lax.axis_size(axis)
    edges = jnp.stack([value[..., 0], value[..., -1]]).transpose(0, 2, 1)
    spread = jnp.broadcast_to(edges[None], (size,) + edges.shape)
    return lax.all_to_all(spread, axis, 0, 0, tiled=False)


def forecast_call(state, received, here):
    members, rows, cols = state.shape
    size = received.shape[0]
    position = jnp.reshape(here, (1,)).astype(jnp.int32)

    def kernel(pos_ref, x_ref, h_ref, o_ref):
        col = lax.broadcasted_iota(jnp.int32, (rows, cols), 1)
        row = lax.broadcasted_iota(jnp.int32, (rows, cols), 0)
        t = pos_ref[0]
        west_from = (t + size - 1) % size
        east_from = (t + 1) % size

        def one(m, carry):
            x = x_ref[m].astype(jnp.float32)
            west_col = h_ref[west_from, 1][:, m:m + 1].astype(jnp.float32)
            east_col = h_ref[east_from, 0][:, m:m + 1].astype(jnp.float32)
            east_n = jnp.where(col == cols - 1, east_col, pltpu.roll(x, cols - 1, 1))
            west_n = jnp.where(col == 0, west_col, pltpu.roll(x, 1, 1))
            north = jnp.where(row == rows - 1, 0.0, pltpu.roll(x, rows - 1, 0))
            south = jnp.where(row == 0, 0.0, pltpu.roll(x, 1, 0))
            spread = east_n + west_n + north + south - 4.0 * x
            o_ref[:, m, :] = (x + 0.2 * spread - 0.3 * (east_n - west_n)).astype(jnp.bfloat16)
            return carry

        for m in range(members):
            one(m, 0)

    grid_spec = pltpu.PrefetchScalarGridSpec(
        num_scalar_prefetch=1,
        grid=(1,),
        in_specs=[
            pl.BlockSpec(state.shape, lambda i, p: (0, 0, 0)),
            pl.BlockSpec(received.shape, lambda i, p: (0, 0, 0, 0)),
        ],
        out_specs=pl.BlockSpec((rows, members, cols), lambda i, p: (0, 0, 0)),
    )
    return pl.pallas_call(
        kernel, grid_spec=grid_spec, out_shape=jax.ShapeDtypeStruct((rows, members, cols), jnp.bfloat16)
    )(position, state, received)


def observe_region(state, index, weight):
    members, cells = state.shape
    count = index.shape[1]
    width = math.gcd(512, count)
    nblocks = count // width
    index_blocks = index.reshape(4, nblocks, width).transpose(1, 0, 2)
    weight_blocks = weight.reshape(4, nblocks, width).transpose(1, 0, 2)
    cell_ids = lax.broadcasted_iota(jnp.int32, (cells, width), 0)

    def observe_one_block(pieces):
        index_here, weight_here = pieces
        summed = jnp.zeros((members, width), jnp.float32)
        for k in range(4):
            selector = (cell_ids == index_here[k][None, :]).astype(jnp.bfloat16)
            picked = jnp.dot(state, selector, preferred_element_type=jnp.float32)
            summed = summed + weight_here[k][None, :] * picked
        return summed.astype(jnp.bfloat16)

    result = lax.map(observe_one_block, (index_blocks, weight_blocks))
    return result.transpose(1, 0, 2).reshape(members, count)


OBS_STEP = 256
def observe_dev_call(state, index, weight, extra=None):
    members, cells = state.shape
    count = index.shape[1]
    carry = extra is not None

    def kernel(f_ref, i_ref, w_ref, *rest):
        if carry:
            x_ref, o_ref = rest
        else:
            (o_ref,) = rest
        cell_ids = lax.broadcasted_iota(jnp.int32, (cells, OBS_STEP), 0)
        f = f_ref[...]
        summed = jnp.zeros((members, OBS_STEP), jnp.float32)
        for k in range(4):
            selector = (cell_ids == i_ref[k:k + 1, :]).astype(jnp.bfloat16)
            picked = jnp.dot(f, selector, preferred_element_type=jnp.float32)
            summed = summed + w_ref[k:k + 1, :] * picked
        ens = summed.astype(jnp.bfloat16).astype(jnp.float32)
        mean = jnp.sum(ens, axis=0, keepdims=True) / members
        dev = (ens - mean).astype(jnp.bfloat16)
        if carry:
            o_ref[0] = dev
            o_ref[1] = x_ref[...]
        else:
            o_ref[...] = dev

    in_specs = [
        pl.BlockSpec((members, cells), lambda j: (0, 0)),
        pl.BlockSpec((4, OBS_STEP), lambda j: (0, j)),
        pl.BlockSpec((4, OBS_STEP), lambda j: (0, j)),
    ]
    operands = [state, index, weight]
    if carry:
        in_specs.append(pl.BlockSpec((members, OBS_STEP), lambda j: (0, j)))
        operands.append(extra)
        out_spec = pl.BlockSpec((2, members, OBS_STEP), lambda j: (0, 0, j))
        out_shape = jax.ShapeDtypeStruct((2, members, count), jnp.bfloat16)
    else:
        out_spec = pl.BlockSpec((members, OBS_STEP), lambda j: (0, j))
        out_shape = jax.ShapeDtypeStruct((members, count), jnp.bfloat16)
    return pl.pallas_call(
        kernel,
        grid=(count // OBS_STEP,),
        in_specs=in_specs,
        out_specs=out_spec,
        out_shape=out_shape,
    )(*operands)


def anomaly_from_mean(state_values):
    centred = state_values.astype(jnp.float32)
    return (centred - jnp.mean(centred, axis=-2, keepdims=True)).astype(jnp.bfloat16)


def taper_tiles(classes, in_use, tile_width):
    row_ids = lax.broadcasted_iota(jnp.float32, (tile_width, tile_width), 0)
    col_ids = lax.broadcasted_iota(jnp.float32, (tile_width, tile_width), 1)
    offset = row_ids - col_ids
    length = 8.0 * jnp.exp2(classes.astype(jnp.float32))
    scaled = offset / length[..., None, None]
    return in_use[..., None, None] / (1.0 + scaled * scaled)


def body(background_ensemble, innov, obs_index, obs_weight, obs_list, tile_count, taper_class):
    received = column_halo(background_ensemble, "lon")
    prediction_increment = forecast_call(background_ensemble, received, lax.axis_index("lon"))
    whole_parallel_set, ensemble_lines_here, patch_meridian_lines = prediction_increment.shape
    members = innov.shape[0]
    band_rows = innov.shape[1]
    patch_gridpoints = band_rows * patch_meridian_lines
    region = lax.all_to_all(prediction_increment, "wide", split_axis=0, concat_axis=1, tiled=True)
    region_state = region.transpose(1, 0, 2).reshape(members, patch_gridpoints)
    first_row = lax.axis_index("wide") * band_rows
    local_index = lax.dynamic_slice_in_dim(obs_index, first_row, band_rows, 1).reshape(
        4, patch_gridpoints
    )
    local_index = local_index - first_row * patch_meridian_lines
    local_weight = lax.dynamic_slice_in_dim(obs_weight, first_row, band_rows, 1).reshape(
        4, patch_gridpoints
    )
    halo = HALO_BLK * BLK
    innov_flat = innov.reshape(members, patch_gridpoints)
    lon_size = lax.axis_size("lon")
    up = [(i, (i + 1) % lon_size) for i in range(lon_size)]
    down = [(j, i) for i, j in up]
    last_edge = observe_dev_call(
        region_state, local_index[:, -halo:], local_weight[:, -halo:], innov_flat[:, -halo:]
    )
    west = lax.ppermute(last_edge, "lon", up)
    first_edge = observe_dev_call(
        region_state, local_index[:, :halo], local_weight[:, :halo], innov_flat[:, :halo]
    )
    east = lax.ppermute(first_edge, "lon", down)
    middle_dev = observe_dev_call(region_state, local_index[:, halo:-halo], local_weight[:, halo:-halo])
    obs_dev = jnp.concatenate([first_edge[0], middle_dev, last_edge[0]], axis=1)
    halo_blocks = halo // BLK
    block_count = patch_gridpoints // BLK
    candidate_count = block_count + 2 * halo_blocks
    code = block_codes(obs_list[0], tile_count[0], taper_class[0], candidate_count)
    own_code = code[:, halo_blocks:halo_blocks + block_count]
    halo_code = jnp.concatenate([code[:, :halo_blocks], code[:, halo_blocks + block_count:]], axis=1)
    tiles = taper_table(BLK, members)
    partial = update_call(
        own_code.reshape(-1),
        region_state,
        None,
        [(first_edge, 0), (middle_dev, None), (last_edge, 0)],
        [(innov_flat, None)],
        tiles,
        block_count,
        block_count,
        group=8,
    )
    result = update_call(
        halo_code.reshape(-1),
        region_state,
        partial,
        [(west, 0), (east, 0)],
        [(west, 1), (east, 1)],
        tiles,
        block_count,
        2 * halo_blocks,
        group=8,
    )
    return lax.all_to_all(
        result.reshape(members, band_rows, patch_meridian_lines),
        "wide",
        split_axis=0,
        concat_axis=1,
        tiled=True,
    )


def block_codes(lists, counts, classes, candidate_count):
    zero_code = 4
    entries = jnp.arange(lists.shape[1], dtype=jnp.int32)
    value = jnp.where(entries[None, :] < counts[:, None], classes, zero_code)
    hit = lists[:, :, None] == jnp.arange(candidate_count, dtype=jnp.int32)[None, None, :]
    code = zero_code + jnp.sum(jnp.where(hit, value[:, :, None] - zero_code, 0), axis=1)
    return jnp.clip(code, 0, zero_code).astype(jnp.int32)


def taper_table(tile_width, members):
    row_ids = lax.broadcasted_iota(jnp.float32, (tile_width, tile_width), 0)
    col_ids = lax.broadcasted_iota(jnp.float32, (tile_width, tile_width), 1)
    offset = row_ids - col_ids
    length = 8.0 * jnp.exp2(jnp.arange(4, dtype=jnp.float32))
    scaled = offset[None] / length[:, None, None]
    tiles = (1.0 / (1.0 + scaled * scaled)) / (members - 1.0)
    return jnp.concatenate([tiles, jnp.zeros((1, tile_width, tile_width), jnp.float32)], axis=0)


GROUP = 4


def piece_spec(array):
    if array.ndim == 3:
        return pl.BlockSpec(array.shape, lambda g, code: (0, 0, 0))
    return pl.BlockSpec(array.shape, lambda g, code: (0, 0))


def piece_value(ref, pick):
    return ref[...] if pick is None else ref[pick]


def update_call(code, forecast, partial, obs_pieces, innov_pieces, tiles, block_count, candidate_count, group=GROUP):
    members, cells = forecast.shape
    rows = group * BLK
    width = candidate_count * BLK
    final = partial is not None
    obs_arrays = [a for a, _ in obs_pieces]
    innov_arrays = [a for a, _ in innov_pieces]
    n_obs = len(obs_pieces)
    n_innov = len(innov_pieces)

    def kernel(code_ref, f_ref, taper_ref, *rest):
        obs_refs = rest[:n_obs]
        innov_refs = rest[n_obs:n_obs + n_innov]
        rest = rest[n_obs + n_innov:]
        if final:
            part_ref, out_ref, cov_scr, tap_scr = rest
        else:
            out_ref, cov_scr, tap_scr = rest
        g = pl.program_id(0)
        forecast_block = f_ref[...].astype(jnp.float32)
        mean = jnp.sum(forecast_block, axis=0, keepdims=True) / members
        state = (forecast_block - mean).astype(jnp.bfloat16)
        offset = 0
        for ref, (_, pick) in zip(obs_refs, obs_pieces):
            piece = piece_value(ref, pick)
            span = piece.shape[1]
            cov_scr[:, offset:offset + span] = lax.dot_general(
                state, piece, (((0,), (0,)), ((), ())), preferred_element_type=jnp.float32
            )
            offset += span
        for sl in range(group):
            s = g * group + sl
            for b in range(candidate_count):
                c = code_ref[s * candidate_count + b]
                tile = cov_scr[sl * BLK:(sl + 1) * BLK, b * BLK:(b + 1) * BLK] * taper_ref[c]
                tap_scr[sl * BLK:(sl + 1) * BLK, b * BLK:(b + 1) * BLK] = tile.astype(jnp.bfloat16)
        change = None
        offset = 0
        for ref, (_, pick) in zip(innov_refs, innov_pieces):
            piece = piece_value(ref, pick)
            span = piece.shape[1]
            term = lax.dot_general(
                piece, tap_scr[:, offset:offset + span], (((1,), (1,)), ((), ())),
                preferred_element_type=jnp.float32,
            )
            change = term if change is None else change + term
            offset += span
        if final:
            total = part_ref[...] + change
            out_ref[...] = (forecast_block + total).astype(jnp.bfloat16)
        else:
            out_ref[...] = change

    col_spec = pl.BlockSpec((members, rows), lambda g, code: (0, g))
    in_specs = [col_spec, pl.BlockSpec(tiles.shape, lambda g, code: (0, 0, 0))]
    in_specs += [piece_spec(a) for a in obs_arrays] + [piece_spec(a) for a in innov_arrays]
    operands = [forecast, tiles] + obs_arrays + innov_arrays
    if final:
        in_specs.append(col_spec)
        operands.append(partial)
    grid_spec = pltpu.PrefetchScalarGridSpec(
        num_scalar_prefetch=1,
        grid=(block_count // group,),
        in_specs=in_specs,
        out_specs=col_spec,
        scratch_shapes=[
            pltpu.VMEM((rows, width), jnp.float32),
            pltpu.VMEM((rows, width), jnp.bfloat16),
        ],
    )
    out_type = jnp.bfloat16 if final else jnp.float32
    return pl.pallas_call(
        kernel,
        grid_spec=grid_spec,
        out_shape=jax.ShapeDtypeStruct((members, cells), out_type),
        cost_estimate=pl.CostEstimate(flops=4 * cells * members * width, transcendentals=0, bytes_accessed=8 * cells * members),
    )(code, *operands)


def solution(mesh):
    in_specs = (
        P("wide", None, "lon"),
        P(None, "wide", "lon"),
        P(None, None, "lon"),
        P(None, None, "lon"),
        P("lon", "wide", None),
        P("lon", "wide"),
        P("lon", "wide", None),
    )
    out_specs = P("wide", None, "lon")
    return jax.shard_map(body, mesh=mesh, in_specs=in_specs, out_specs=out_specs, check_vma=False)
```

```python
import math

import jax
import jax.numpy as jnp
from jax import lax
from jax.sharding import PartitionSpec as P
from jax.experimental import pallas as pl
from jax.experimental.pallas import tpu as pltpu

BLK = 128
HALO_BLK = 4


def padded_2(value, sides, width):
    for axis, dim in sides:
        size, length = (lax.axis_size(axis), value.shape[dim])
        up = [(i, (i + 1) % size) for i in range(size)]
        down = [(j, i) for i, j in up]
        last = lax.slice_in_dim(value, length - width, length, axis=dim)
        first = lax.slice_in_dim(value, 0, width, axis=dim)
        before = lax.ppermute(last, axis, up)
        after = lax.ppermute(first, axis, down)
        value = jnp.concatenate([before, value, after], axis=dim)
    return value


def column_halo(value, axis):
    size = lax.axis_size(axis)
    edges = jnp.stack([value[..., 0], value[..., -1]]).transpose(0, 2, 1)
    flat = edges.reshape(2, -1)
    spread = jnp.broadcast_to(flat[None], (size,) + flat.shape)
    got = lax.all_to_all(spread, axis, 0, 0, tiled=False)
    return got.reshape((size,) + edges.shape)


def forecast_call(state, received, here):
    members, rows, cols = state.shape
    size = received.shape[0]
    position = jnp.reshape(here, (1,)).astype(jnp.int32)

    def kernel(pos_ref, x_ref, h_ref, o_ref):
        col = lax.broadcasted_iota(jnp.int32, (rows, cols), 1)
        row = lax.broadcasted_iota(jnp.int32, (rows, cols), 0)
        t = pos_ref[0]
        west_from = (t + size - 1) % size
        east_from = (t + 1) % size

        def one(m, carry):
            x = x_ref[m].astype(jnp.float32)
            west_col = h_ref[west_from, 1][:, m:m + 1].astype(jnp.float32)
            east_col = h_ref[east_from, 0][:, m:m + 1].astype(jnp.float32)
            east_n = jnp.where(col == cols - 1, east_col, pltpu.roll(x, cols - 1, 1))
            west_n = jnp.where(col == 0, west_col, pltpu.roll(x, 1, 1))
            north = jnp.where(row == rows - 1, 0.0, pltpu.roll(x, rows - 1, 0))
            south = jnp.where(row == 0, 0.0, pltpu.roll(x, 1, 0))
            spread = east_n + west_n + north + south - 4.0 * x
            o_ref[:, m, :] = (x + 0.2 * spread - 0.3 * (east_n - west_n)).astype(jnp.bfloat16)
            return carry

        for m in range(members):
            one(m, 0)

    grid_spec = pltpu.PrefetchScalarGridSpec(
        num_scalar_prefetch=1,
        grid=(1,),
        in_specs=[
            pl.BlockSpec(state.shape, lambda i, p: (0, 0, 0)),
            pl.BlockSpec(received.shape, lambda i, p: (0, 0, 0, 0)),
        ],
        out_specs=pl.BlockSpec((rows, members, cols), lambda i, p: (0, 0, 0)),
    )
    return pl.pallas_call(
        kernel, grid_spec=grid_spec, out_shape=jax.ShapeDtypeStruct((rows, members, cols), jnp.bfloat16)
    )(position, state, received)


def observe_region(state, index, weight):
    members, cells = state.shape
    count = index.shape[1]
    width = math.gcd(512, count)
    nblocks = count // width
    index_blocks = index.reshape(4, nblocks, width).transpose(1, 0, 2)
    weight_blocks = weight.reshape(4, nblocks, width).transpose(1, 0, 2)
    cell_ids = lax.broadcasted_iota(jnp.int32, (cells, width), 0)

    def observe_one_block(pieces):
        index_here, weight_here = pieces
        summed = jnp.zeros((members, width), jnp.float32)
        for k in range(4):
            selector = (cell_ids == index_here[k][None, :]).astype(jnp.bfloat16)
            picked = jnp.dot(state, selector, preferred_element_type=jnp.float32)
            summed = summed + weight_here[k][None, :] * picked
        return summed.astype(jnp.bfloat16)

    result = lax.map(observe_one_block, (index_blocks, weight_blocks))
    return result.transpose(1, 0, 2).reshape(members, count)


OBS_STEP = 256
def observe_dev_call(state, index, weight, extra=None):
    members, cells = state.shape
    count = index.shape[1]
    carry = extra is not None

    def kernel(f_ref, i_ref, w_ref, *rest):
        if carry:
            x_ref, o_ref = rest
        else:
            (o_ref,) = rest
        cell_ids = lax.broadcasted_iota(jnp.int32, (cells, OBS_STEP), 0)
        f = f_ref[...]
        summed = jnp.zeros((members, OBS_STEP), jnp.float32)
        for k in range(4):
            selector = (cell_ids == i_ref[k:k + 1, :]).astype(jnp.bfloat16)
            picked = jnp.dot(f, selector, preferred_element_type=jnp.float32)
            summed = summed + w_ref[k:k + 1, :] * picked
        ens = summed.astype(jnp.bfloat16).astype(jnp.float32)
        mean = jnp.sum(ens, axis=0, keepdims=True) / members
        dev = (ens - mean).astype(jnp.bfloat16)
        if carry:
            o_ref[0] = dev
            o_ref[1] = x_ref[...]
        else:
            o_ref[...] = dev

    in_specs = [
        pl.BlockSpec((members, cells), lambda j: (0, 0)),
        pl.BlockSpec((4, OBS_STEP), lambda j: (0, j)),
        pl.BlockSpec((4, OBS_STEP), lambda j: (0, j)),
    ]
    operands = [state, index, weight]
    if carry:
        in_specs.append(pl.BlockSpec((members, OBS_STEP), lambda j: (0, j)))
        operands.append(extra)
        out_spec = pl.BlockSpec((2, members, OBS_STEP), lambda j: (0, 0, j))
        out_shape = jax.ShapeDtypeStruct((2, members, count), jnp.bfloat16)
    else:
        out_spec = pl.BlockSpec((members, OBS_STEP), lambda j: (0, j))
        out_shape = jax.ShapeDtypeStruct((members, count), jnp.bfloat16)
    return pl.pallas_call(
        kernel,
        grid=(count // OBS_STEP,),
        in_specs=in_specs,
        out_specs=out_spec,
        out_shape=out_shape,
    )(*operands)


def anomaly_from_mean(state_values):
    centred = state_values.astype(jnp.float32)
    return (centred - jnp.mean(centred, axis=-2, keepdims=True)).astype(jnp.bfloat16)


def taper_tiles(classes, in_use, tile_width):
    row_ids = lax.broadcasted_iota(jnp.float32, (tile_width, tile_width), 0)
    col_ids = lax.broadcasted_iota(jnp.float32, (tile_width, tile_width), 1)
    offset = row_ids - col_ids
    length = 8.0 * jnp.exp2(classes.astype(jnp.float32))
    scaled = offset / length[..., None, None]
    return in_use[..., None, None] / (1.0 + scaled * scaled)


def body(background_ensemble, innov, obs_index, obs_weight, obs_list, tile_count, taper_class):
    received = column_halo(background_ensemble, "lon")
    prediction_increment = forecast_call(background_ensemble, received, lax.axis_index("lon"))
    whole_parallel_set, ensemble_lines_here, patch_meridian_lines = prediction_increment.shape
    members = innov.shape[0]
    band_rows = innov.shape[1]
    patch_gridpoints = band_rows * patch_meridian_lines
    region = lax.all_to_all(prediction_increment, "wide", split_axis=0, concat_axis=1, tiled=True)
    region_state = region.transpose(1, 0, 2).reshape(members, patch_gridpoints)
    first_row = lax.axis_index("wide") * band_rows
    local_index = lax.dynamic_slice_in_dim(obs_index, first_row, band_rows, 1).reshape(
        4, patch_gridpoints
    )
    local_index = local_index - first_row * patch_meridian_lines
    local_weight = lax.dynamic_slice_in_dim(obs_weight, first_row, band_rows, 1).reshape(
        4, patch_gridpoints
    )
    halo = HALO_BLK * BLK
    innov_flat = innov.reshape(members, patch_gridpoints)
    lon_size = lax.axis_size("lon")
    up = [(i, (i + 1) % lon_size) for i in range(lon_size)]
    down = [(j, i) for i, j in up]
    last_edge = observe_dev_call(
        region_state, local_index[:, -halo:], local_weight[:, -halo:], innov_flat[:, -halo:]
    )
    west = lax.ppermute(last_edge, "lon", up)
    first_edge = observe_dev_call(
        region_state, local_index[:, :halo], local_weight[:, :halo], innov_flat[:, :halo]
    )
    east = lax.ppermute(first_edge, "lon", down)
    middle_dev = observe_dev_call(region_state, local_index[:, halo:-halo], local_weight[:, halo:-halo])
    obs_dev = jnp.concatenate([first_edge[0], middle_dev, last_edge[0]], axis=1)
    halo_blocks = halo // BLK
    block_count = patch_gridpoints // BLK
    candidate_count = block_count + 2 * halo_blocks
    code = block_codes(obs_list[0], tile_count[0], taper_class[0], candidate_count)
    own_code = code[:, halo_blocks:halo_blocks + block_count]
    halo_code = jnp.concatenate([code[:, :halo_blocks], code[:, halo_blocks + block_count:]], axis=1)
    tiles = taper_table(BLK, members)
    partial = update_call(
        own_code.reshape(-1),
        region_state,
        None,
        [(first_edge, 0), (middle_dev, None), (last_edge, 0)],
        [(innov_flat, None)],
        tiles,
        block_count,
        block_count,
        group=8,
    )
    result = update_call(
        halo_code.reshape(-1),
        region_state,
        partial,
        [(west, 0), (east, 0)],
        [(west, 1), (east, 1)],
        tiles,
        block_count,
        2 * halo_blocks,
        group=8,
    )
    return lax.all_to_all(
        result.reshape(members, band_rows, patch_meridian_lines),
        "wide",
        split_axis=0,
        concat_axis=1,
        tiled=True,
    )


def block_codes(lists, counts, classes, candidate_count):
    zero_code = 4
    entries = jnp.arange(lists.shape[1], dtype=jnp.int32)
    value = jnp.where(entries[None, :] < counts[:, None], classes, zero_code)
    hit = lists[:, :, None] == jnp.arange(candidate_count, dtype=jnp.int32)[None, None, :]
    code = zero_code + jnp.sum(jnp.where(hit, value[:, :, None] - zero_code, 0), axis=1)
    return jnp.clip(code, 0, zero_code).astype(jnp.int32)


def taper_table(tile_width, members):
    row_ids = lax.broadcasted_iota(jnp.float32, (tile_width, tile_width), 0)
    col_ids = lax.broadcasted_iota(jnp.float32, (tile_width, tile_width), 1)
    offset = row_ids - col_ids
    length = 8.0 * jnp.exp2(jnp.arange(4, dtype=jnp.float32))
    scaled = offset[None] / length[:, None, None]
    tiles = (1.0 / (1.0 + scaled * scaled)) / (members - 1.0)
    return jnp.concatenate([tiles, jnp.zeros((1, tile_width, tile_width), jnp.float32)], axis=0)


GROUP = 4


def piece_spec(array):
    if array.ndim == 3:
        return pl.BlockSpec(array.shape, lambda g, code: (0, 0, 0))
    return pl.BlockSpec(array.shape, lambda g, code: (0, 0))


def piece_value(ref, pick):
    return ref[...] if pick is None else ref[pick]


def update_call(code, forecast, partial, obs_pieces, innov_pieces, tiles, block_count, candidate_count, group=GROUP):
    members, cells = forecast.shape
    rows = group * BLK
    width = candidate_count * BLK
    final = partial is not None
    obs_arrays = [a for a, _ in obs_pieces]
    innov_arrays = [a for a, _ in innov_pieces]
    n_obs = len(obs_pieces)
    n_innov = len(innov_pieces)

    def kernel(code_ref, f_ref, taper_ref, *rest):
        obs_refs = rest[:n_obs]
        innov_refs = rest[n_obs:n_obs + n_innov]
        rest = rest[n_obs + n_innov:]
        if final:
            part_ref, out_ref, cov_scr, tap_scr = rest
        else:
            out_ref, cov_scr, tap_scr = rest
        g = pl.program_id(0)
        forecast_block = f_ref[...].astype(jnp.float32)
        mean = jnp.sum(forecast_block, axis=0, keepdims=True) / members
        state = (forecast_block - mean).astype(jnp.bfloat16)
        offset = 0
        for ref, (_, pick) in zip(obs_refs, obs_pieces):
            piece = piece_value(ref, pick)
            span = piece.shape[1]
            cov_scr[:, offset:offset + span] = lax.dot_general(
                state, piece, (((0,), (0,)), ((), ())), preferred_element_type=jnp.float32
            )
            offset += span
        for sl in range(group):
            s = g * group + sl
            for b in range(candidate_count):
                c = code_ref[s * candidate_count + b]
                tile = cov_scr[sl * BLK:(sl + 1) * BLK, b * BLK:(b + 1) * BLK] * taper_ref[c]
                tap_scr[sl * BLK:(sl + 1) * BLK, b * BLK:(b + 1) * BLK] = tile.astype(jnp.bfloat16)
        change = None
        offset = 0
        for ref, (_, pick) in zip(innov_refs, innov_pieces):
            piece = piece_value(ref, pick)
            span = piece.shape[1]
            term = lax.dot_general(
                piece, tap_scr[:, offset:offset + span], (((1,), (1,)), ((), ())),
                preferred_element_type=jnp.float32,
            )
            change = term if change is None else change + term
            offset += span
        if final:
            total = part_ref[...] + change
            out_ref[...] = (forecast_block + total).astype(jnp.bfloat16)
        else:
            out_ref[...] = change

    col_spec = pl.BlockSpec((members, rows), lambda g, code: (0, g))
    in_specs = [col_spec, pl.BlockSpec(tiles.shape, lambda g, code: (0, 0, 0))]
    in_specs += [piece_spec(a) for a in obs_arrays] + [piece_spec(a) for a in innov_arrays]
    operands = [forecast, tiles] + obs_arrays + innov_arrays
    if final:
        in_specs.append(col_spec)
        operands.append(partial)
    grid_spec = pltpu.PrefetchScalarGridSpec(
        num_scalar_prefetch=1,
        grid=(block_count // group,),
        in_specs=in_specs,
        out_specs=col_spec,
        scratch_shapes=[
            pltpu.VMEM((rows, width), jnp.float32),
            pltpu.VMEM((rows, width), jnp.bfloat16),
        ],
    )
    out_type = jnp.bfloat16 if final else jnp.float32
    return pl.pallas_call(
        kernel,
        grid_spec=grid_spec,
        out_shape=jax.ShapeDtypeStruct((members, cells), out_type),
        cost_estimate=pl.CostEstimate(flops=4 * cells * members * width, transcendentals=0, bytes_accessed=8 * cells * members),
    )(code, *operands)


def solution(mesh):
    in_specs = (
        P("wide", None, "lon"),
        P(None, "wide", "lon"),
        P(None, None, "lon"),
        P(None, None, "lon"),
        P("lon", "wide", None),
        P("lon", "wide"),
        P("lon", "wide", None),
    )
    out_specs = P("wide", None, "lon")
    return jax.shard_map(body, mesh=mesh, in_specs=in_specs, out_specs=out_specs, check_vma=False)
```

```python
import math

import jax
import jax.numpy as jnp
from jax import lax
from jax.sharding import PartitionSpec as P
from jax.experimental import pallas as pl
from jax.experimental.pallas import tpu as pltpu

BLK = 128
HALO_BLK = 4


def padded_2(value, sides, width):
    for axis, dim in sides:
        size, length = (lax.axis_size(axis), value.shape[dim])
        up = [(i, (i + 1) % size) for i in range(size)]
        down = [(j, i) for i, j in up]
        last = lax.slice_in_dim(value, length - width, length, axis=dim)
        first = lax.slice_in_dim(value, 0, width, axis=dim)
        before = lax.ppermute(last, axis, up)
        after = lax.ppermute(first, axis, down)
        value = jnp.concatenate([before, value, after], axis=dim)
    return value


def column_halo(value, axis):
    size = lax.axis_size(axis)
    edges = jnp.stack([value[..., 0], value[..., -1]]).transpose(0, 2, 1)
    spread = jnp.broadcast_to(edges[None], (size,) + edges.shape)
    return lax.all_to_all(spread, axis, 0, 0, tiled=False)


def forecast_call(state, received, here):
    members, rows, cols = state.shape
    size = received.shape[0]
    position = jnp.reshape(here, (1,)).astype(jnp.int32)

    def kernel(pos_ref, x_ref, h_ref, o_ref):
        col = lax.broadcasted_iota(jnp.int32, (rows, cols), 1)
        row = lax.broadcasted_iota(jnp.int32, (rows, cols), 0)
        t = pos_ref[0]
        west_from = (t + size - 1) % size
        east_from = (t + 1) % size

        def one(m, carry):
            x = x_ref[m].astype(jnp.float32)
            west_col = h_ref[west_from, 1][:, m:m + 1].astype(jnp.float32)
            east_col = h_ref[east_from, 0][:, m:m + 1].astype(jnp.float32)
            east_n = jnp.where(col == cols - 1, east_col, pltpu.roll(x, cols - 1, 1))
            west_n = jnp.where(col == 0, west_col, pltpu.roll(x, 1, 1))
            north = jnp.where(row == rows - 1, 0.0, pltpu.roll(x, rows - 1, 0))
            south = jnp.where(row == 0, 0.0, pltpu.roll(x, 1, 0))
            spread = east_n + west_n + north + south - 4.0 * x
            o_ref[:, m, :] = (x + 0.2 * spread - 0.3 * (east_n - west_n)).astype(jnp.bfloat16)
            return carry

        for m in range(members):
            one(m, 0)

    grid_spec = pltpu.PrefetchScalarGridSpec(
        num_scalar_prefetch=1,
        grid=(1,),
        in_specs=[
            pl.BlockSpec(state.shape, lambda i, p: (0, 0, 0)),
            pl.BlockSpec(received.shape, lambda i, p: (0, 0, 0, 0)),
        ],
        out_specs=pl.BlockSpec((rows, members, cols), lambda i, p: (0, 0, 0)),
    )
    return pl.pallas_call(
        kernel, grid_spec=grid_spec, out_shape=jax.ShapeDtypeStruct((rows, members, cols), jnp.bfloat16)
    )(position, state, received)


def observe_region(state, index, weight):
    members, cells = state.shape
    count = index.shape[1]
    width = math.gcd(512, count)
    nblocks = count // width
    index_blocks = index.reshape(4, nblocks, width).transpose(1, 0, 2)
    weight_blocks = weight.reshape(4, nblocks, width).transpose(1, 0, 2)
    cell_ids = lax.broadcasted_iota(jnp.int32, (cells, width), 0)

    def observe_one_block(pieces):
        index_here, weight_here = pieces
        summed = jnp.zeros((members, width), jnp.float32)
        for k in range(4):
            selector = (cell_ids == index_here[k][None, :]).astype(jnp.bfloat16)
            picked = jnp.dot(state, selector, preferred_element_type=jnp.float32)
            summed = summed + weight_here[k][None, :] * picked
        return summed.astype(jnp.bfloat16)

    result = lax.map(observe_one_block, (index_blocks, weight_blocks))
    return result.transpose(1, 0, 2).reshape(members, count)


OBS_STEP = 512
def observe_dev_call(state, index, weight, extra=None):
    members, cells = state.shape
    count = index.shape[1]
    carry = extra is not None

    def kernel(f_ref, i_ref, w_ref, *rest):
        if carry:
            x_ref, o_ref = rest
        else:
            (o_ref,) = rest
        cell_ids = lax.broadcasted_iota(jnp.int32, (cells, OBS_STEP), 0)
        f = f_ref[...]
        summed = jnp.zeros((members, OBS_STEP), jnp.float32)
        for k in range(4):
            selector = (cell_ids == i_ref[k:k + 1, :]).astype(jnp.bfloat16)
            picked = jnp.dot(f, selector, preferred_element_type=jnp.float32)
            summed = summed + w_ref[k:k + 1, :] * picked
        ens = summed.astype(jnp.bfloat16).astype(jnp.float32)
        mean = jnp.sum(ens, axis=0, keepdims=True) / members
        dev = (ens - mean).astype(jnp.bfloat16)
        if carry:
            o_ref[0] = dev
            o_ref[1] = x_ref[...]
        else:
            o_ref[...] = dev

    in_specs = [
        pl.BlockSpec((members, cells), lambda j: (0, 0)),
        pl.BlockSpec((4, OBS_STEP), lambda j: (0, j)),
        pl.BlockSpec((4, OBS_STEP), lambda j: (0, j)),
    ]
    operands = [state, index, weight]
    if carry:
        in_specs.append(pl.BlockSpec((members, OBS_STEP), lambda j: (0, j)))
        operands.append(extra)
        out_spec = pl.BlockSpec((2, members, OBS_STEP), lambda j: (0, 0, j))
        out_shape = jax.ShapeDtypeStruct((2, members, count), jnp.bfloat16)
    else:
        out_spec = pl.BlockSpec((members, OBS_STEP), lambda j: (0, j))
        out_shape = jax.ShapeDtypeStruct((members, count), jnp.bfloat16)
    return pl.pallas_call(
        kernel,
        grid=(count // OBS_STEP,),
        in_specs=in_specs,
        out_specs=out_spec,
        out_shape=out_shape,
    )(*operands)


def anomaly_from_mean(state_values):
    centred = state_values.astype(jnp.float32)
    return (centred - jnp.mean(centred, axis=-2, keepdims=True)).astype(jnp.bfloat16)


def taper_tiles(classes, in_use, tile_width):
    row_ids = lax.broadcasted_iota(jnp.float32, (tile_width, tile_width), 0)
    col_ids = lax.broadcasted_iota(jnp.float32, (tile_width, tile_width), 1)
    offset = row_ids - col_ids
    length = 8.0 * jnp.exp2(classes.astype(jnp.float32))
    scaled = offset / length[..., None, None]
    return in_use[..., None, None] / (1.0 + scaled * scaled)


def body(background_ensemble, innov, obs_index, obs_weight, obs_list, tile_count, taper_class):
    received = column_halo(background_ensemble, "lon")
    prediction_increment = forecast_call(background_ensemble, received, lax.axis_index("lon"))
    whole_parallel_set, ensemble_lines_here, patch_meridian_lines = prediction_increment.shape
    members = innov.shape[0]
    band_rows = innov.shape[1]
    patch_gridpoints = band_rows * patch_meridian_lines
    region = lax.all_to_all(prediction_increment, "wide", split_axis=0, concat_axis=1, tiled=True)
    region_state = region.transpose(1, 0, 2).reshape(members, patch_gridpoints)
    first_row = lax.axis_index("wide") * band_rows
    local_index = lax.dynamic_slice_in_dim(obs_index, first_row, band_rows, 1).reshape(
        4, patch_gridpoints
    )
    local_index = local_index - first_row * patch_meridian_lines
    local_weight = lax.dynamic_slice_in_dim(obs_weight, first_row, band_rows, 1).reshape(
        4, patch_gridpoints
    )
    halo = HALO_BLK * BLK
    innov_flat = innov.reshape(members, patch_gridpoints)
    lon_size = lax.axis_size("lon")
    up = [(i, (i + 1) % lon_size) for i in range(lon_size)]
    down = [(j, i) for i, j in up]
    last_edge = observe_dev_call(
        region_state, local_index[:, -halo:], local_weight[:, -halo:], innov_flat[:, -halo:]
    )
    west = lax.ppermute(last_edge, "lon", up)
    first_edge = observe_dev_call(
        region_state, local_index[:, :halo], local_weight[:, :halo], innov_flat[:, :halo]
    )
    east = lax.ppermute(first_edge, "lon", down)
    middle_dev = observe_dev_call(region_state, local_index[:, halo:-halo], local_weight[:, halo:-halo])
    obs_dev = jnp.concatenate([first_edge[0], middle_dev, last_edge[0]], axis=1)
    halo_blocks = halo // BLK
    block_count = patch_gridpoints // BLK
    candidate_count = block_count + 2 * halo_blocks
    code = block_codes(obs_list[0], tile_count[0], taper_class[0], candidate_count)
    own_code = code[:, halo_blocks:halo_blocks + block_count]
    halo_code = jnp.concatenate([code[:, :halo_blocks], code[:, halo_blocks + block_count:]], axis=1)
    tiles = taper_table(BLK, members)
    partial = update_call(
        own_code.reshape(-1),
        region_state,
        None,
        [(first_edge, 0), (middle_dev, None), (last_edge, 0)],
        [(innov_flat, None)],
        tiles,
        block_count,
        block_count,
        group=8,
    )
    result = update_call(
        halo_code.reshape(-1),
        region_state,
        partial,
        [(west, 0), (east, 0)],
        [(west, 1), (east, 1)],
        tiles,
        block_count,
        2 * halo_blocks,
        group=16,
    )
    return lax.all_to_all(
        result.reshape(members, band_rows, patch_meridian_lines),
        "wide",
        split_axis=0,
        concat_axis=1,
        tiled=True,
    )


def block_codes(lists, counts, classes, candidate_count):
    zero_code = 4
    entries = jnp.arange(lists.shape[1], dtype=jnp.int32)
    value = jnp.where(entries[None, :] < counts[:, None], classes, zero_code)
    hit = lists[:, :, None] == jnp.arange(candidate_count, dtype=jnp.int32)[None, None, :]
    code = zero_code + jnp.sum(jnp.where(hit, value[:, :, None] - zero_code, 0), axis=1)
    return jnp.clip(code, 0, zero_code).astype(jnp.int32)


def taper_table(tile_width, members):
    row_ids = lax.broadcasted_iota(jnp.float32, (tile_width, tile_width), 0)
    col_ids = lax.broadcasted_iota(jnp.float32, (tile_width, tile_width), 1)
    offset = row_ids - col_ids
    length = 8.0 * jnp.exp2(jnp.arange(4, dtype=jnp.float32))
    scaled = offset[None] / length[:, None, None]
    tiles = (1.0 / (1.0 + scaled * scaled)) / (members - 1.0)
    return jnp.concatenate([tiles, jnp.zeros((1, tile_width, tile_width), jnp.float32)], axis=0)


GROUP = 4


def piece_spec(array):
    if array.ndim == 3:
        return pl.BlockSpec(array.shape, lambda g, code: (0, 0, 0))
    return pl.BlockSpec(array.shape, lambda g, code: (0, 0))


def piece_value(ref, pick):
    return ref[...] if pick is None else ref[pick]


def update_call(code, forecast, partial, obs_pieces, innov_pieces, tiles, block_count, candidate_count, group=GROUP):
    members, cells = forecast.shape
    rows = group * BLK
    width = candidate_count * BLK
    final = partial is not None
    obs_arrays = [a for a, _ in obs_pieces]
    innov_arrays = [a for a, _ in innov_pieces]
    n_obs = len(obs_pieces)
    n_innov = len(innov_pieces)

    def kernel(code_ref, f_ref, taper_ref, *rest):
        obs_refs = rest[:n_obs]
        innov_refs = rest[n_obs:n_obs + n_innov]
        rest = rest[n_obs + n_innov:]
        if final:
            part_ref, out_ref, cov_scr, tap_scr = rest
        else:
            out_ref, cov_scr, tap_scr = rest
        g = pl.program_id(0)
        forecast_block = f_ref[...].astype(jnp.float32)
        mean = jnp.sum(forecast_block, axis=0, keepdims=True) / members
        state = (forecast_block - mean).astype(jnp.bfloat16)
        offset = 0
        for ref, (_, pick) in zip(obs_refs, obs_pieces):
            piece = piece_value(ref, pick)
            span = piece.shape[1]
            cov_scr[:, offset:offset + span] = lax.dot_general(
                state, piece, (((0,), (0,)), ((), ())), preferred_element_type=jnp.float32
            )
            offset += span
        for sl in range(group):
            s = g * group + sl
            for b in range(candidate_count):
                c = code_ref[s * candidate_count + b]
                tile = cov_scr[sl * BLK:(sl + 1) * BLK, b * BLK:(b + 1) * BLK] * taper_ref[c]
                tap_scr[sl * BLK:(sl + 1) * BLK, b * BLK:(b + 1) * BLK] = tile.astype(jnp.bfloat16)
        change = None
        offset = 0
        for ref, (_, pick) in zip(innov_refs, innov_pieces):
            piece = piece_value(ref, pick)
            span = piece.shape[1]
            term = lax.dot_general(
                piece, tap_scr[:, offset:offset + span], (((1,), (1,)), ((), ())),
                preferred_element_type=jnp.float32,
            )
            change = term if change is None else change + term
            offset += span
        if final:
            total = part_ref[...] + change
            out_ref[...] = (forecast_block + total).astype(jnp.bfloat16)
        else:
            out_ref[...] = change

    col_spec = pl.BlockSpec((members, rows), lambda g, code: (0, g))
    in_specs = [col_spec, pl.BlockSpec(tiles.shape, lambda g, code: (0, 0, 0))]
    in_specs += [piece_spec(a) for a in obs_arrays] + [piece_spec(a) for a in innov_arrays]
    operands = [forecast, tiles] + obs_arrays + innov_arrays
    if final:
        in_specs.append(col_spec)
        operands.append(partial)
    grid_spec = pltpu.PrefetchScalarGridSpec(
        num_scalar_prefetch=1,
        grid=(block_count // group,),
        in_specs=in_specs,
        out_specs=col_spec,
        scratch_shapes=[
            pltpu.VMEM((rows, width), jnp.float32),
            pltpu.VMEM((rows, width), jnp.bfloat16),
        ],
    )
    out_type = jnp.bfloat16 if final else jnp.float32
    return pl.pallas_call(
        kernel,
        grid_spec=grid_spec,
        out_shape=jax.ShapeDtypeStruct((members, cells), out_type),
        cost_estimate=pl.CostEstimate(flops=4 * cells * members * width, transcendentals=0, bytes_accessed=8 * cells * members),
    )(code, *operands)


def solution(mesh):
    in_specs = (
        P("wide", None, "lon"),
        P(None, "wide", "lon"),
        P(None, None, "lon"),
        P(None, None, "lon"),
        P("lon", "wide", None),
        P("lon", "wide"),
        P("lon", "wide", None),
    )
    out_specs = P("wide", None, "lon")
    return jax.shard_map(body, mesh=mesh, in_specs=in_specs, out_specs=out_specs, check_vma=False)
```

```python
import math

import jax
import jax.numpy as jnp
from jax import lax
from jax.sharding import PartitionSpec as P
from jax.experimental import pallas as pl
from jax.experimental.pallas import tpu as pltpu

BLK = 128
HALO_BLK = 4


def padded_2(value, sides, width):
    for axis, dim in sides:
        size, length = (lax.axis_size(axis), value.shape[dim])
        up = [(i, (i + 1) % size) for i in range(size)]
        down = [(j, i) for i, j in up]
        last = lax.slice_in_dim(value, length - width, length, axis=dim)
        first = lax.slice_in_dim(value, 0, width, axis=dim)
        before = lax.ppermute(last, axis, up)
        after = lax.ppermute(first, axis, down)
        value = jnp.concatenate([before, value, after], axis=dim)
    return value


def column_halo(value, axis):
    size = lax.axis_size(axis)
    edges = jnp.stack([value[..., 0], value[..., -1]]).transpose(0, 2, 1)
    spread = jnp.broadcast_to(edges[None], (size,) + edges.shape)
    return lax.all_to_all(spread, axis, 0, 0, tiled=False)


def forecast_call(state, received, here):
    members, rows, cols = state.shape
    size = received.shape[0]
    position = jnp.reshape(here, (1,)).astype(jnp.int32)

    def kernel(pos_ref, x_ref, h_ref, o_ref):
        col = lax.broadcasted_iota(jnp.int32, (rows, cols), 1)
        row = lax.broadcasted_iota(jnp.int32, (rows, cols), 0)
        t = pos_ref[0]
        west_from = (t + size - 1) % size
        east_from = (t + 1) % size

        def one(m, carry):
            x = x_ref[m].astype(jnp.float32)
            west_col = h_ref[west_from, 1][:, m:m + 1].astype(jnp.float32)
            east_col = h_ref[east_from, 0][:, m:m + 1].astype(jnp.float32)
            east_n = jnp.where(col == cols - 1, east_col, pltpu.roll(x, cols - 1, 1))
            west_n = jnp.where(col == 0, west_col, pltpu.roll(x, 1, 1))
            north = jnp.where(row == rows - 1, 0.0, pltpu.roll(x, rows - 1, 0))
            south = jnp.where(row == 0, 0.0, pltpu.roll(x, 1, 0))
            spread = east_n + west_n + north + south - 4.0 * x
            o_ref[:, m, :] = (x + 0.2 * spread - 0.3 * (east_n - west_n)).astype(jnp.bfloat16)
            return carry

        for m in range(members):
            one(m, 0)

    grid_spec = pltpu.PrefetchScalarGridSpec(
        num_scalar_prefetch=1,
        grid=(1,),
        in_specs=[
            pl.BlockSpec(state.shape, lambda i, p: (0, 0, 0)),
            pl.BlockSpec(received.shape, lambda i, p: (0, 0, 0, 0)),
        ],
        out_specs=pl.BlockSpec((rows, members, cols), lambda i, p: (0, 0, 0)),
    )
    return pl.pallas_call(
        kernel, grid_spec=grid_spec, out_shape=jax.ShapeDtypeStruct((rows, members, cols), jnp.bfloat16)
    )(position, state, received)


def observe_region(state, index, weight):
    members, cells = state.shape
    count = index.shape[1]
    width = math.gcd(512, count)
    nblocks = count // width
    index_blocks = index.reshape(4, nblocks, width).transpose(1, 0, 2)
    weight_blocks = weight.reshape(4, nblocks, width).transpose(1, 0, 2)
    cell_ids = lax.broadcasted_iota(jnp.int32, (cells, width), 0)

    def observe_one_block(pieces):
        index_here, weight_here = pieces
        summed = jnp.zeros((members, width), jnp.float32)
        for k in range(4):
            selector = (cell_ids == index_here[k][None, :]).astype(jnp.bfloat16)
            picked = jnp.dot(state, selector, preferred_element_type=jnp.float32)
            summed = summed + weight_here[k][None, :] * picked
        return summed.astype(jnp.bfloat16)

    result = lax.map(observe_one_block, (index_blocks, weight_blocks))
    return result.transpose(1, 0, 2).reshape(members, count)


OBS_STEP = 256
def observe_dev_call(state, index, weight, extra=None):
    band, members, cols = state.shape
    cells = band * cols
    count = index.shape[1]
    carry = extra is not None

    def kernel(f_ref, i_ref, w_ref, *rest):
        if carry:
            x_ref, o_ref = rest
        else:
            (o_ref,) = rest
        cell_ids = lax.broadcasted_iota(jnp.int32, (cells, OBS_STEP), 0)
        summed = jnp.zeros((members, OBS_STEP), jnp.float32)
        for k in range(4):
            selector = (cell_ids == i_ref[k:k + 1, :]).astype(jnp.bfloat16)
            picked = jnp.dot(f_ref[0], selector[:cols], preferred_element_type=jnp.float32)
            for r in range(1, band):
                picked = picked + jnp.dot(
                    f_ref[r], selector[r * cols:(r + 1) * cols], preferred_element_type=jnp.float32
                )
            summed = summed + w_ref[k:k + 1, :] * picked
        ens = summed.astype(jnp.bfloat16).astype(jnp.float32)
        mean = jnp.sum(ens, axis=0, keepdims=True) / members
        dev = (ens - mean).astype(jnp.bfloat16)
        if carry:
            o_ref[0] = dev
            o_ref[1] = x_ref[...]
        else:
            o_ref[...] = dev

    in_specs = [
        pl.BlockSpec(state.shape, lambda j: (0, 0, 0)),
        pl.BlockSpec((4, OBS_STEP), lambda j: (0, j)),
        pl.BlockSpec((4, OBS_STEP), lambda j: (0, j)),
    ]
    operands = [state, index, weight]
    if carry:
        in_specs.append(pl.BlockSpec((members, OBS_STEP), lambda j: (0, j)))
        operands.append(extra)
        out_spec = pl.BlockSpec((2, members, OBS_STEP), lambda j: (0, 0, j))
        out_shape = jax.ShapeDtypeStruct((2, members, count), jnp.bfloat16)
    else:
        out_spec = pl.BlockSpec((members, OBS_STEP), lambda j: (0, j))
        out_shape = jax.ShapeDtypeStruct((members, count), jnp.bfloat16)
    return pl.pallas_call(
        kernel,
        grid=(count // OBS_STEP,),
        in_specs=in_specs,
        out_specs=out_spec,
        out_shape=out_shape,
    )(*operands)


def anomaly_from_mean(state_values):
    centred = state_values.astype(jnp.float32)
    return (centred - jnp.mean(centred, axis=-2, keepdims=True)).astype(jnp.bfloat16)


def taper_tiles(classes, in_use, tile_width):
    row_ids = lax.broadcasted_iota(jnp.float32, (tile_width, tile_width), 0)
    col_ids = lax.broadcasted_iota(jnp.float32, (tile_width, tile_width), 1)
    offset = row_ids - col_ids
    length = 8.0 * jnp.exp2(classes.astype(jnp.float32))
    scaled = offset / length[..., None, None]
    return in_use[..., None, None] / (1.0 + scaled * scaled)


def body(background_ensemble, innov, obs_index, obs_weight, obs_list, tile_count, taper_class):
    received = column_halo(background_ensemble, "lon")
    prediction_increment = forecast_call(background_ensemble, received, lax.axis_index("lon"))
    whole_parallel_set, ensemble_lines_here, patch_meridian_lines = prediction_increment.shape
    members = innov.shape[0]
    band_rows = innov.shape[1]
    patch_gridpoints = band_rows * patch_meridian_lines
    region = lax.all_to_all(prediction_increment, "wide", split_axis=0, concat_axis=1, tiled=True)
    region_state = region
    first_row = lax.axis_index("wide") * band_rows
    local_index = lax.dynamic_slice_in_dim(obs_index, first_row, band_rows, 1).reshape(
        4, patch_gridpoints
    )
    local_index = local_index - first_row * patch_meridian_lines
    local_weight = lax.dynamic_slice_in_dim(obs_weight, first_row, band_rows, 1).reshape(
        4, patch_gridpoints
    )
    halo = HALO_BLK * BLK
    innov_flat = innov.reshape(members, patch_gridpoints)
    lon_size = lax.axis_size("lon")
    up = [(i, (i + 1) % lon_size) for i in range(lon_size)]
    down = [(j, i) for i, j in up]
    last_edge = observe_dev_call(
        region_state, local_index[:, -halo:], local_weight[:, -halo:], innov_flat[:, -halo:]
    )
    west = lax.ppermute(last_edge, "lon", up)
    first_edge = observe_dev_call(
        region_state, local_index[:, :halo], local_weight[:, :halo], innov_flat[:, :halo]
    )
    east = lax.ppermute(first_edge, "lon", down)
    middle_dev = observe_dev_call(region_state, local_index[:, halo:-halo], local_weight[:, halo:-halo])
    obs_dev = jnp.concatenate([first_edge[0], middle_dev, last_edge[0]], axis=1)
    halo_blocks = halo // BLK
    block_count = patch_gridpoints // BLK
    candidate_count = block_count + 2 * halo_blocks
    code = block_codes(obs_list[0], tile_count[0], taper_class[0], candidate_count)
    own_code = code[:, halo_blocks:halo_blocks + block_count]
    halo_code = jnp.concatenate([code[:, :halo_blocks], code[:, halo_blocks + block_count:]], axis=1)
    tiles = taper_table(BLK, members)
    partial = update_call(
        own_code.reshape(-1),
        region_state,
        None,
        [(first_edge, 0), (middle_dev, None), (last_edge, 0)],
        [(innov_flat, None)],
        tiles,
        block_count,
        block_count,
        group=8,
    )
    result = update_call(
        halo_code.reshape(-1),
        region_state,
        partial,
        [(west, 0), (east, 0)],
        [(west, 1), (east, 1)],
        tiles,
        block_count,
        2 * halo_blocks,
        group=8,
    )
    return lax.all_to_all(
        result.reshape(members, band_rows, patch_meridian_lines),
        "wide",
        split_axis=0,
        concat_axis=1,
        tiled=True,
    )


def block_codes(lists, counts, classes, candidate_count):
    zero_code = 4
    entries = jnp.arange(lists.shape[1], dtype=jnp.int32)
    value = jnp.where(entries[None, :] < counts[:, None], classes, zero_code)
    hit = lists[:, :, None] == jnp.arange(candidate_count, dtype=jnp.int32)[None, None, :]
    code = zero_code + jnp.sum(jnp.where(hit, value[:, :, None] - zero_code, 0), axis=1)
    return jnp.clip(code, 0, zero_code).astype(jnp.int32)


def taper_table(tile_width, members):
    row_ids = lax.broadcasted_iota(jnp.float32, (tile_width, tile_width), 0)
    col_ids = lax.broadcasted_iota(jnp.float32, (tile_width, tile_width), 1)
    offset = row_ids - col_ids
    length = 8.0 * jnp.exp2(jnp.arange(4, dtype=jnp.float32))
    scaled = offset[None] / length[:, None, None]
    tiles = (1.0 / (1.0 + scaled * scaled)) / (members - 1.0)
    return jnp.concatenate([tiles, jnp.zeros((1, tile_width, tile_width), jnp.float32)], axis=0)


GROUP = 4


def piece_spec(array):
    if array.ndim == 3:
        return pl.BlockSpec(array.shape, lambda g, code: (0, 0, 0))
    return pl.BlockSpec(array.shape, lambda g, code: (0, 0))


def piece_value(ref, pick):
    return ref[...] if pick is None else ref[pick]


def update_call(code, forecast, partial, obs_pieces, innov_pieces, tiles, block_count, candidate_count, group=GROUP):
    band, members, cols = forecast.shape
    cells = band * cols
    rows = group * BLK
    band_step = rows // cols
    width = candidate_count * BLK
    final = partial is not None
    obs_arrays = [a for a, _ in obs_pieces]
    innov_arrays = [a for a, _ in innov_pieces]
    n_obs = len(obs_pieces)
    n_innov = len(innov_pieces)

    def kernel(code_ref, f_ref, taper_ref, *rest):
        obs_refs = rest[:n_obs]
        innov_refs = rest[n_obs:n_obs + n_innov]
        rest = rest[n_obs + n_innov:]
        if final:
            part_ref, out_ref, cov_scr, tap_scr = rest
        else:
            out_ref, cov_scr, tap_scr = rest
        g = pl.program_id(0)
        forecast_block = jnp.concatenate([f_ref[r] for r in range(band_step)], axis=1).astype(jnp.float32)
        mean = jnp.sum(forecast_block, axis=0, keepdims=True) / members
        state = (forecast_block - mean).astype(jnp.bfloat16)
        offset = 0
        for ref, (_, pick) in zip(obs_refs, obs_pieces):
            piece = piece_value(ref, pick)
            span = piece.shape[1]
            cov_scr[:, offset:offset + span] = lax.dot_general(
                state, piece, (((0,), (0,)), ((), ())), preferred_element_type=jnp.float32
            )
            offset += span
        for sl in range(group):
            s = g * group + sl
            for b in range(candidate_count):
                c = code_ref[s * candidate_count + b]
                tile = cov_scr[sl * BLK:(sl + 1) * BLK, b * BLK:(b + 1) * BLK] * taper_ref[c]
                tap_scr[sl * BLK:(sl + 1) * BLK, b * BLK:(b + 1) * BLK] = tile.astype(jnp.bfloat16)
        change = None
        offset = 0
        for ref, (_, pick) in zip(innov_refs, innov_pieces):
            piece = piece_value(ref, pick)
            span = piece.shape[1]
            term = lax.dot_general(
                piece, tap_scr[:, offset:offset + span], (((1,), (1,)), ((), ())),
                preferred_element_type=jnp.float32,
            )
            change = term if change is None else change + term
            offset += span
        if final:
            total = part_ref[...] + change
            out_ref[...] = (forecast_block + total).astype(jnp.bfloat16)
        else:
            out_ref[...] = change

    col_spec = pl.BlockSpec((members, rows), lambda g, code: (0, g))
    band_spec = pl.BlockSpec((band_step, members, cols), lambda g, code: (g, 0, 0))
    in_specs = [band_spec, pl.BlockSpec(tiles.shape, lambda g, code: (0, 0, 0))]
    in_specs += [piece_spec(a) for a in obs_arrays] + [piece_spec(a) for a in innov_arrays]
    operands = [forecast, tiles] + obs_arrays + innov_arrays
    if final:
        in_specs.append(col_spec)
        operands.append(partial)
    grid_spec = pltpu.PrefetchScalarGridSpec(
        num_scalar_prefetch=1,
        grid=(block_count // group,),
        in_specs=in_specs,
        out_specs=col_spec,
        scratch_shapes=[
            pltpu.VMEM((rows, width), jnp.float32),
            pltpu.VMEM((rows, width), jnp.bfloat16),
        ],
    )
    out_type = jnp.bfloat16 if final else jnp.float32
    return pl.pallas_call(
        kernel,
        grid_spec=grid_spec,
        out_shape=jax.ShapeDtypeStruct((members, cells), out_type),
        cost_estimate=pl.CostEstimate(flops=4 * cells * members * width, transcendentals=0, bytes_accessed=8 * cells * members),
    )(code, *operands)


def solution(mesh):
    in_specs = (
        P("wide", None, "lon"),
        P(None, "wide", "lon"),
        P(None, None, "lon"),
        P(None, None, "lon"),
        P("lon", "wide", None),
        P("lon", "wide"),
        P("lon", "wide", None),
    )
    out_specs = P("wide", None, "lon")
    return jax.shard_map(body, mesh=mesh, in_specs=in_specs, out_specs=out_specs, check_vma=False)
```

```python
import math

import jax
import jax.numpy as jnp
from jax import lax
from jax.sharding import PartitionSpec as P
from jax.experimental import pallas as pl
from jax.experimental.pallas import tpu as pltpu

BLK = 128
HALO_BLK = 4


def padded_2(value, sides, width):
    for axis, dim in sides:
        size, length = (lax.axis_size(axis), value.shape[dim])
        up = [(i, (i + 1) % size) for i in range(size)]
        down = [(j, i) for i, j in up]
        last = lax.slice_in_dim(value, length - width, length, axis=dim)
        first = lax.slice_in_dim(value, 0, width, axis=dim)
        before = lax.ppermute(last, axis, up)
        after = lax.ppermute(first, axis, down)
        value = jnp.concatenate([before, value, after], axis=dim)
    return value


def column_halo(value, axis):
    size = lax.axis_size(axis)
    edges = jnp.stack([value[..., 0], value[..., -1]]).transpose(0, 2, 1)
    spread = jnp.broadcast_to(edges[None], (size,) + edges.shape)
    return lax.all_to_all(spread, axis, 0, 0, tiled=False)


def forecast_call(state, received, here):
    members, rows, cols = state.shape
    size = received.shape[0]
    position = jnp.reshape(here, (1,)).astype(jnp.int32)

    def kernel(pos_ref, x_ref, h_ref, o_ref):
        col = lax.broadcasted_iota(jnp.int32, (rows, cols), 1)
        row = lax.broadcasted_iota(jnp.int32, (rows, cols), 0)
        t = pos_ref[0]
        west_from = (t + size - 1) % size
        east_from = (t + 1) % size

        def one(m, carry):
            x = x_ref[m].astype(jnp.float32)
            west_col = h_ref[west_from, 1][:, m:m + 1].astype(jnp.float32)
            east_col = h_ref[east_from, 0][:, m:m + 1].astype(jnp.float32)
            east_n = jnp.where(col == cols - 1, east_col, pltpu.roll(x, cols - 1, 1))
            west_n = jnp.where(col == 0, west_col, pltpu.roll(x, 1, 1))
            north = jnp.where(row == rows - 1, 0.0, pltpu.roll(x, rows - 1, 0))
            south = jnp.where(row == 0, 0.0, pltpu.roll(x, 1, 0))
            spread = east_n + west_n + north + south - 4.0 * x
            o_ref[:, m, :] = (x + 0.2 * spread - 0.3 * (east_n - west_n)).astype(jnp.bfloat16)
            return carry

        for m in range(members):
            one(m, 0)

    grid_spec = pltpu.PrefetchScalarGridSpec(
        num_scalar_prefetch=1,
        grid=(1,),
        in_specs=[
            pl.BlockSpec(state.shape, lambda i, p: (0, 0, 0)),
            pl.BlockSpec(received.shape, lambda i, p: (0, 0, 0, 0)),
        ],
        out_specs=pl.BlockSpec((rows, members, cols), lambda i, p: (0, 0, 0)),
    )
    return pl.pallas_call(
        kernel, grid_spec=grid_spec, out_shape=jax.ShapeDtypeStruct((rows, members, cols), jnp.bfloat16)
    )(position, state, received)


def observe_region(state, index, weight):
    members, cells = state.shape
    count = index.shape[1]
    width = math.gcd(512, count)
    nblocks = count // width
    index_blocks = index.reshape(4, nblocks, width).transpose(1, 0, 2)
    weight_blocks = weight.reshape(4, nblocks, width).transpose(1, 0, 2)
    cell_ids = lax.broadcasted_iota(jnp.int32, (cells, width), 0)

    def observe_one_block(pieces):
        index_here, weight_here = pieces
        summed = jnp.zeros((members, width), jnp.float32)
        for k in range(4):
            selector = (cell_ids == index_here[k][None, :]).astype(jnp.bfloat16)
            picked = jnp.dot(state, selector, preferred_element_type=jnp.float32)
            summed = summed + weight_here[k][None, :] * picked
        return summed.astype(jnp.bfloat16)

    result = lax.map(observe_one_block, (index_blocks, weight_blocks))
    return result.transpose(1, 0, 2).reshape(members, count)


OBS_STEP = 256
def observe_dev_call(state, index, weight, extra=None):
    band, members, cols = state.shape
    cells = band * cols
    count = index.shape[1]
    carry = extra is not None

    def kernel(f_ref, i_ref, w_ref, *rest):
        if carry:
            x_ref, o_ref = rest
        else:
            (o_ref,) = rest
        cell_ids = lax.broadcasted_iota(jnp.int32, (cells, OBS_STEP), 0)
        summed = jnp.zeros((members, OBS_STEP), jnp.float32)
        for k in range(4):
            selector = (cell_ids == i_ref[k:k + 1, :]).astype(jnp.bfloat16)
            picked = jnp.dot(f_ref[0], selector[:cols], preferred_element_type=jnp.float32)
            for r in range(1, band):
                picked = picked + jnp.dot(
                    f_ref[r], selector[r * cols:(r + 1) * cols], preferred_element_type=jnp.float32
                )
            summed = summed + w_ref[k:k + 1, :] * picked
        ens = summed.astype(jnp.bfloat16).astype(jnp.float32)
        mean = jnp.sum(ens, axis=0, keepdims=True) / members
        dev = (ens - mean).astype(jnp.bfloat16)
        if carry:
            o_ref[0] = dev
            o_ref[1] = x_ref[...]
        else:
            o_ref[...] = dev

    in_specs = [
        pl.BlockSpec(state.shape, lambda j: (0, 0, 0)),
        pl.BlockSpec((4, OBS_STEP), lambda j: (0, j)),
        pl.BlockSpec((4, OBS_STEP), lambda j: (0, j)),
    ]
    operands = [state, index, weight]
    if carry:
        in_specs.append(pl.BlockSpec((members, OBS_STEP), lambda j: (0, j)))
        operands.append(extra)
        out_spec = pl.BlockSpec((2, members, OBS_STEP), lambda j: (0, 0, j))
        out_shape = jax.ShapeDtypeStruct((2, members, count), jnp.bfloat16)
    else:
        out_spec = pl.BlockSpec((members, OBS_STEP), lambda j: (0, j))
        out_shape = jax.ShapeDtypeStruct((members, count), jnp.bfloat16)
    return pl.pallas_call(
        kernel,
        grid=(count // OBS_STEP,),
        in_specs=in_specs,
        out_specs=out_spec,
        out_shape=out_shape,
    )(*operands)


def anomaly_from_mean(state_values):
    centred = state_values.astype(jnp.float32)
    return (centred - jnp.mean(centred, axis=-2, keepdims=True)).astype(jnp.bfloat16)


def taper_tiles(classes, in_use, tile_width):
    row_ids = lax.broadcasted_iota(jnp.float32, (tile_width, tile_width), 0)
    col_ids = lax.broadcasted_iota(jnp.float32, (tile_width, tile_width), 1)
    offset = row_ids - col_ids
    length = 8.0 * jnp.exp2(classes.astype(jnp.float32))
    scaled = offset / length[..., None, None]
    return in_use[..., None, None] / (1.0 + scaled * scaled)


def body(background_ensemble, innov, obs_index, obs_weight, obs_list, tile_count, taper_class):
    received = column_halo(background_ensemble, "lon")
    prediction_increment = forecast_call(background_ensemble, received, lax.axis_index("lon"))
    whole_parallel_set, ensemble_lines_here, patch_meridian_lines = prediction_increment.shape
    members = innov.shape[0]
    band_rows = innov.shape[1]
    patch_gridpoints = band_rows * patch_meridian_lines
    region = lax.all_to_all(prediction_increment, "wide", split_axis=0, concat_axis=1, tiled=True)
    region_state = region
    first_row = lax.axis_index("wide") * band_rows
    local_index = lax.dynamic_slice_in_dim(obs_index, first_row, band_rows, 1).reshape(
        4, patch_gridpoints
    )
    local_index = local_index - first_row * patch_meridian_lines
    local_weight = lax.dynamic_slice_in_dim(obs_weight, first_row, band_rows, 1).reshape(
        4, patch_gridpoints
    )
    halo = HALO_BLK * BLK
    innov_flat = innov.reshape(members, patch_gridpoints)
    lon_size = lax.axis_size("lon")
    up = [(i, (i + 1) % lon_size) for i in range(lon_size)]
    down = [(j, i) for i, j in up]
    last_edge = observe_dev_call(
        region_state, local_index[:, -halo:], local_weight[:, -halo:], innov_flat[:, -halo:]
    )
    west = lax.ppermute(last_edge, "lon", up)
    first_edge = observe_dev_call(
        region_state, local_index[:, :halo], local_weight[:, :halo], innov_flat[:, :halo]
    )
    east = lax.ppermute(first_edge, "lon", down)
    middle_dev = observe_dev_call(region_state, local_index[:, halo:-halo], local_weight[:, halo:-halo])
    obs_dev = jnp.concatenate([first_edge[0], middle_dev, last_edge[0]], axis=1)
    halo_blocks = halo // BLK
    block_count = patch_gridpoints // BLK
    candidate_count = block_count + 2 * halo_blocks
    code = block_codes(obs_list[0], tile_count[0], taper_class[0], candidate_count)
    own_code = code[:, halo_blocks:halo_blocks + block_count]
    halo_code = jnp.concatenate([code[:, :halo_blocks], code[:, halo_blocks + block_count:]], axis=1)
    tiles = taper_table(BLK, members)
    partial = update_call(
        own_code.reshape(-1),
        region_state,
        None,
        [(first_edge, 0), (middle_dev, None), (last_edge, 0)],
        [(innov_flat, None)],
        tiles,
        block_count,
        block_count,
        group=8,
    )
    result = update_call(
        halo_code.reshape(-1),
        region_state,
        partial,
        [(west, 0), (east, 0)],
        [(west, 1), (east, 1)],
        tiles,
        block_count,
        2 * halo_blocks,
        group=8,
    )
    return lax.all_to_all(
        result.reshape(members, band_rows, patch_meridian_lines),
        "wide",
        split_axis=0,
        concat_axis=1,
        tiled=True,
    )


def block_codes(lists, counts, classes, candidate_count):
    zero_code = 4
    entries = jnp.arange(lists.shape[1], dtype=jnp.int32)
    value = jnp.where(entries[None, :] < counts[:, None], classes, zero_code)
    hit = lists[:, :, None] == jnp.arange(candidate_count, dtype=jnp.int32)[None, None, :]
    code = zero_code + jnp.sum(jnp.where(hit, value[:, :, None] - zero_code, 0), axis=1)
    return jnp.clip(code, 0, zero_code).astype(jnp.int32)


def taper_table(tile_width, members):
    row_ids = lax.broadcasted_iota(jnp.float32, (tile_width, tile_width), 0)
    col_ids = lax.broadcasted_iota(jnp.float32, (tile_width, tile_width), 1)
    offset = row_ids - col_ids
    length = 8.0 * jnp.exp2(jnp.arange(4, dtype=jnp.float32))
    scaled = offset[None] / length[:, None, None]
    tiles = (1.0 / (1.0 + scaled * scaled)) / (members - 1.0)
    return jnp.concatenate([tiles, jnp.zeros((1, tile_width, tile_width), jnp.float32)], axis=0)


GROUP = 4


def piece_spec(array):
    if array.ndim == 3:
        return pl.BlockSpec(array.shape, lambda g, code: (0, 0, 0))
    return pl.BlockSpec(array.shape, lambda g, code: (0, 0))


def piece_value(ref, pick):
    return ref[...] if pick is None else ref[pick]


def update_call(code, forecast, partial, obs_pieces, innov_pieces, tiles, block_count, candidate_count, group=GROUP):
    band, members, cols = forecast.shape
    cells = band * cols
    rows = group * BLK
    band_step = rows // cols
    width = candidate_count * BLK
    final = partial is not None
    obs_arrays = [a for a, _ in obs_pieces]
    innov_arrays = [a for a, _ in innov_pieces]
    n_obs = len(obs_pieces)
    n_innov = len(innov_pieces)

    def kernel(code_ref, f_ref, *rest):
        obs_refs = rest[:n_obs]
        innov_refs = rest[n_obs:n_obs + n_innov]
        rest = rest[n_obs + n_innov:]
        if final:
            part_ref, out_ref, cov_scr, tap_scr, taper_ref = rest
        else:
            out_ref, cov_scr, tap_scr, taper_ref = rest
        g = pl.program_id(0)

        @pl.when(g == 0)
        def _():
            row_ids = lax.broadcasted_iota(jnp.int32, (BLK, BLK), 0)
            col_ids = lax.broadcasted_iota(jnp.int32, (BLK, BLK), 1)
            offset = (row_ids - col_ids).astype(jnp.float32)
            for k in range(4):
                scaled = offset / (8.0 * 2.0 ** k)
                taper_ref[k] = (1.0 / (1.0 + scaled * scaled)) / (members - 1.0)
            taper_ref[4] = jnp.zeros((BLK, BLK), jnp.float32)

        forecast_block = jnp.concatenate([f_ref[r] for r in range(band_step)], axis=1).astype(jnp.float32)
        mean = jnp.sum(forecast_block, axis=0, keepdims=True) / members
        state = (forecast_block - mean).astype(jnp.bfloat16)
        offset = 0
        for ref, (_, pick) in zip(obs_refs, obs_pieces):
            piece = piece_value(ref, pick)
            span = piece.shape[1]
            cov_scr[:, offset:offset + span] = lax.dot_general(
                state, piece, (((0,), (0,)), ((), ())), preferred_element_type=jnp.float32
            )
            offset += span
        for sl in range(group):
            s = g * group + sl
            for b in range(candidate_count):
                c = code_ref[s * candidate_count + b]
                tile = cov_scr[sl * BLK:(sl + 1) * BLK, b * BLK:(b + 1) * BLK] * taper_ref[c]
                tap_scr[sl * BLK:(sl + 1) * BLK, b * BLK:(b + 1) * BLK] = tile.astype(jnp.bfloat16)
        change = None
        offset = 0
        for ref, (_, pick) in zip(innov_refs, innov_pieces):
            piece = piece_value(ref, pick)
            span = piece.shape[1]
            term = lax.dot_general(
                piece, tap_scr[:, offset:offset + span], (((1,), (1,)), ((), ())),
                preferred_element_type=jnp.float32,
            )
            change = term if change is None else change + term
            offset += span
        if final:
            total = part_ref[...] + change
            out_ref[...] = (forecast_block + total).astype(jnp.bfloat16)
        else:
            out_ref[...] = change

    col_spec = pl.BlockSpec((members, rows), lambda g, code: (0, g))
    band_spec = pl.BlockSpec((band_step, members, cols), lambda g, code: (g, 0, 0))
    in_specs = [band_spec]
    in_specs += [piece_spec(a) for a in obs_arrays] + [piece_spec(a) for a in innov_arrays]
    operands = [forecast] + obs_arrays + innov_arrays
    if final:
        in_specs.append(col_spec)
        operands.append(partial)
    grid_spec = pltpu.PrefetchScalarGridSpec(
        num_scalar_prefetch=1,
        grid=(block_count // group,),
        in_specs=in_specs,
        out_specs=col_spec,
        scratch_shapes=[
            pltpu.VMEM((rows, width), jnp.float32),
            pltpu.VMEM((rows, width), jnp.bfloat16),
            pltpu.VMEM((5, BLK, BLK), jnp.float32),
        ],
    )
    out_type = jnp.bfloat16 if final else jnp.float32
    return pl.pallas_call(
        kernel,
        grid_spec=grid_spec,
        out_shape=jax.ShapeDtypeStruct((members, cells), out_type),
        cost_estimate=pl.CostEstimate(flops=4 * cells * members * width, transcendentals=0, bytes_accessed=8 * cells * members),
    )(code, *operands)


def solution(mesh):
    in_specs = (
        P("wide", None, "lon"),
        P(None, "wide", "lon"),
        P(None, None, "lon"),
        P(None, None, "lon"),
        P("lon", "wide", None),
        P("lon", "wide"),
        P("lon", "wide", None),
    )
    out_specs = P("wide", None, "lon")
    return jax.shard_map(body, mesh=mesh, in_specs=in_specs, out_specs=out_specs, check_vma=False)
```

```python
import math

import jax
import jax.numpy as jnp
from jax import lax
from jax.sharding import PartitionSpec as P
from jax.experimental import pallas as pl
from jax.experimental.pallas import tpu as pltpu

BLK = 128
HALO_BLK = 4


def padded_2(value, sides, width):
    for axis, dim in sides:
        size, length = (lax.axis_size(axis), value.shape[dim])
        up = [(i, (i + 1) % size) for i in range(size)]
        down = [(j, i) for i, j in up]
        last = lax.slice_in_dim(value, length - width, length, axis=dim)
        first = lax.slice_in_dim(value, 0, width, axis=dim)
        before = lax.ppermute(last, axis, up)
        after = lax.ppermute(first, axis, down)
        value = jnp.concatenate([before, value, after], axis=dim)
    return value


def column_halo(value, axis):
    size = lax.axis_size(axis)
    edges = jnp.stack([value[..., 0], value[..., -1]]).transpose(0, 2, 1)
    spread = jnp.broadcast_to(edges[None], (size,) + edges.shape)
    return lax.all_to_all(spread, axis, 0, 0, tiled=False)


def forecast_call(state, received, here):
    members, rows, cols = state.shape
    size = received.shape[0]
    position = jnp.reshape(here, (1,)).astype(jnp.int32)

    def kernel(pos_ref, x_ref, h_ref, o_ref):
        col = lax.broadcasted_iota(jnp.int32, (rows, cols), 1)
        row = lax.broadcasted_iota(jnp.int32, (rows, cols), 0)
        t = pos_ref[0]
        west_from = (t + size - 1) % size
        east_from = (t + 1) % size

        def one(m, carry):
            x = x_ref[m].astype(jnp.float32)
            west_col = h_ref[west_from, 1][:, m:m + 1].astype(jnp.float32)
            east_col = h_ref[east_from, 0][:, m:m + 1].astype(jnp.float32)
            east_n = jnp.where(col == cols - 1, east_col, pltpu.roll(x, cols - 1, 1))
            west_n = jnp.where(col == 0, west_col, pltpu.roll(x, 1, 1))
            north = jnp.where(row == rows - 1, 0.0, pltpu.roll(x, rows - 1, 0))
            south = jnp.where(row == 0, 0.0, pltpu.roll(x, 1, 0))
            spread = east_n + west_n + north + south - 4.0 * x
            o_ref[:, m, :] = (x + 0.2 * spread - 0.3 * (east_n - west_n)).astype(jnp.bfloat16)
            return carry

        for m in range(members):
            one(m, 0)

    grid_spec = pltpu.PrefetchScalarGridSpec(
        num_scalar_prefetch=1,
        grid=(1,),
        in_specs=[
            pl.BlockSpec(state.shape, lambda i, p: (0, 0, 0)),
            pl.BlockSpec(received.shape, lambda i, p: (0, 0, 0, 0)),
        ],
        out_specs=pl.BlockSpec((rows, members, cols), lambda i, p: (0, 0, 0)),
    )
    return pl.pallas_call(
        kernel, grid_spec=grid_spec, out_shape=jax.ShapeDtypeStruct((rows, members, cols), jnp.bfloat16)
    )(position, state, received)


def observe_region(state, index, weight):
    members, cells = state.shape
    count = index.shape[1]
    width = math.gcd(512, count)
    nblocks = count // width
    index_blocks = index.reshape(4, nblocks, width).transpose(1, 0, 2)
    weight_blocks = weight.reshape(4, nblocks, width).transpose(1, 0, 2)
    cell_ids = lax.broadcasted_iota(jnp.int32, (cells, width), 0)

    def observe_one_block(pieces):
        index_here, weight_here = pieces
        summed = jnp.zeros((members, width), jnp.float32)
        for k in range(4):
            selector = (cell_ids == index_here[k][None, :]).astype(jnp.bfloat16)
            picked = jnp.dot(state, selector, preferred_element_type=jnp.float32)
            summed = summed + weight_here[k][None, :] * picked
        return summed.astype(jnp.bfloat16)

    result = lax.map(observe_one_block, (index_blocks, weight_blocks))
    return result.transpose(1, 0, 2).reshape(members, count)


OBS_STEP = 256
def observe_dev_call(state, index, weight, extra=None, step=OBS_STEP):
    band, members, cols = state.shape
    cells = band * cols
    count = index.shape[1]
    carry = extra is not None

    def kernel(f_ref, i_ref, w_ref, *rest):
        if carry:
            x_ref, o_ref = rest
        else:
            (o_ref,) = rest
        cell_ids = lax.broadcasted_iota(jnp.int32, (cells, step), 0)
        summed = jnp.zeros((members, step), jnp.float32)
        for k in range(4):
            selector = (cell_ids == i_ref[k:k + 1, :]).astype(jnp.bfloat16)
            picked = jnp.dot(f_ref[0], selector[:cols], preferred_element_type=jnp.float32)
            for r in range(1, band):
                picked = picked + jnp.dot(
                    f_ref[r], selector[r * cols:(r + 1) * cols], preferred_element_type=jnp.float32
                )
            summed = summed + w_ref[k:k + 1, :] * picked
        ens = summed.astype(jnp.bfloat16).astype(jnp.float32)
        mean = jnp.sum(ens, axis=0, keepdims=True) / members
        dev = (ens - mean).astype(jnp.bfloat16)
        if carry:
            o_ref[0] = dev
            o_ref[1] = x_ref[...]
        else:
            o_ref[...] = dev

    in_specs = [
        pl.BlockSpec(state.shape, lambda j: (0, 0, 0)),
        pl.BlockSpec((4, step), lambda j: (0, j)),
        pl.BlockSpec((4, step), lambda j: (0, j)),
    ]
    operands = [state, index, weight]
    if carry:
        in_specs.append(pl.BlockSpec((members, step), lambda j: (0, j)))
        operands.append(extra)
        out_spec = pl.BlockSpec((2, members, step), lambda j: (0, 0, j))
        out_shape = jax.ShapeDtypeStruct((2, members, count), jnp.bfloat16)
    else:
        out_spec = pl.BlockSpec((members, step), lambda j: (0, j))
        out_shape = jax.ShapeDtypeStruct((members, count), jnp.bfloat16)
    return pl.pallas_call(
        kernel,
        grid=(count // step,),
        in_specs=in_specs,
        out_specs=out_spec,
        out_shape=out_shape,
    )(*operands)


def anomaly_from_mean(state_values):
    centred = state_values.astype(jnp.float32)
    return (centred - jnp.mean(centred, axis=-2, keepdims=True)).astype(jnp.bfloat16)


def taper_tiles(classes, in_use, tile_width):
    row_ids = lax.broadcasted_iota(jnp.float32, (tile_width, tile_width), 0)
    col_ids = lax.broadcasted_iota(jnp.float32, (tile_width, tile_width), 1)
    offset = row_ids - col_ids
    length = 8.0 * jnp.exp2(classes.astype(jnp.float32))
    scaled = offset / length[..., None, None]
    return in_use[..., None, None] / (1.0 + scaled * scaled)


def body(background_ensemble, innov, obs_index, obs_weight, obs_list, tile_count, taper_class):
    received = column_halo(background_ensemble, "lon")
    prediction_increment = forecast_call(background_ensemble, received, lax.axis_index("lon"))
    whole_parallel_set, ensemble_lines_here, patch_meridian_lines = prediction_increment.shape
    members = innov.shape[0]
    band_rows = innov.shape[1]
    patch_gridpoints = band_rows * patch_meridian_lines
    region = lax.all_to_all(prediction_increment, "wide", split_axis=0, concat_axis=1, tiled=True)
    region_state = region
    first_row = lax.axis_index("wide") * band_rows
    local_index = lax.dynamic_slice_in_dim(obs_index, first_row, band_rows, 1).reshape(
        4, patch_gridpoints
    )
    local_index = local_index - first_row * patch_meridian_lines
    local_weight = lax.dynamic_slice_in_dim(obs_weight, first_row, band_rows, 1).reshape(
        4, patch_gridpoints
    )
    halo = HALO_BLK * BLK
    innov_flat = innov.reshape(members, patch_gridpoints)
    lon_size = lax.axis_size("lon")
    up = [(i, (i + 1) % lon_size) for i in range(lon_size)]
    down = [(j, i) for i, j in up]
    last_edge = observe_dev_call(
        region_state, local_index[:, -halo:], local_weight[:, -halo:], innov_flat[:, -halo:]
    )
    west = lax.ppermute(last_edge, "lon", up)
    first_edge = observe_dev_call(
        region_state, local_index[:, :halo], local_weight[:, :halo], innov_flat[:, :halo]
    )
    east = lax.ppermute(first_edge, "lon", down)
    middle_dev = observe_dev_call(region_state, local_index[:, halo:-halo], local_weight[:, halo:-halo], step=512)
    obs_dev = jnp.concatenate([first_edge[0], middle_dev, last_edge[0]], axis=1)
    halo_blocks = halo // BLK
    block_count = patch_gridpoints // BLK
    candidate_count = block_count + 2 * halo_blocks
    code = block_codes(obs_list[0], tile_count[0], taper_class[0], candidate_count)
    own_code = code[:, halo_blocks:halo_blocks + block_count]
    halo_code = jnp.concatenate([code[:, :halo_blocks], code[:, halo_blocks + block_count:]], axis=1)
    tiles = taper_table(BLK, members)
    partial = update_call(
        own_code.reshape(-1),
        region_state,
        None,
        [(first_edge, 0), (middle_dev, None), (last_edge, 0)],
        [(innov_flat, None)],
        tiles,
        block_count,
        block_count,
        group=8,
    )
    result = update_call(
        halo_code.reshape(-1),
        region_state,
        partial,
        [(west, 0), (east, 0)],
        [(west, 1), (east, 1)],
        tiles,
        block_count,
        2 * halo_blocks,
        group=8,
    )
    return lax.all_to_all(
        result.reshape(members, band_rows, patch_meridian_lines),
        "wide",
        split_axis=0,
        concat_axis=1,
        tiled=True,
    )


def block_codes(lists, counts, classes, candidate_count):
    zero_code = 4
    entries = jnp.arange(lists.shape[1], dtype=jnp.int32)
    value = jnp.where(entries[None, :] < counts[:, None], classes, zero_code)
    hit = lists[:, :, None] == jnp.arange(candidate_count, dtype=jnp.int32)[None, None, :]
    code = zero_code + jnp.sum(jnp.where(hit, value[:, :, None] - zero_code, 0), axis=1)
    return jnp.clip(code, 0, zero_code).astype(jnp.int32)


def taper_table(tile_width, members):
    row_ids = lax.broadcasted_iota(jnp.float32, (tile_width, tile_width), 0)
    col_ids = lax.broadcasted_iota(jnp.float32, (tile_width, tile_width), 1)
    offset = row_ids - col_ids
    length = 8.0 * jnp.exp2(jnp.arange(4, dtype=jnp.float32))
    scaled = offset[None] / length[:, None, None]
    tiles = (1.0 / (1.0 + scaled * scaled)) / (members - 1.0)
    return jnp.concatenate([tiles, jnp.zeros((1, tile_width, tile_width), jnp.float32)], axis=0)


GROUP = 4


def piece_spec(array):
    if array.ndim == 3:
        return pl.BlockSpec(array.shape, lambda g, code: (0, 0, 0))
    return pl.BlockSpec(array.shape, lambda g, code: (0, 0))


def piece_value(ref, pick):
    return ref[...] if pick is None else ref[pick]


def update_call(code, forecast, partial, obs_pieces, innov_pieces, tiles, block_count, candidate_count, group=GROUP):
    band, members, cols = forecast.shape
    cells = band * cols
    rows = group * BLK
    band_step = rows // cols
    width = candidate_count * BLK
    final = partial is not None
    obs_arrays = [a for a, _ in obs_pieces]
    innov_arrays = [a for a, _ in innov_pieces]
    n_obs = len(obs_pieces)
    n_innov = len(innov_pieces)

    def kernel(code_ref, f_ref, taper_ref, *rest):
        obs_refs = rest[:n_obs]
        innov_refs = rest[n_obs:n_obs + n_innov]
        rest = rest[n_obs + n_innov:]
        if final:
            part_ref, out_ref, cov_scr, tap_scr = rest
        else:
            out_ref, cov_scr, tap_scr = rest
        g = pl.program_id(0)
        forecast_block = jnp.concatenate([f_ref[r] for r in range(band_step)], axis=1).astype(jnp.float32)
        mean = jnp.sum(forecast_block, axis=0, keepdims=True) / members
        state = (forecast_block - mean).astype(jnp.bfloat16)
        offset = 0
        for ref, (_, pick) in zip(obs_refs, obs_pieces):
            piece = piece_value(ref, pick)
            span = piece.shape[1]
            cov_scr[:, offset:offset + span] = lax.dot_general(
                state, piece, (((0,), (0,)), ((), ())), preferred_element_type=jnp.float32
            )
            offset += span
        for sl in range(group):
            s = g * group + sl
            for b in range(candidate_count):
                c = code_ref[s * candidate_count + b]
                tile = cov_scr[sl * BLK:(sl + 1) * BLK, b * BLK:(b + 1) * BLK] * taper_ref[c]
                tap_scr[sl * BLK:(sl + 1) * BLK, b * BLK:(b + 1) * BLK] = tile.astype(jnp.bfloat16)
        change = None
        offset = 0
        for ref, (_, pick) in zip(innov_refs, innov_pieces):
            piece = piece_value(ref, pick)
            span = piece.shape[1]
            term = lax.dot_general(
                piece, tap_scr[:, offset:offset + span], (((1,), (1,)), ((), ())),
                preferred_element_type=jnp.float32,
            )
            change = term if change is None else change + term
            offset += span
        if final:
            total = part_ref[...] + change
            out_ref[...] = (forecast_block + total).astype(jnp.bfloat16)
        else:
            out_ref[...] = change

    col_spec = pl.BlockSpec((members, rows), lambda g, code: (0, g))
    band_spec = pl.BlockSpec((band_step, members, cols), lambda g, code: (g, 0, 0))
    in_specs = [band_spec, pl.BlockSpec(tiles.shape, lambda g, code: (0, 0, 0))]
    in_specs += [piece_spec(a) for a in obs_arrays] + [piece_spec(a) for a in innov_arrays]
    operands = [forecast, tiles] + obs_arrays + innov_arrays
    if final:
        in_specs.append(col_spec)
        operands.append(partial)
    grid_spec = pltpu.PrefetchScalarGridSpec(
        num_scalar_prefetch=1,
        grid=(block_count // group,),
        in_specs=in_specs,
        out_specs=col_spec,
        scratch_shapes=[
            pltpu.VMEM((rows, width), jnp.float32),
            pltpu.VMEM((rows, width), jnp.bfloat16),
        ],
    )
    out_type = jnp.bfloat16 if final else jnp.float32
    return pl.pallas_call(
        kernel,
        grid_spec=grid_spec,
        out_shape=jax.ShapeDtypeStruct((members, cells), out_type),
        cost_estimate=pl.CostEstimate(flops=4 * cells * members * width, transcendentals=0, bytes_accessed=8 * cells * members),
    )(code, *operands)


def solution(mesh):
    in_specs = (
        P("wide", None, "lon"),
        P(None, "wide", "lon"),
        P(None, None, "lon"),
        P(None, None, "lon"),
        P("lon", "wide", None),
        P("lon", "wide"),
        P("lon", "wide", None),
    )
    out_specs = P("wide", None, "lon")
    return jax.shard_map(body, mesh=mesh, in_specs=in_specs, out_specs=out_specs, check_vma=False)
```

```python
import math

import jax
import jax.numpy as jnp
from jax import lax
from jax.sharding import PartitionSpec as P
from jax.experimental import pallas as pl
from jax.experimental.pallas import tpu as pltpu

BLK = 128
HALO_BLK = 4


def padded_2(value, sides, width):
    for axis, dim in sides:
        size, length = (lax.axis_size(axis), value.shape[dim])
        up = [(i, (i + 1) % size) for i in range(size)]
        down = [(j, i) for i, j in up]
        last = lax.slice_in_dim(value, length - width, length, axis=dim)
        first = lax.slice_in_dim(value, 0, width, axis=dim)
        before = lax.ppermute(last, axis, up)
        after = lax.ppermute(first, axis, down)
        value = jnp.concatenate([before, value, after], axis=dim)
    return value


def column_halo(value, axis):
    size = lax.axis_size(axis)
    edges = jnp.stack([value[..., 0], value[..., -1]]).transpose(0, 2, 1)
    spread = jnp.broadcast_to(edges[None], (size,) + edges.shape)
    return lax.all_to_all(spread, axis, 0, 0, tiled=False)


def forecast_call(state, received, here):
    members, rows, cols = state.shape
    size = received.shape[0]
    position = jnp.reshape(here, (1,)).astype(jnp.int32)

    def kernel(pos_ref, x_ref, h_ref, o_ref):
        col = lax.broadcasted_iota(jnp.int32, (rows, cols), 1)
        row = lax.broadcasted_iota(jnp.int32, (rows, cols), 0)
        t = pos_ref[0]
        west_from = (t + size - 1) % size
        east_from = (t + 1) % size

        def one(m, carry):
            x = x_ref[m].astype(jnp.float32)
            west_col = h_ref[west_from, 1][:, m:m + 1].astype(jnp.float32)
            east_col = h_ref[east_from, 0][:, m:m + 1].astype(jnp.float32)
            east_n = jnp.where(col == cols - 1, east_col, pltpu.roll(x, cols - 1, 1))
            west_n = jnp.where(col == 0, west_col, pltpu.roll(x, 1, 1))
            north = jnp.where(row == rows - 1, 0.0, pltpu.roll(x, rows - 1, 0))
            south = jnp.where(row == 0, 0.0, pltpu.roll(x, 1, 0))
            spread = east_n + west_n + north + south - 4.0 * x
            o_ref[:, m, :] = (x + 0.2 * spread - 0.3 * (east_n - west_n)).astype(jnp.bfloat16)
            return carry

        for m in range(members):
            one(m, 0)

    grid_spec = pltpu.PrefetchScalarGridSpec(
        num_scalar_prefetch=1,
        grid=(1,),
        in_specs=[
            pl.BlockSpec(state.shape, lambda i, p: (0, 0, 0)),
            pl.BlockSpec(received.shape, lambda i, p: (0, 0, 0, 0)),
        ],
        out_specs=pl.BlockSpec((rows, members, cols), lambda i, p: (0, 0, 0)),
    )
    return pl.pallas_call(
        kernel, grid_spec=grid_spec, out_shape=jax.ShapeDtypeStruct((rows, members, cols), jnp.bfloat16)
    )(position, state, received)


def observe_region(state, index, weight):
    members, cells = state.shape
    count = index.shape[1]
    width = math.gcd(512, count)
    nblocks = count // width
    index_blocks = index.reshape(4, nblocks, width).transpose(1, 0, 2)
    weight_blocks = weight.reshape(4, nblocks, width).transpose(1, 0, 2)
    cell_ids = lax.broadcasted_iota(jnp.int32, (cells, width), 0)

    def observe_one_block(pieces):
        index_here, weight_here = pieces
        summed = jnp.zeros((members, width), jnp.float32)
        for k in range(4):
            selector = (cell_ids == index_here[k][None, :]).astype(jnp.bfloat16)
            picked = jnp.dot(state, selector, preferred_element_type=jnp.float32)
            summed = summed + weight_here[k][None, :] * picked
        return summed.astype(jnp.bfloat16)

    result = lax.map(observe_one_block, (index_blocks, weight_blocks))
    return result.transpose(1, 0, 2).reshape(members, count)


OBS_STEP = 256
def observe_dev_call(state, index, weight, extra=None, step=OBS_STEP):
    band, members, cols = state.shape
    cells = band * cols
    count = index.shape[1]
    carry = extra is not None

    def kernel(f_ref, i_ref, w_ref, *rest):
        if carry:
            x_ref, o_ref = rest
        else:
            (o_ref,) = rest
        cell_ids = lax.broadcasted_iota(jnp.int32, (cells, step), 0)
        summed = jnp.zeros((members, step), jnp.float32)
        for k in range(4):
            selector = (cell_ids == i_ref[k:k + 1, :]).astype(jnp.bfloat16)
            picked = jnp.dot(f_ref[0], selector[:cols], preferred_element_type=jnp.float32)
            for r in range(1, band):
                picked = picked + jnp.dot(
                    f_ref[r], selector[r * cols:(r + 1) * cols], preferred_element_type=jnp.float32
                )
            summed = summed + w_ref[k:k + 1, :] * picked
        ens = summed.astype(jnp.bfloat16).astype(jnp.float32)
        mean = jnp.sum(ens, axis=0, keepdims=True) / members
        dev = (ens - mean).astype(jnp.bfloat16)
        if carry:
            o_ref[0] = dev
            o_ref[1] = x_ref[...]
        else:
            o_ref[...] = dev

    in_specs = [
        pl.BlockSpec(state.shape, lambda j: (0, 0, 0)),
        pl.BlockSpec((4, step), lambda j: (0, j)),
        pl.BlockSpec((4, step), lambda j: (0, j)),
    ]
    operands = [state, index, weight]
    if carry:
        in_specs.append(pl.BlockSpec((members, step), lambda j: (0, j)))
        operands.append(extra)
        out_spec = pl.BlockSpec((2, members, step), lambda j: (0, 0, j))
        out_shape = jax.ShapeDtypeStruct((2, members, count), jnp.bfloat16)
    else:
        out_spec = pl.BlockSpec((members, step), lambda j: (0, j))
        out_shape = jax.ShapeDtypeStruct((members, count), jnp.bfloat16)
    return pl.pallas_call(
        kernel,
        grid=(count // step,),
        in_specs=in_specs,
        out_specs=out_spec,
        out_shape=out_shape,
    )(*operands)


def anomaly_from_mean(state_values):
    centred = state_values.astype(jnp.float32)
    return (centred - jnp.mean(centred, axis=-2, keepdims=True)).astype(jnp.bfloat16)


def taper_tiles(classes, in_use, tile_width):
    row_ids = lax.broadcasted_iota(jnp.float32, (tile_width, tile_width), 0)
    col_ids = lax.broadcasted_iota(jnp.float32, (tile_width, tile_width), 1)
    offset = row_ids - col_ids
    length = 8.0 * jnp.exp2(classes.astype(jnp.float32))
    scaled = offset / length[..., None, None]
    return in_use[..., None, None] / (1.0 + scaled * scaled)


def body(background_ensemble, innov, obs_index, obs_weight, obs_list, tile_count, taper_class):
    received = column_halo(background_ensemble, "lon")
    prediction_increment = forecast_call(background_ensemble, received, lax.axis_index("lon"))
    whole_parallel_set, ensemble_lines_here, patch_meridian_lines = prediction_increment.shape
    members = innov.shape[0]
    band_rows = innov.shape[1]
    patch_gridpoints = band_rows * patch_meridian_lines
    region = lax.all_to_all(prediction_increment, "wide", split_axis=0, concat_axis=1, tiled=True)
    region_state = region
    first_row = lax.axis_index("wide") * band_rows
    local_index = lax.dynamic_slice_in_dim(obs_index, first_row, band_rows, 1).reshape(
        4, patch_gridpoints
    )
    local_index = local_index - first_row * patch_meridian_lines
    local_weight = lax.dynamic_slice_in_dim(obs_weight, first_row, band_rows, 1).reshape(
        4, patch_gridpoints
    )
    halo = HALO_BLK * BLK
    innov_flat = innov.reshape(members, patch_gridpoints)
    lon_size = lax.axis_size("lon")
    up = [(i, (i + 1) % lon_size) for i in range(lon_size)]
    down = [(j, i) for i, j in up]
    last_edge = observe_dev_call(
        region_state, local_index[:, -halo:], local_weight[:, -halo:], innov_flat[:, -halo:]
    )
    west = lax.ppermute(last_edge, "lon", up)
    first_edge = observe_dev_call(
        region_state, local_index[:, :halo], local_weight[:, :halo], innov_flat[:, :halo]
    )
    east = lax.ppermute(first_edge, "lon", down)
    middle_dev = observe_dev_call(region_state, local_index[:, halo:-halo], local_weight[:, halo:-halo], step=512)
    obs_dev = jnp.concatenate([first_edge[0], middle_dev, last_edge[0]], axis=1)
    halo_blocks = halo // BLK
    block_count = patch_gridpoints // BLK
    candidate_count = block_count + 2 * halo_blocks
    code = block_codes(obs_list[0], tile_count[0], taper_class[0], candidate_count)
    own_code = code[:, halo_blocks:halo_blocks + block_count]
    halo_code = jnp.concatenate([code[:, :halo_blocks], code[:, halo_blocks + block_count:]], axis=1)
    tiles = taper_table(BLK, members)
    partial = update_call(
        own_code.reshape(-1),
        region_state,
        None,
        [(first_edge, 0), (middle_dev, None), (last_edge, 0)],
        [(innov_flat, None)],
        tiles,
        block_count,
        block_count,
        group=16,
    )
    result = update_call(
        halo_code.reshape(-1),
        region_state,
        partial,
        [(west, 0), (east, 0)],
        [(west, 1), (east, 1)],
        tiles,
        block_count,
        2 * halo_blocks,
        group=8,
    )
    return lax.all_to_all(
        result.reshape(members, band_rows, patch_meridian_lines),
        "wide",
        split_axis=0,
        concat_axis=1,
        tiled=True,
    )


def block_codes(lists, counts, classes, candidate_count):
    zero_code = 4
    entries = jnp.arange(lists.shape[1], dtype=jnp.int32)
    value = jnp.where(entries[None, :] < counts[:, None], classes, zero_code)
    hit = lists[:, :, None] == jnp.arange(candidate_count, dtype=jnp.int32)[None, None, :]
    code = zero_code + jnp.sum(jnp.where(hit, value[:, :, None] - zero_code, 0), axis=1)
    return jnp.clip(code, 0, zero_code).astype(jnp.int32)


def taper_table(tile_width, members):
    row_ids = lax.broadcasted_iota(jnp.float32, (tile_width, tile_width), 0)
    col_ids = lax.broadcasted_iota(jnp.float32, (tile_width, tile_width), 1)
    offset = row_ids - col_ids
    length = 8.0 * jnp.exp2(jnp.arange(4, dtype=jnp.float32))
    scaled = offset[None] / length[:, None, None]
    tiles = (1.0 / (1.0 + scaled * scaled)) / (members - 1.0)
    return jnp.concatenate([tiles, jnp.zeros((1, tile_width, tile_width), jnp.float32)], axis=0)


GROUP = 4


def piece_spec(array):
    if array.ndim == 3:
        return pl.BlockSpec(array.shape, lambda g, code: (0, 0, 0))
    return pl.BlockSpec(array.shape, lambda g, code: (0, 0))


def piece_value(ref, pick):
    return ref[...] if pick is None else ref[pick]


def update_call(code, forecast, partial, obs_pieces, innov_pieces, tiles, block_count, candidate_count, group=GROUP):
    band, members, cols = forecast.shape
    cells = band * cols
    rows = group * BLK
    band_step = rows // cols
    width = candidate_count * BLK
    final = partial is not None
    obs_arrays = [a for a, _ in obs_pieces]
    innov_arrays = [a for a, _ in innov_pieces]
    n_obs = len(obs_pieces)
    n_innov = len(innov_pieces)

    def kernel(code_ref, f_ref, taper_ref, *rest):
        obs_refs = rest[:n_obs]
        innov_refs = rest[n_obs:n_obs + n_innov]
        rest = rest[n_obs + n_innov:]
        if final:
            part_ref, out_ref, cov_scr, tap_scr = rest
        else:
            out_ref, cov_scr, tap_scr = rest
        g = pl.program_id(0)
        forecast_block = jnp.concatenate([f_ref[r] for r in range(band_step)], axis=1).astype(jnp.float32)
        mean = jnp.sum(forecast_block, axis=0, keepdims=True) / members
        state = (forecast_block - mean).astype(jnp.bfloat16)
        offset = 0
        for ref, (_, pick) in zip(obs_refs, obs_pieces):
            piece = piece_value(ref, pick)
            span = piece.shape[1]
            cov_scr[:, offset:offset + span] = lax.dot_general(
                state, piece, (((0,), (0,)), ((), ())), preferred_element_type=jnp.float32
            )
            offset += span
        for sl in range(group):
            s = g * group + sl
            for b in range(candidate_count):
                c = code_ref[s * candidate_count + b]
                tile = cov_scr[sl * BLK:(sl + 1) * BLK, b * BLK:(b + 1) * BLK] * taper_ref[c]
                tap_scr[sl * BLK:(sl + 1) * BLK, b * BLK:(b + 1) * BLK] = tile.astype(jnp.bfloat16)
        change = None
        offset = 0
        for ref, (_, pick) in zip(innov_refs, innov_pieces):
            piece = piece_value(ref, pick)
            span = piece.shape[1]
            term = lax.dot_general(
                piece, tap_scr[:, offset:offset + span], (((1,), (1,)), ((), ())),
                preferred_element_type=jnp.float32,
            )
            change = term if change is None else change + term
            offset += span
        if final:
            total = part_ref[...] + change
            out_ref[...] = (forecast_block + total).astype(jnp.bfloat16)
        else:
            out_ref[...] = change

    col_spec = pl.BlockSpec((members, rows), lambda g, code: (0, g))
    band_spec = pl.BlockSpec((band_step, members, cols), lambda g, code: (g, 0, 0))
    in_specs = [band_spec, pl.BlockSpec(tiles.shape, lambda g, code: (0, 0, 0))]
    in_specs += [piece_spec(a) for a in obs_arrays] + [piece_spec(a) for a in innov_arrays]
    operands = [forecast, tiles] + obs_arrays + innov_arrays
    if final:
        in_specs.append(col_spec)
        operands.append(partial)
    grid_spec = pltpu.PrefetchScalarGridSpec(
        num_scalar_prefetch=1,
        grid=(block_count // group,),
        in_specs=in_specs,
        out_specs=col_spec,
        scratch_shapes=[
            pltpu.VMEM((rows, width), jnp.float32),
            pltpu.VMEM((rows, width), jnp.bfloat16),
        ],
    )
    out_type = jnp.bfloat16 if final else jnp.float32
    return pl.pallas_call(
        kernel,
        grid_spec=grid_spec,
        out_shape=jax.ShapeDtypeStruct((members, cells), out_type),
        cost_estimate=pl.CostEstimate(flops=4 * cells * members * width, transcendentals=0, bytes_accessed=8 * cells * members),
    )(code, *operands)


def solution(mesh):
    in_specs = (
        P("wide", None, "lon"),
        P(None, "wide", "lon"),
        P(None, None, "lon"),
        P(None, None, "lon"),
        P("lon", "wide", None),
        P("lon", "wide"),
        P("lon", "wide", None),
    )
    out_specs = P("wide", None, "lon")
    return jax.shard_map(body, mesh=mesh, in_specs=in_specs, out_specs=out_specs, check_vma=False)
```
